32 devices in a mesh: dp: 4 (over x, core), expert: 8 (over z, y).
Axes of the slice: x: 2, y: 2, z: 4, core: 2. Of those that a mesh axis runs over, the one named last changes fastest.
Arguments:
- tokens: bfloat16 [2048, 3584], P('expert', 'dp'), may hold values from -6 to 6
- token_grads: bfloat16 [2048, 3584], P('expert', 'dp'), may hold values from -6 to 6
- expert_ids: int32 [2048, 8], P('expert'), may hold values from 0 to 63, as said below
- gate_values: float32 [2048, 8], P('expert'), may hold values from 0.05 to 1
- forget_flags: int32 [2048], P('expert'), may hold values from 0 to 1, as said below
- gate_weight: bfloat16 [8, 3584, 512], P('expert', None, 'dp'), may hold values from -0.09375 to 0.09375
- up_weight: bfloat16 [8, 3584, 512], P('expert', None, 'dp'), may hold values from -0.09375 to 0.09375
- down_weight: bfloat16 [8, 512, 3584], P('expert', 'dp'), may hold values from -0.25 to 0.25
Outputs:
- grad_gate: bfloat16 [8, 3584, 512], P('expert', None, 'dp')
- grad_up: bfloat16 [8, 3584, 512], P('expert', None, 'dp')
- input_grad: bfloat16 [2048, 3584], P('expert', 'dp')
The draws below stay inside these ranges and needn't reach their ends.
Inputs may be any that keep to these rules, and one draw needn't show every extreme that they name: `expert_ids`: each row names 8 different experts. Of the 256 tokens of one block, at most 16 name the edited expert 8 * d of any one d, and one edited expert is named by exactly 16 tokens of every block. `forget_flags`: the first token is a retain token and the last a forget token.
All inputs are finite; a program needn't handle non-finite values.
Results may differ from the reference program's by a relative error of at most 0.009.
Values may be sent and summed in bfloat16 or wider, within the bound.
No kernel may reach another device: no remote copies, remote signals or barrier semaphores. Data moves between devices by JAX's collectives and lax.ppermute only.
A program may use at most 64 MiB of HBM per device.

```python
import math
import jax
import jax.numpy as jnp
from jax import lax

D = 3584
FF_DEV = 128
EXP_DEV = 8
TOP = 8
TOK_DEV = 256
CAP = 16
TOKENS = 2048
EXPERTS = 64
EDITED = 8
FF = 512


def one_order(key):
    return jax.random.permutation(key, TOK_DEV)


def draw_expert_ids(key, part):
    blocks = TOKENS // TOK_DEV
    keys = jax.random.split(jax.random.fold_in(key, 11), 5)
    hottest = jax.random.randint(keys[0], (), 0, blocks)
    counts = jax.random.randint(keys[1], (blocks, blocks), CAP // 4, CAP // 2 + 1)
    destination = jnp.arange(blocks, dtype=jnp.int32)
    counts = jnp.where(destination[None, :] == hottest, CAP, counts)
    offset = jax.random.randint(keys[2], (blocks, 1), 0, TOK_DEV)
    starts = jnp.cumsum(counts, axis=1) - counts + offset
    orders = jax.vmap(one_order)(jax.random.split(keys[3], blocks)).astype(jnp.int32)
    relative = (orders[:, :, None] - starts[:, None, :]) % TOK_DEV
    forced = relative < counts[:, None, :]
    numbers = jnp.arange(EXPERTS, dtype=jnp.int32)
    is_edited = numbers % EXP_DEV == 0
    forced_full = jnp.repeat(forced, EXP_DEV, axis=2) & is_edited[None, None, :]
    noise = jax.random.randint(keys[4], (blocks, TOK_DEV, EXPERTS), 0, 1 << 20) * EXPERTS + numbers[None, None, :]
    scores = jnp.where(forced_full, 1 << 30, jnp.where(is_edited[None, None, :], -1, noise))
    chosen = lax.top_k(scores, TOP)[1].astype(jnp.int32)
    return chosen.reshape(TOKENS, TOP)


def draw_forget_flags(key, part):
    keys = jax.random.split(jax.random.fold_in(key, 23), 2)
    percent = jax.random.randint(keys[0], (), 50, 151)
    position = jnp.arange(TOKENS, dtype=jnp.int32)
    threshold = (TOKENS + 2 * position) * percent * 10 // (6 * TOKENS)
    sample = jax.random.randint(keys[1], (TOKENS,), 0, 1000)
    flags = (sample < threshold).astype(jnp.int32)
    flags = jnp.where(position == 0, 0, jnp.where(position == TOKENS - 1, 1, flags))
    return flags.astype(jnp.int32)


def shard_levels(stream_key, shape, pieces, smallest, largest):
    def one(axis_at, shards_of):
        heights = jax.random.uniform(jax.random.fold_in(jax.random.fold_in(stream_key, 6), axis_at), (shards_of,), jnp.float32, smallest / len(pieces), largest / len(pieces))
        return jnp.repeat(jnp.exp(heights), shape[axis_at] // shards_of).reshape((-1,) + (1,) * (len(shape) - axis_at - 1))

    loudness = one(*pieces[0])
    for cut in pieces[1:]:
        loudness = loudness * one(*cut)
    return loudness


def bell_draw(key, dims, deviation, most, cuts=(), kind=jnp.bfloat16):
    result = jax.random.normal(key, dims, jnp.float32) * deviation
    if len(cuts) > 0:
        result = shard_levels(key, dims, cuts, -0.22, 0.18) * result
    return jnp.clip(result, min=-most, max=most).astype(kind)


def setup_inputs(seed: int = 0) -> dict:
    key_of = jax.random.split(jax.random.key(seed), 9)
    tokens = bell_draw(key_of[0], (TOKENS, D), 1.0, 6.0, ((0, 8), (1, 4)))
    token_grads = bell_draw(key_of[1], (TOKENS, D), 1.0, 6.0, ((0, 8), (1, 4)))
    expert_ids = draw_expert_ids(jax.random.fold_in(key_of[8], 71), 0)
    gate_values = jnp.clip(jnp.exp(math.log(1.0) - 2.9957323 * jax.random.uniform(key_of[3], (TOKENS, TOP), jnp.float32) ** shard_levels(key_of[3], (TOKENS, TOP), ((0, 8),), -0.2, 0.2)), 0.05, 1.0)
    forget_flags = draw_forget_flags(jax.random.fold_in(key_of[8], 71), 0)
    gate_weight = bell_draw(key_of[5], (EDITED, D, FF), D ** -0.5, 0.09375, ((0, 8), (2, 4)))
    up_weight = bell_draw(key_of[6], (EDITED, D, FF), D ** -0.5, 0.09375, ((0, 8), (2, 4)))
    down_weight = bell_draw(key_of[7], (EDITED, FF, D), FF ** -0.5, 0.25, ((0, 8), (1, 4)))
    return {"tokens": tokens, "token_grads": token_grads, "expert_ids": expert_ids, "gate_values": gate_values, "forget_flags": forget_flags, "gate_weight": gate_weight, "up_weight": up_weight, "down_weight": down_weight}


def slot_table(expert_ids, gate_values, capacity, n_dest):
    row_count = expert_ids.shape[0]
    edited = jnp.arange(n_dest, dtype=jnp.int32) * EXP_DEV
    match = expert_ids[:, :, None] == edited[None, None, :]
    hits = jnp.sum(match.astype(jnp.int32), axis=1)
    gate_sel = jnp.sum(jnp.where(match, gate_values[:, :, None], jnp.zeros((), gate_values.dtype)), axis=1)
    rank = jnp.cumsum(hits, axis=0) - hits
    places = jnp.arange(capacity, dtype=jnp.int32)
    taken = (hits[:, :, None] == 1) & (rank[:, :, None] == places[None, None, :])
    row_index = jnp.arange(row_count, dtype=jnp.int32)[:, None, None]
    source = jnp.sum(jnp.where(taken, row_index, 0), axis=0).astype(jnp.int32)
    filled = jnp.any(taken, axis=0)
    source = jnp.where(filled, source, row_count).astype(jnp.int32)
    return source, gate_sel, taken


def silu_parts(pre):
    sigmoid_gate = jax.nn.sigmoid(pre)
    return pre * sigmoid_gate, sigmoid_gate * (1.0 + pre * (1.0 - sigmoid_gate))


def reference(tokens, token_grads, expert_ids, gate_values, forget_flags, gate_weight, up_weight, down_weight):
    blocks = TOKENS // TOK_DEV
    groups = FF // FF_DEV
    n_forget = jnp.sum(forget_flags).astype(jnp.int32)
    n_retain = TOKENS - n_forget
    half_total = jnp.float32(TOKENS) / 2.0
    weight_tok = jnp.where(forget_flags == 1, -half_total / n_forget.astype(jnp.float32), half_total / n_retain.astype(jnp.float32))

    def per_block(ids_one, gates_one, weight_one):
        source, gate_sel, taken = slot_table(ids_one, gates_one, CAP, blocks)
        scale_tok = gate_sel * weight_one[:, None]
        slot_scale = jnp.sum(jnp.where(taken, scale_tok[:, :, None], jnp.zeros((), scale_tok.dtype)), axis=0)
        return source, slot_scale

    source, slot_scale = jax.vmap(per_block)(expert_ids.reshape(blocks, TOK_DEV, TOP), gate_values.reshape(blocks, TOK_DEV, TOP), weight_tok.reshape(blocks, TOK_DEV))
    offsets = (jnp.arange(blocks, dtype=jnp.int32) * TOK_DEV)[:, None, None]
    global_rows = jnp.where(source < TOK_DEV, source + offsets, TOKENS).astype(jnp.int32)
    rows_by_expert = jnp.transpose(global_rows, (1, 0, 2)).reshape(blocks, blocks * CAP)
    scale_by_expert = jnp.transpose(slot_scale, (1, 0, 2)).reshape(blocks, blocks * CAP)
    tokens_pad = jnp.concatenate([tokens, jnp.zeros((1, D), tokens.dtype)], axis=0)
    grads_pad = jnp.concatenate([token_grads, jnp.zeros((1, D), token_grads.dtype)], axis=0)

    def per_expert(operands):
        rows, scale, w_gate, w_up, w_down = operands
        slots = rows.shape[0]
        slot_tokens = jnp.take(tokens_pad, rows, axis=0)
        slot_grads = (scale[:, None] * jnp.take(grads_pad, rows, axis=0).astype(jnp.float32)).astype(jnp.bfloat16)
        gate_pre = jnp.dot(slot_tokens, w_gate, preferred_element_type=jnp.float32)
        up_pre = jnp.dot(slot_tokens, w_up, preferred_element_type=jnp.float32)
        hidden_grad = jnp.dot(slot_grads, w_down.T, preferred_element_type=jnp.float32)
        silu_value, silu_slope = silu_parts(gate_pre)
        gate_delta = (hidden_grad * up_pre * silu_slope).astype(jnp.bfloat16)
        up_delta = (hidden_grad * silu_value).astype(jnp.bfloat16)
        grad_gate = jnp.dot(slot_tokens.T, gate_delta, preferred_element_type=jnp.float32).astype(jnp.bfloat16)
        grad_up = jnp.dot(slot_tokens.T, up_delta, preferred_element_type=jnp.float32).astype(jnp.bfloat16)
        gate_parts = jnp.einsum("sgh,dgh->gsd", gate_delta.astype(jnp.float32).reshape(slots, groups, FF_DEV), w_gate.astype(jnp.float32).reshape(D, groups, FF_DEV))
        up_parts = jnp.einsum("sgh,dgh->gsd", up_delta.astype(jnp.float32).reshape(slots, groups, FF_DEV), w_up.astype(jnp.float32).reshape(D, groups, FF_DEV))
        rounded = lax.optimization_barrier((gate_parts + up_parts).astype(jnp.bfloat16))
        contribution = jnp.sum(rounded.astype(jnp.float32), axis=0)
        return grad_gate, grad_up, contribution

    grad_gate, grad_up, contributions = lax.map(per_expert, (rows_by_expert, scale_by_expert, gate_weight, up_weight, down_weight))
    summed = jax.ops.segment_sum(contributions.reshape(-1, D), rows_by_expert.reshape(-1), num_segments=TOKENS + 1)
    input_grad = summed[:TOKENS].astype(jnp.bfloat16)
    return grad_gate, grad_up, input_grad
```

```python
import jax
import jax.numpy as jnp
from jax import lax
from jax.sharding import PartitionSpec as P

EXP_DEV = 8
CAP = 16
SIDE = 128


def slot_table(expert_ids, gate_values, forget_flags, capacity, n_dest):
    row_count = expert_ids.shape[0]
    edited = jnp.arange(n_dest, dtype=jnp.int32) * EXP_DEV
    match = expert_ids[:, :, None] == edited[None, None, :]
    hits = jnp.sum(match.astype(jnp.int32), axis=1)
    gate_sel = jnp.sum(
        jnp.where(match, gate_values[:, :, None], jnp.zeros((), gate_values.dtype)), axis=1
    )
    rank = jnp.cumsum(hits, axis=0) - hits
    places = jnp.arange(capacity, dtype=jnp.int32)
    taken = (hits[:, :, None] == 1) & (rank[:, :, None] == places[None, None, :])
    row_index = jnp.arange(row_count, dtype=jnp.int32)[:, None, None]
    source = jnp.sum(jnp.where(taken, row_index, 0), axis=0)
    filled = jnp.any(taken, axis=0)
    source = jnp.where(filled, source, row_count)
    slot_gate = jnp.sum(jnp.where(taken, gate_sel[:, :, None], 0.0), axis=0)
    slot_flag = jnp.sum(jnp.where(taken, forget_flags[:, None, None], 0), axis=0)
    return source, slot_gate, slot_flag


def silu_parts(pre):
    sigmoid_gate = jax.nn.sigmoid(pre)
    return (pre * sigmoid_gate, sigmoid_gate * (1.0 + pre * (1.0 - sigmoid_gate)))


def bf16_part(x):
    return lax.reduce_precision(x, exponent_bits=8, mantissa_bits=7)


def side_columns(slot_gate, slot_flag, local_count):
    hi = bf16_part(slot_gate)
    rest = slot_gate - hi
    mid = bf16_part(rest)
    lo = rest - mid
    count = jnp.broadcast_to(local_count, slot_gate.shape)
    cols = [hi, mid, lo, slot_flag.astype(jnp.float32),
            (count // 256).astype(jnp.float32), (count % 256).astype(jnp.float32)]
    packed = jnp.stack(cols, axis=-1)
    pad = jnp.zeros(packed.shape[:-1] + (SIDE - len(cols),), jnp.float32)
    return jnp.concatenate([packed, pad], axis=-1).astype(jnp.bfloat16)


def partner(x, bit, n):
    return lax.ppermute(x, "dp", [(i, i ^ bit) for i in range(n)])


def gather_dp(x, n):
    me = lax.axis_index("dp")
    acc = x[None]
    bit = n // 2
    while bit >= 1:
        other = partner(acc, bit, n)
        low_first = jnp.stack([acc, other], axis=1)
        high_first = jnp.stack([other, acc], axis=1)
        acc = jnp.where((me & bit) == 0, low_first, high_first)
        acc = acc.reshape((-1,) + x.shape)
        bit //= 2
    return acc


def scatter_dp(parts, n):
    me = lax.axis_index("dp")
    acc = parts
    bit = 1
    while bit < n:
        pairs = acc.reshape((acc.shape[0] // 2, 2) + acc.shape[1:])
        mine = (me & bit) != 0
        keep = jnp.where(mine, pairs[:, 1], pairs[:, 0])
        send = jnp.where(mine, pairs[:, 0], pairs[:, 1])
        got = partner(send.astype(jnp.bfloat16), bit, n)
        acc = keep.astype(jnp.float32) + got.astype(jnp.float32)
        bit *= 2
    return acc[0]


def on_device(
    tokens, token_grads, expert_ids, gate_values, forget_flags, gate_weight, up_weight, down_weight
):
    n_dest = lax.axis_size("expert")
    n_dp = lax.axis_size("dp")
    row_count, width = tokens.shape
    source, slot_gate, slot_flag = slot_table(expert_ids, gate_values, forget_flags, CAP, n_dest)
    local_count = jnp.sum(forget_flags)
    flat_source = source.reshape(-1)
    blank = jnp.zeros((1, width), tokens.dtype)
    chosen_tokens = jnp.take(jnp.concatenate([tokens, blank], axis=0), flat_source, axis=0)
    chosen_grads = jnp.take(jnp.concatenate([token_grads, blank], axis=0), flat_source, axis=0)
    side = side_columns(slot_gate, slot_flag, local_count).reshape(-1, SIDE)
    payload = jnp.concatenate([chosen_tokens, chosen_grads, side], axis=1)
    arrived = lax.all_to_all(payload, "expert", split_axis=0, concat_axis=0, tiled=True)
    slots = arrived.shape[0]
    part_tokens = arrived[:, :width]
    raw_grads = arrived[:, width : 2 * width]
    info = arrived[:, 2 * width :].astype(jnp.float32)
    gate_sel = (info[:, 0] + info[:, 1]) + info[:, 2]
    flag = info[:, 3]
    counts = info.reshape(n_dest, CAP, SIDE)[:, 0, 4] * 256.0 + info.reshape(n_dest, CAP, SIDE)[:, 0, 5]
    forget_count = jnp.sum(counts)
    all_rows = row_count * n_dest
    half_total = jnp.float32(all_rows) / 2.0
    weight = jnp.where(
        flag == 1.0,
        -half_total / forget_count,
        half_total / (jnp.float32(all_rows) - forget_count),
    )
    scale = gate_sel * weight
    part_grads = (scale[:, None] * raw_grads.astype(jnp.float32)).astype(jnp.bfloat16)
    both = jnp.concatenate([part_tokens, part_grads], axis=1)
    gathered = gather_dp(both, n_dp)
    slot_tokens = jnp.transpose(gathered[:, :, :width], (1, 0, 2)).reshape(slots, n_dp * width)
    slot_grads = jnp.transpose(gathered[:, :, width:], (1, 0, 2)).reshape(slots, n_dp * width)
    w_gate = gate_weight[0]
    w_up = up_weight[0]
    w_down = down_weight[0]
    gate_pre = jnp.dot(slot_tokens, w_gate, preferred_element_type=jnp.float32)
    up_pre = jnp.dot(slot_tokens, w_up, preferred_element_type=jnp.float32)
    last_dims = (((1,), (1,)), ((), ()))
    hidden_grad = lax.dot_general(slot_grads, w_down, last_dims, preferred_element_type=jnp.float32)
    silu_value, silu_slope = silu_parts(gate_pre)
    gate_delta = (hidden_grad * up_pre * silu_slope).astype(jnp.bfloat16)
    up_delta = (hidden_grad * silu_value).astype(jnp.bfloat16)
    first_dims = (((0,), (0,)), ((), ()))
    grad_gate = lax.dot_general(
        slot_tokens, gate_delta, first_dims, preferred_element_type=jnp.float32
    ).astype(jnp.bfloat16)
    grad_up = lax.dot_general(
        slot_tokens, up_delta, first_dims, preferred_element_type=jnp.float32
    ).astype(jnp.bfloat16)
    from_gate = lax.dot_general(gate_delta, w_gate, last_dims, preferred_element_type=jnp.float32)
    from_up = lax.dot_general(up_delta, w_up, last_dims, preferred_element_type=jnp.float32)
    part = (from_gate + from_up).astype(jnp.bfloat16)
    chunks = jnp.transpose(part.reshape(slots, n_dp, width), (1, 0, 2))
    summed = scatter_dp(chunks, n_dp).astype(jnp.bfloat16)
    returned = lax.all_to_all(summed, "expert", split_axis=0, concat_axis=0, tiled=True)
    owner_match = (
        flat_source[:, None] == jnp.arange(row_count, dtype=jnp.int32)[None, :]
    ).astype(jnp.bfloat16)
    input_grad = lax.dot_general(
        owner_match, returned, (((0,), (0,)), ((), ())), preferred_element_type=jnp.float32
    )
    return (grad_gate[None], grad_up[None], input_grad.astype(jnp.bfloat16))


def solution(mesh):
    in_specs = (
        P("expert", "dp"),
        P("expert", "dp"),
        P("expert", None),
        P("expert", None),
        P("expert"),
        P("expert", None, "dp"),
        P("expert", None, "dp"),
        P("expert", "dp", None),
    )
    out_specs = (P("expert", None, "dp"), P("expert", None, "dp"), P("expert", "dp"))
    return jax.shard_map(
        on_device, mesh=mesh, in_specs=in_specs, out_specs=out_specs, check_vma=False
    )
```

```python
import jax
import jax.numpy as jnp
from jax import lax
from jax.sharding import PartitionSpec as P

EXP_DEV = 8
CAP = 16


def one_hot_slots(expert_ids, capacity, n_dest):
    row_count = expert_ids.shape[0]
    edited = jnp.arange(n_dest, dtype=jnp.int32) * EXP_DEV
    match = expert_ids[:, :, None] == edited[None, None, :]
    hits = jnp.sum(match.astype(jnp.int32), axis=1)
    before = (
        jnp.arange(row_count, dtype=jnp.int32)[:, None] > jnp.arange(row_count, dtype=jnp.int32)[None, :]
    ).astype(jnp.bfloat16)
    rank = jnp.dot(before, hits.astype(jnp.bfloat16), preferred_element_type=jnp.float32)
    places = jnp.arange(capacity, dtype=jnp.float32)
    taken = (hits[:, :, None] == 1) & (rank[:, :, None] == places[None, None, :])
    return match, taken.reshape(row_count, n_dest * capacity).astype(jnp.bfloat16)


def silu_parts(pre):
    sigmoid_gate = jax.nn.sigmoid(pre)
    return (pre * sigmoid_gate, sigmoid_gate * (1.0 + pre * (1.0 - sigmoid_gate)))


def bf16_part(x):
    return lax.reduce_precision(x, exponent_bits=8, mantissa_bits=7)


def side_width(n_dest):
    return -(-(3 * n_dest + 3) // 128) * 128


def token_side(match, gate_values, forget_flags, n_dest):
    gate_sel = jnp.sum(
        jnp.where(match, gate_values[:, :, None], jnp.zeros((), gate_values.dtype)), axis=1
    )
    hi = bf16_part(gate_sel)
    rest = gate_sel - hi
    mid = bf16_part(rest)
    lo = rest - mid
    flag = forget_flags.astype(jnp.float32)[:, None]
    cols = jnp.concatenate([hi, mid, lo, flag], axis=1)
    pad = jnp.zeros((cols.shape[0], side_width(n_dest) - cols.shape[1]), jnp.float32)
    return jnp.concatenate([cols, pad], axis=1).astype(jnp.bfloat16)


def partner(x, bit, n):
    return lax.ppermute(x, "dp", [(i, i ^ bit) for i in range(n)])


def gather_dp(x, n):
    me = lax.axis_index("dp")
    acc = x[None]
    bit = n // 2
    while bit >= 1:
        other = partner(acc, bit, n)
        low_first = jnp.stack([acc, other], axis=1)
        high_first = jnp.stack([other, acc], axis=1)
        acc = jnp.where((me & bit) == 0, low_first, high_first)
        acc = acc.reshape((-1,) + x.shape)
        bit //= 2
    return acc


def scatter_dp(parts, n):
    me = lax.axis_index("dp")
    acc = parts
    bit = 1
    while bit < n:
        pairs = acc.reshape((acc.shape[0] // 2, 2) + acc.shape[1:])
        mine = (me & bit) != 0
        keep = jnp.where(mine, pairs[:, 1], pairs[:, 0])
        send = jnp.where(mine, pairs[:, 0], pairs[:, 1])
        got = partner(send.astype(jnp.bfloat16), bit, n)
        acc = keep.astype(jnp.float32) + got.astype(jnp.float32)
        bit *= 2
    return acc[0]


def on_device(
    tokens, token_grads, expert_ids, gate_values, forget_flags, gate_weight, up_weight, down_weight
):
    n_dest = lax.axis_size("expert")
    n_dp = lax.axis_size("dp")
    me = lax.axis_index("expert")
    row_count, width = tokens.shape
    side = side_width(n_dest)
    match, pick = one_hot_slots(expert_ids, CAP, n_dest)
    per_token = jnp.concatenate(
        [tokens, token_grads, token_side(match, gate_values, forget_flags, n_dest)], axis=1
    )
    local_count = jnp.sum(forget_flags)
    at_col = jnp.arange(2 * width + side, dtype=jnp.int32)
    count_row = jnp.where(
        at_col == 2 * width + 3 * n_dest + 1,
        (local_count // 256).astype(jnp.float32),
        jnp.where(at_col == 2 * width + 3 * n_dest + 2, (local_count % 256).astype(jnp.float32), 0.0),
    )
    chosen = lax.dot_general(pick, per_token, (((0,), (0,)), ((), ())), preferred_element_type=jnp.float32)
    payload = (chosen + count_row[None, :]).astype(jnp.bfloat16)
    arrived = lax.all_to_all(payload, "expert", split_axis=0, concat_axis=0, tiled=True)
    slots = arrived.shape[0]
    part_tokens = arrived[:, :width]
    raw_grads = arrived[:, width : 2 * width]
    info = arrived[:, 2 * width :].astype(jnp.float32)
    pieces = lax.dynamic_slice_in_dim(info[:, : 3 * n_dest].reshape(slots, 3, n_dest), me, 1, axis=2)
    gate_sel = (pieces[:, 0, 0] + pieces[:, 1, 0]) + pieces[:, 2, 0]
    flag = info[:, 3 * n_dest]
    by_block = info.reshape(n_dest, CAP, side)[:, 0]
    forget_count = jnp.sum(by_block[:, 3 * n_dest + 1] * 256.0 + by_block[:, 3 * n_dest + 2])
    all_rows = row_count * n_dest
    half_total = jnp.float32(all_rows) / 2.0
    weight = jnp.where(
        flag == 1.0,
        -half_total / forget_count,
        half_total / (jnp.float32(all_rows) - forget_count),
    )
    scale = gate_sel * weight
    part_grads = (scale[:, None] * raw_grads.astype(jnp.float32)).astype(jnp.bfloat16)
    both = jnp.concatenate([part_tokens, part_grads], axis=1)
    gathered = gather_dp(both, n_dp)
    slot_tokens = gathered[:, :, :width]
    slot_grads = gathered[:, :, width:]
    ff = gate_weight.shape[2]
    w_gate = gate_weight[0].reshape(n_dp, width, ff)
    w_up = up_weight[0].reshape(n_dp, width, ff)
    w_down = down_weight[0].reshape(ff, n_dp, width)
    chunk_dims = (((0, 2), (0, 1)), ((), ()))
    gate_pre = lax.dot_general(slot_tokens, w_gate, chunk_dims, preferred_element_type=jnp.float32)
    up_pre = lax.dot_general(slot_tokens, w_up, chunk_dims, preferred_element_type=jnp.float32)
    hidden_grad = lax.dot_general(
        slot_grads, w_down, (((0, 2), (1, 2)), ((), ())), preferred_element_type=jnp.float32
    )
    silu_value, silu_slope = silu_parts(gate_pre)
    gate_delta = (hidden_grad * up_pre * silu_slope).astype(jnp.bfloat16)
    up_delta = (hidden_grad * silu_value).astype(jnp.bfloat16)
    slot_dims = (((1,), (0,)), ((), ()))
    grad_gate = lax.dot_general(
        slot_tokens, gate_delta, slot_dims, preferred_element_type=jnp.float32
    ).astype(jnp.bfloat16)
    grad_up = lax.dot_general(
        slot_tokens, up_delta, slot_dims, preferred_element_type=jnp.float32
    ).astype(jnp.bfloat16)
    back_dims = (((2,), (1,)), ((), ()))
    from_gate = lax.dot_general(w_gate, gate_delta, back_dims, preferred_element_type=jnp.float32)
    from_up = lax.dot_general(w_up, up_delta, back_dims, preferred_element_type=jnp.float32)
    part = (from_gate + from_up).astype(jnp.bfloat16)
    summed = scatter_dp(jnp.swapaxes(part, 1, 2), n_dp).astype(jnp.bfloat16)
    returned = lax.all_to_all(summed, "expert", split_axis=0, concat_axis=0, tiled=True)
    input_grad = lax.dot_general(pick, returned, slot_dims, preferred_element_type=jnp.float32)
    return (
        grad_gate.reshape(1, n_dp * width, ff),
        grad_up.reshape(1, n_dp * width, ff),
        input_grad.astype(jnp.bfloat16),
    )


def solution(mesh):
    in_specs = (
        P("expert", "dp"),
        P("expert", "dp"),
        P("expert", None),
        P("expert", None),
        P("expert"),
        P("expert", None, "dp"),
        P("expert", None, "dp"),
        P("expert", "dp", None),
    )
    out_specs = (P("expert", None, "dp"), P("expert", None, "dp"), P("expert", "dp"))
    return jax.shard_map(
        on_device, mesh=mesh, in_specs=in_specs, out_specs=out_specs, check_vma=False
    )
```

```python
import jax
import jax.numpy as jnp
from jax import lax
from jax.sharding import PartitionSpec as P

EXP_DEV = 8
CAP = 16


def one_hot_slots(expert_ids, capacity, n_dest):
    row_count = expert_ids.shape[0]
    edited = jnp.arange(n_dest, dtype=jnp.int32) * EXP_DEV
    match = expert_ids[:, :, None] == edited[None, None, :]
    hits = jnp.sum(match.astype(jnp.int32), axis=1)
    before = (
        jnp.arange(row_count, dtype=jnp.int32)[:, None] > jnp.arange(row_count, dtype=jnp.int32)[None, :]
    ).astype(jnp.bfloat16)
    rank = jnp.dot(before, hits.astype(jnp.bfloat16), preferred_element_type=jnp.float32)
    places = jnp.arange(capacity, dtype=jnp.float32)
    taken = (hits[:, :, None] == 1) & (rank[:, :, None] == places[None, None, :])
    return match, taken.reshape(row_count, n_dest * capacity).astype(jnp.bfloat16)


def silu_parts(pre):
    sigmoid_gate = jax.nn.sigmoid(pre)
    return (pre * sigmoid_gate, sigmoid_gate * (1.0 + pre * (1.0 - sigmoid_gate)))


def bf16_part(x):
    return lax.reduce_precision(x, exponent_bits=8, mantissa_bits=7)


def side_width(n_dest):
    return -(-(3 * n_dest + 3) // 128) * 128


def token_side(match, gate_values, forget_flags, n_dest):
    gate_sel = jnp.sum(
        jnp.where(match, gate_values[:, :, None], jnp.zeros((), gate_values.dtype)), axis=1
    )
    hi = bf16_part(gate_sel)
    rest = gate_sel - hi
    mid = bf16_part(rest)
    lo = rest - mid
    flag = forget_flags.astype(jnp.float32)[:, None]
    cols = jnp.concatenate([hi, mid, lo, flag], axis=1)
    pad = jnp.zeros((cols.shape[0], side_width(n_dest) - cols.shape[1]), jnp.float32)
    return jnp.concatenate([cols, pad], axis=1).astype(jnp.bfloat16)


def partner(x, bit, n):
    return lax.ppermute(x, "dp", [(i, i ^ bit) for i in range(n)])


def gather_dp(x, n):
    me = lax.axis_index("dp")
    acc = x[None]
    bit = n // 2
    while bit >= 1:
        acc = jnp.concatenate([acc, partner(acc, bit, n)], axis=0)
        bit //= 2
    rel = me ^ jnp.arange(n, dtype=jnp.int32)
    pos = jnp.zeros_like(rel)
    width = n.bit_length() - 1
    for b in range(width):
        pos = pos | (((rel >> b) & 1) << (width - 1 - b))
    return jnp.take(acc, pos, axis=0)


def scatter_dp(parts, n):
    me = lax.axis_index("dp")
    acc = parts
    bit = 1
    while bit < n:
        pairs = acc.reshape((acc.shape[0] // 2, 2) + acc.shape[1:])
        mine = (me & bit) != 0
        keep = jnp.where(mine, pairs[:, 1], pairs[:, 0])
        send = jnp.where(mine, pairs[:, 0], pairs[:, 1])
        got = partner(send.astype(jnp.bfloat16), bit, n)
        acc = keep.astype(jnp.float32) + got.astype(jnp.float32)
        bit *= 2
    return acc[0]


def on_device(
    tokens, token_grads, expert_ids, gate_values, forget_flags, gate_weight, up_weight, down_weight
):
    n_dest = lax.axis_size("expert")
    n_dp = lax.axis_size("dp")
    me = lax.axis_index("expert")
    row_count, width = tokens.shape
    side = side_width(n_dest)
    match, pick = one_hot_slots(expert_ids, CAP, n_dest)
    side_cols = token_side(match, gate_values, forget_flags, n_dest)
    local_count = jnp.sum(side_cols[:, 3 * n_dest].astype(jnp.float32))
    at_col = jnp.arange(side, dtype=jnp.int32)
    count_row = jnp.where(
        at_col == 3 * n_dest + 1,
        jnp.floor(local_count / 256.0),
        jnp.where(at_col == 3 * n_dest + 2, local_count - 256.0 * jnp.floor(local_count / 256.0), 0.0),
    )
    pick_dims = (((0,), (0,)), ((), ()))
    chosen_tokens = lax.dot_general(pick, tokens, pick_dims, preferred_element_type=jnp.float32)
    chosen_grads = lax.dot_general(pick, token_grads, pick_dims, preferred_element_type=jnp.float32)
    chosen_side = lax.dot_general(pick, side_cols, pick_dims, preferred_element_type=jnp.float32)
    payload = jnp.concatenate(
        [
            chosen_tokens.astype(jnp.bfloat16),
            chosen_grads.astype(jnp.bfloat16),
            (chosen_side + count_row[None, :]).astype(jnp.bfloat16),
        ],
        axis=1,
    )
    arrived = lax.all_to_all(payload, "expert", split_axis=0, concat_axis=0, tiled=True)
    slots = arrived.shape[0]
    part_tokens = arrived[:, :width]
    raw_grads = arrived[:, width : 2 * width]
    info = arrived[:, 2 * width :].astype(jnp.float32)
    pieces = lax.dynamic_slice_in_dim(info[:, : 3 * n_dest].reshape(slots, 3, n_dest), me, 1, axis=2)
    gate_sel = (pieces[:, 0, 0] + pieces[:, 1, 0]) + pieces[:, 2, 0]
    flag = info[:, 3 * n_dest]
    by_block = info.reshape(n_dest, CAP, side)[:, 0]
    forget_count = jnp.sum(by_block[:, 3 * n_dest + 1] * 256.0 + by_block[:, 3 * n_dest + 2])
    all_rows = row_count * n_dest
    half_total = jnp.float32(all_rows) / 2.0
    weight = jnp.where(
        flag == 1.0,
        -half_total / forget_count,
        half_total / (jnp.float32(all_rows) - forget_count),
    )
    scale = gate_sel * weight
    part_grads = (scale[:, None] * raw_grads.astype(jnp.float32)).astype(jnp.bfloat16)
    both = jnp.concatenate([part_tokens, part_grads], axis=1)
    gathered = gather_dp(both, n_dp)
    slot_tokens = gathered[:, :, :width]
    slot_grads = gathered[:, :, width:]
    ff = gate_weight.shape[2]
    w_gate = gate_weight[0].reshape(n_dp, width, ff)
    w_up = up_weight[0].reshape(n_dp, width, ff)
    w_down = down_weight[0]
    chunk_dims = (((0, 2), (0, 1)), ((), ()))
    gate_pre = lax.dot_general(slot_tokens, w_gate, chunk_dims, preferred_element_type=jnp.float32)
    up_pre = lax.dot_general(slot_tokens, w_up, chunk_dims, preferred_element_type=jnp.float32)
    last_dims = (((1,), (1,)), ((), ()))
    hidden_grad = lax.dot_general(
        slot_grads[0], w_down[:, :width], last_dims, preferred_element_type=jnp.float32
    )
    for j in range(1, n_dp):
        hidden_grad = hidden_grad + lax.dot_general(
            slot_grads[j], w_down[:, j * width : (j + 1) * width], last_dims,
            preferred_element_type=jnp.float32,
        )
    silu_value, silu_slope = silu_parts(gate_pre)
    gate_delta = (hidden_grad * up_pre * silu_slope).astype(jnp.bfloat16)
    up_delta = (hidden_grad * silu_value).astype(jnp.bfloat16)
    slot_dims = (((1,), (0,)), ((), ()))
    grad_gate = lax.dot_general(
        slot_tokens, gate_delta, slot_dims, preferred_element_type=jnp.float32
    ).astype(jnp.bfloat16)
    grad_up = lax.dot_general(
        slot_tokens, up_delta, slot_dims, preferred_element_type=jnp.float32
    ).astype(jnp.bfloat16)
    back_dims = (((2,), (1,)), ((), ()))
    from_gate = lax.dot_general(w_gate, gate_delta, back_dims, preferred_element_type=jnp.float32)
    from_up = lax.dot_general(w_up, up_delta, back_dims, preferred_element_type=jnp.float32)
    part = (from_gate + from_up).astype(jnp.bfloat16)
    summed = scatter_dp(jnp.swapaxes(part, 1, 2), n_dp).astype(jnp.bfloat16)
    returned = lax.all_to_all(summed, "expert", split_axis=0, concat_axis=0, tiled=True)
    input_grad = lax.dot_general(pick, returned, slot_dims, preferred_element_type=jnp.float32)
    return (
        grad_gate.reshape(1, n_dp * width, ff),
        grad_up.reshape(1, n_dp * width, ff),
        input_grad.astype(jnp.bfloat16),
    )


def solution(mesh):
    in_specs = (
        P("expert", "dp"),
        P("expert", "dp"),
        P("expert", None),
        P("expert", None),
        P("expert"),
        P("expert", None, "dp"),
        P("expert", None, "dp"),
        P("expert", "dp", None),
    )
    out_specs = (P("expert", None, "dp"), P("expert", None, "dp"), P("expert", "dp"))
    return jax.shard_map(
        on_device, mesh=mesh, in_specs=in_specs, out_specs=out_specs, check_vma=False
    )
```

```python
import jax
import jax.numpy as jnp
from jax import lax
from jax.sharding import PartitionSpec as P
from jax.experimental import pallas as pl
from jax.experimental.pallas import tpu as pltpu

EXP_DEV = 8
CAP = 16


def glue_kernel(n_dest, width, side, split, ids_ref, gates_ref, flags_ref, tok_ref, grd_ref, *outs):
    f32, bf16 = jnp.float32, jnp.bfloat16
    rows = tok_ref.shape[0]
    slots = n_dest * CAP
    lanes = max(16, -(-n_dest // 16) * 16)
    ids = ids_ref[...]
    gates = gates_ref[...]
    flags = flags_ref[...].astype(f32)
    dest = lax.broadcasted_iota(jnp.int32, (lanes, rows), 0)
    edited = dest * EXP_DEV
    valid = dest < n_dest
    hits = jnp.zeros((lanes, rows), f32)
    gsel = jnp.zeros((lanes, rows), f32)
    for k in range(ids.shape[0]):
        m = (ids[k : k + 1, :] == edited) & valid
        hits = hits + jnp.where(m, 1.0, 0.0)
        gsel = gsel + jnp.where(m, gates[k : k + 1, :], 0.0)
    before = jnp.where(
        lax.broadcasted_iota(jnp.int32, (rows, rows), 0) < lax.broadcasted_iota(jnp.int32, (rows, rows), 1),
        1.0, 0.0,
    ).astype(bf16)
    rank = jnp.dot(hits.astype(bf16), before, preferred_element_type=f32)
    slot_of = lax.broadcasted_iota(jnp.int32, (slots, lanes), 0)
    expand = jnp.where(
        lax.shift_right_logical(slot_of, 4) == lax.broadcasted_iota(jnp.int32, (slots, lanes), 1), 1.0, 0.0
    ).astype(bf16)
    hit_s = jnp.dot(expand, hits.astype(bf16), preferred_element_type=f32)
    rank_s = jnp.dot(expand, rank.astype(bf16), preferred_element_type=f32)
    place = (lax.broadcasted_iota(jnp.int32, (slots, rows), 0) & (CAP - 1)).astype(f32)
    pick = jnp.where((hit_s == 1.0) & (rank_s == place), 1.0, 0.0)
    pick_b = pick.astype(bf16)
    tok = jnp.dot(pick_b, tok_ref[...], preferred_element_type=f32).astype(bf16)
    grd = jnp.dot(pick_b, grd_ref[...], preferred_element_type=f32).astype(bf16)
    hi = gsel.astype(bf16).astype(f32)
    rest = gsel - hi
    mid = rest.astype(bf16).astype(f32)
    lo = rest - mid

    def per_slot(x):
        spread = jnp.dot(expand, x.astype(bf16), preferred_element_type=f32)
        return jnp.sum(spread * pick, axis=1, keepdims=True)

    s_hi, s_mid, s_lo = per_slot(hi), per_slot(mid), per_slot(lo)
    s_flag = jnp.sum(pick * flags, axis=1, keepdims=True)
    count = jnp.sum(flags, axis=1, keepdims=True)
    c_hi = jnp.floor(count / 256.0)
    c_lo = count - 256.0 * c_hi
    col = lax.broadcasted_iota(jnp.int32, (slots, side), 1)
    side_v = jnp.where(col == 0, s_hi, 0.0)
    for c, v in ((1, s_mid), (2, s_lo), (3, s_flag), (4, c_hi), (5, c_lo)):
        side_v = jnp.where(col == c, v, side_v)
    side_v = side_v.astype(bf16)
    if split:
        tok_out, grd_out, side_out, pick_out = outs
        tok_out[...] = tok
        grd_out[...] = grd
        side_out[...] = side_v
    else:
        pay_out, pick_out = outs
        pay_out[:, :width] = tok
        pay_out[:, width : 2 * width] = grd
        pay_out[:, 2 * width :] = side_v
    pick_out[...] = pick_b


def glue(expert_ids, gate_values, forget_flags, tokens, token_grads, n_dest):
    import functools

    rows, width = tokens.shape
    slots = n_dest * CAP
    side = 128
    split = width % 128 != 0
    bf16 = jnp.bfloat16
    if split:
        shapes = [(slots, width), (slots, width), (slots, side), (slots, rows)]
    else:
        shapes = [(slots, 2 * width + side), (slots, rows)]
    vmem = pl.BlockSpec(memory_space=pltpu.VMEM)
    outs = pl.pallas_call(
        functools.partial(glue_kernel, n_dest, width, side, split),
        out_shape=[jax.ShapeDtypeStruct(s, bf16) for s in shapes],
        in_specs=[vmem] * 5,
        out_specs=[vmem] * len(shapes),
    )(expert_ids.T, gate_values.T, forget_flags.reshape(1, rows), tokens, token_grads)
    if split:
        return jnp.concatenate(outs[:3], axis=1), outs[3]
    return outs[0], outs[1]


def silu_parts(pre):
    sigmoid_gate = jax.nn.sigmoid(pre)
    return (pre * sigmoid_gate, sigmoid_gate * (1.0 + pre * (1.0 - sigmoid_gate)))


def bf16_part(x):
    return lax.reduce_precision(x, exponent_bits=8, mantissa_bits=7)


def partner(x, bit, n):
    return lax.ppermute(x, "dp", [(i, i ^ bit) for i in range(n)])


def gather_dp(x, n):
    me = lax.axis_index("dp")
    acc = x[None]
    bit = n // 2
    while bit >= 1:
        other = partner(acc, bit, n)
        low_first = jnp.stack([acc, other], axis=1)
        high_first = jnp.stack([other, acc], axis=1)
        acc = jnp.where((me & bit) == 0, low_first, high_first)
        acc = acc.reshape((-1,) + x.shape)
        bit //= 2
    return acc


def scatter_dp(parts, n):
    me = lax.axis_index("dp")
    acc = parts
    bit = 1
    while bit < n:
        pairs = acc.reshape((acc.shape[0] // 2, 2) + acc.shape[1:])
        mine = (me & bit) != 0
        keep = jnp.where(mine, pairs[:, 1], pairs[:, 0])
        send = jnp.where(mine, pairs[:, 0], pairs[:, 1])
        got = partner(send.astype(jnp.bfloat16), bit, n)
        acc = keep.astype(jnp.float32) + got.astype(jnp.float32)
        bit *= 2
    return acc[0]


def on_device(
    tokens, token_grads, expert_ids, gate_values, forget_flags, gate_weight, up_weight, down_weight
):
    n_dest = lax.axis_size("expert")
    n_dp = lax.axis_size("dp")
    row_count, width = tokens.shape
    payload, pick_t = glue(expert_ids, gate_values, forget_flags, tokens, token_grads, n_dest)
    side = payload.shape[1] - 2 * width
    arrived = lax.all_to_all(payload, "expert", split_axis=0, concat_axis=0, tiled=True)
    slots = arrived.shape[0]
    part_tokens = arrived[:, :width]
    raw_grads = arrived[:, width : 2 * width]
    info = arrived[:, 2 * width :].astype(jnp.float32)
    gate_sel = (info[:, 0] + info[:, 1]) + info[:, 2]
    flag = info[:, 3]
    by_block = info.reshape(n_dest, CAP, side)[:, 0]
    forget_count = jnp.sum(by_block[:, 4] * 256.0 + by_block[:, 5])
    all_rows = row_count * n_dest
    half_total = jnp.float32(all_rows) / 2.0
    weight = jnp.where(
        flag == 1.0,
        -half_total / forget_count,
        half_total / (jnp.float32(all_rows) - forget_count),
    )
    scale = gate_sel * weight
    part_grads = (scale[:, None] * raw_grads.astype(jnp.float32)).astype(jnp.bfloat16)
    both = jnp.concatenate([part_tokens, part_grads], axis=1)
    gathered = gather_dp(both, n_dp)
    slot_tokens = gathered[:, :, :width]
    slot_grads = gathered[:, :, width:]
    ff = gate_weight.shape[2]
    w_gate = gate_weight[0].reshape(n_dp, width, ff)
    w_up = up_weight[0].reshape(n_dp, width, ff)
    w_down = down_weight[0].reshape(ff, n_dp, width)
    chunk_dims = (((0, 2), (0, 1)), ((), ()))
    gate_pre = lax.dot_general(slot_tokens, w_gate, chunk_dims, preferred_element_type=jnp.float32)
    up_pre = lax.dot_general(slot_tokens, w_up, chunk_dims, preferred_element_type=jnp.float32)
    hidden_grad = lax.dot_general(
        slot_grads, w_down, (((0, 2), (1, 2)), ((), ())), preferred_element_type=jnp.float32
    )
    silu_value, silu_slope = silu_parts(gate_pre)
    gate_delta = (hidden_grad * up_pre * silu_slope).astype(jnp.bfloat16)
    up_delta = (hidden_grad * silu_value).astype(jnp.bfloat16)
    slot_dims = (((1,), (0,)), ((), ()))
    grad_gate = lax.dot_general(
        slot_tokens, gate_delta, slot_dims, preferred_element_type=jnp.float32
    ).astype(jnp.bfloat16)
    grad_up = lax.dot_general(
        slot_tokens, up_delta, slot_dims, preferred_element_type=jnp.float32
    ).astype(jnp.bfloat16)
    back_dims = (((2,), (1,)), ((), ()))
    from_gate = lax.dot_general(w_gate, gate_delta, back_dims, preferred_element_type=jnp.float32)
    from_up = lax.dot_general(w_up, up_delta, back_dims, preferred_element_type=jnp.float32)
    part = (from_gate + from_up).astype(jnp.bfloat16)
    summed = scatter_dp(jnp.swapaxes(part, 1, 2), n_dp).astype(jnp.bfloat16)
    returned = lax.all_to_all(summed, "expert", split_axis=0, concat_axis=0, tiled=True)
    input_grad = lax.dot_general(
        pick_t, returned, (((0,), (0,)), ((), ())), preferred_element_type=jnp.float32
    )
    return (
        grad_gate.reshape(1, n_dp * width, ff),
        grad_up.reshape(1, n_dp * width, ff),
        input_grad.astype(jnp.bfloat16),
    )


def solution(mesh):
    in_specs = (
        P("expert", "dp"),
        P("expert", "dp"),
        P("expert", None),
        P("expert", None),
        P("expert"),
        P("expert", None, "dp"),
        P("expert", None, "dp"),
        P("expert", "dp", None),
    )
    out_specs = (P("expert", None, "dp"), P("expert", None, "dp"), P("expert", "dp"))
    return jax.shard_map(
        on_device, mesh=mesh, in_specs=in_specs, out_specs=out_specs, check_vma=False
    )
```

```python
import jax
import jax.numpy as jnp
from jax import lax
from jax.sharding import PartitionSpec as P
from jax.experimental import pallas as pl
from jax.experimental.pallas import tpu as pltpu

EXP_DEV = 8
CAP = 16


def glue_kernel(n_dest, width, side, split, ids_ref, gates_ref, flags_ref, tok_ref, grd_ref, *outs):
    f32, bf16 = jnp.float32, jnp.bfloat16
    rows = tok_ref.shape[0]
    slots = n_dest * CAP
    lanes = max(16, -(-n_dest // 16) * 16)
    ids = ids_ref[...]
    gates = gates_ref[...]
    flags = flags_ref[...].astype(f32)
    dest = lax.broadcasted_iota(jnp.int32, (lanes, rows), 0)
    edited = dest * EXP_DEV
    valid = dest < n_dest
    hits = jnp.zeros((lanes, rows), f32)
    gsel = jnp.zeros((lanes, rows), f32)
    for k in range(ids.shape[0]):
        m = (ids[k : k + 1, :] == edited) & valid
        hits = hits + jnp.where(m, 1.0, 0.0)
        gsel = gsel + jnp.where(m, gates[k : k + 1, :], 0.0)
    before = jnp.where(
        lax.broadcasted_iota(jnp.int32, (rows, rows), 0) < lax.broadcasted_iota(jnp.int32, (rows, rows), 1),
        1.0, 0.0,
    ).astype(bf16)
    rank = jnp.dot(hits.astype(bf16), before, preferred_element_type=f32)
    slot_of = lax.broadcasted_iota(jnp.int32, (slots, lanes), 0)
    expand = jnp.where(
        lax.shift_right_logical(slot_of, 4) == lax.broadcasted_iota(jnp.int32, (slots, lanes), 1), 1.0, 0.0
    ).astype(bf16)
    hit_s = jnp.dot(expand, hits.astype(bf16), preferred_element_type=f32)
    rank_s = jnp.dot(expand, rank.astype(bf16), preferred_element_type=f32)
    place = (lax.broadcasted_iota(jnp.int32, (slots, rows), 0) & (CAP - 1)).astype(f32)
    pick = jnp.where((hit_s == 1.0) & (rank_s == place), 1.0, 0.0)
    pick_b = pick.astype(bf16)
    tok = jnp.dot(pick_b, tok_ref[...], preferred_element_type=f32).astype(bf16)
    grd = jnp.dot(pick_b, grd_ref[...], preferred_element_type=f32).astype(bf16)
    hi = gsel.astype(bf16).astype(f32)
    rest = gsel - hi
    mid = rest.astype(bf16).astype(f32)
    lo = rest - mid

    def per_slot(x):
        spread = jnp.dot(expand, x.astype(bf16), preferred_element_type=f32)
        return jnp.sum(spread * pick, axis=1, keepdims=True)

    s_hi, s_mid, s_lo = per_slot(hi), per_slot(mid), per_slot(lo)
    s_flag = jnp.sum(pick * flags, axis=1, keepdims=True)
    count = jnp.sum(flags, axis=1, keepdims=True)
    c_hi = jnp.floor(count / 256.0)
    c_lo = count - 256.0 * c_hi
    col = lax.broadcasted_iota(jnp.int32, (slots, side), 1)
    side_v = jnp.where(col == 0, s_hi, 0.0)
    for c, v in ((1, s_mid), (2, s_lo), (3, s_flag), (4, c_hi), (5, c_lo)):
        side_v = jnp.where(col == c, v, side_v)
    side_v = side_v.astype(bf16)
    if split:
        tok_out, grd_out, side_out, pick_out = outs
        tok_out[...] = tok
        grd_out[...] = grd
        side_out[...] = side_v
    else:
        pay_out, pick_out = outs
        pay_out[:, :width] = tok
        pay_out[:, width : 2 * width] = grd
        pay_out[:, 2 * width :] = side_v
    pick_out[...] = pick_b


def glue(expert_ids, gate_values, forget_flags, tokens, token_grads, n_dest):
    import functools

    rows, width = tokens.shape
    slots = n_dest * CAP
    side = 128
    split = width % 128 != 0
    bf16 = jnp.bfloat16
    if split:
        shapes = [(slots, width), (slots, width), (slots, side), (slots, rows)]
    else:
        shapes = [(slots, 2 * width + side), (slots, rows)]
    vmem = pl.BlockSpec(memory_space=pltpu.VMEM)
    outs = pl.pallas_call(
        functools.partial(glue_kernel, n_dest, width, side, split),
        out_shape=[jax.ShapeDtypeStruct(s, bf16) for s in shapes],
        in_specs=[vmem] * 5,
        out_specs=[vmem] * len(shapes),
    )(expert_ids.T, gate_values.T, forget_flags.reshape(1, rows), tokens, token_grads)
    if split:
        return jnp.concatenate(outs[:3], axis=1), outs[3]
    return outs[0], outs[1]


def silu_parts(pre):
    sigmoid_gate = jax.nn.sigmoid(pre)
    return (pre * sigmoid_gate, sigmoid_gate * (1.0 + pre * (1.0 - sigmoid_gate)))


def bf16_part(x):
    return lax.reduce_precision(x, exponent_bits=8, mantissa_bits=7)


def partner(x, bit, n):
    return lax.ppermute(x, "dp", [(i, i ^ bit) for i in range(n)])


def gather_dp(x, n):
    me = lax.axis_index("dp")
    held = [x]
    owners = [me]
    bit = n // 2
    while bit >= 1:
        stacked = jnp.stack(held)
        got = partner(stacked, bit, n)
        held = held + [got[i] for i in range(len(held))]
        owners = owners + [o ^ bit for o in owners]
        bit //= 2
    at = lax.broadcasted_iota(jnp.int32, (n, 1, 1), 0)
    out = jnp.broadcast_to(held[0][None], (n,) + x.shape)
    for piece, owner in zip(held[1:], owners[1:]):
        out = jnp.where(at == owner, piece[None], out)
    return out


def scatter_dp(parts, n):
    me = lax.axis_index("dp")
    acc = parts
    bit = 1
    while bit < n:
        pairs = acc.reshape((acc.shape[0] // 2, 2) + acc.shape[1:])
        mine = (me & bit) != 0
        keep = jnp.where(mine, pairs[:, 1], pairs[:, 0])
        send = jnp.where(mine, pairs[:, 0], pairs[:, 1])
        got = partner(send.astype(jnp.bfloat16), bit, n)
        acc = keep.astype(jnp.float32) + got.astype(jnp.float32)
        bit *= 2
    return acc[0]


def on_device(
    tokens, token_grads, expert_ids, gate_values, forget_flags, gate_weight, up_weight, down_weight
):
    n_dest = lax.axis_size("expert")
    n_dp = lax.axis_size("dp")
    row_count, width = tokens.shape
    payload, pick_t = glue(expert_ids, gate_values, forget_flags, tokens, token_grads, n_dest)
    side = payload.shape[1] - 2 * width
    arrived = lax.all_to_all(payload, "expert", split_axis=0, concat_axis=0, tiled=True)
    slots = arrived.shape[0]
    part_tokens = arrived[:, :width]
    raw_grads = arrived[:, width : 2 * width]
    info = arrived[:, 2 * width :].astype(jnp.float32)
    gate_sel = (info[:, 0] + info[:, 1]) + info[:, 2]
    flag = info[:, 3]
    first_row = jnp.where(lax.broadcasted_iota(jnp.int32, (slots,), 0) % CAP == 0, 1.0, 0.0)
    block_hi = (first_row * info[:, 4]).astype(jnp.bfloat16)
    block_lo = (first_row * info[:, 5]).astype(jnp.bfloat16)
    every = jnp.ones((slots, slots), jnp.bfloat16)
    forget_count = 256.0 * jnp.dot(every, block_hi, preferred_element_type=jnp.float32) + jnp.dot(
        every, block_lo, preferred_element_type=jnp.float32
    )
    all_rows = row_count * n_dest
    half_total = jnp.float32(all_rows) / 2.0
    weight = jnp.where(
        flag == 1.0,
        -half_total / forget_count,
        half_total / (jnp.float32(all_rows) - forget_count),
    )
    scale = gate_sel * weight
    part_grads = (scale[:, None] * raw_grads.astype(jnp.float32)).astype(jnp.bfloat16)
    both = jnp.concatenate([part_tokens, part_grads], axis=1)
    gathered = gather_dp(both, n_dp)
    slot_tokens = gathered[:, :, :width]
    slot_grads = gathered[:, :, width:]
    ff = gate_weight.shape[2]
    w_gate = gate_weight[0].reshape(n_dp, width, ff)
    w_up = up_weight[0].reshape(n_dp, width, ff)
    w_down = down_weight[0]
    chunk_dims = (((0, 2), (0, 1)), ((), ()))
    gate_pre = lax.dot_general(slot_tokens, w_gate, chunk_dims, preferred_element_type=jnp.float32)
    up_pre = lax.dot_general(slot_tokens, w_up, chunk_dims, preferred_element_type=jnp.float32)
    last_dims = (((1,), (1,)), ((), ()))
    hidden_grad = lax.dot_general(
        slot_grads[0], w_down[:, :width], last_dims, preferred_element_type=jnp.float32
    )
    for j in range(1, n_dp):
        hidden_grad = hidden_grad + lax.dot_general(
            slot_grads[j], w_down[:, j * width : (j + 1) * width], last_dims,
            preferred_element_type=jnp.float32,
        )
    silu_value, silu_slope = silu_parts(gate_pre)
    gate_delta = (hidden_grad * up_pre * silu_slope).astype(jnp.bfloat16)
    up_delta = (hidden_grad * silu_value).astype(jnp.bfloat16)
    slot_dims = (((1,), (0,)), ((), ()))
    grad_gate = lax.dot_general(
        slot_tokens, gate_delta, slot_dims, preferred_element_type=jnp.float32
    ).astype(jnp.bfloat16)
    grad_up = lax.dot_general(
        slot_tokens, up_delta, slot_dims, preferred_element_type=jnp.float32
    ).astype(jnp.bfloat16)
    back_dims = (((2,), (1,)), ((), ()))
    from_gate = lax.dot_general(w_gate, gate_delta, back_dims, preferred_element_type=jnp.float32)
    from_up = lax.dot_general(w_up, up_delta, back_dims, preferred_element_type=jnp.float32)
    part = (from_gate + from_up).astype(jnp.bfloat16)
    summed = scatter_dp(jnp.swapaxes(part, 1, 2), n_dp).astype(jnp.bfloat16)
    returned = lax.all_to_all(summed, "expert", split_axis=0, concat_axis=0, tiled=True)
    input_grad = lax.dot_general(
        pick_t, returned, (((0,), (0,)), ((), ())), preferred_element_type=jnp.float32
    )
    return (
        grad_gate.reshape(1, n_dp * width, ff),
        grad_up.reshape(1, n_dp * width, ff),
        input_grad.astype(jnp.bfloat16),
    )


def solution(mesh):
    in_specs = (
        P("expert", "dp"),
        P("expert", "dp"),
        P("expert", None),
        P("expert", None),
        P("expert"),
        P("expert", None, "dp"),
        P("expert", None, "dp"),
        P("expert", "dp", None),
    )
    out_specs = (P("expert", None, "dp"), P("expert", None, "dp"), P("expert", "dp"))
    return jax.shard_map(
        on_device, mesh=mesh, in_specs=in_specs, out_specs=out_specs, check_vma=False
    )
```

```python
import jax
import jax.numpy as jnp
from jax import lax
from jax.sharding import PartitionSpec as P
from jax.experimental import pallas as pl
from jax.experimental.pallas import tpu as pltpu

EXP_DEV = 8
CAP = 16


def glue_kernel(n_dest, width, side, split, me_ref, ids_ref, gates_ref, flags_ref, tok_ref, grd_ref, *outs):
    f32, bf16 = jnp.float32, jnp.bfloat16
    rows = tok_ref.shape[0]
    slots = n_dest * CAP
    lanes = max(16, -(-n_dest // 16) * 16)
    ids = ids_ref[...]
    gates = gates_ref[...]
    flags = flags_ref[...].astype(f32)
    dest = lax.broadcasted_iota(jnp.int32, (lanes, rows), 0)
    edited = dest * EXP_DEV
    valid = dest < n_dest
    hits = jnp.zeros((lanes, rows), f32)
    gsel = jnp.zeros((lanes, rows), f32)
    for k in range(ids.shape[0]):
        m = (ids[k : k + 1, :] == edited) & valid
        hits = hits + jnp.where(m, 1.0, 0.0)
        gsel = gsel + jnp.where(m, gates[k : k + 1, :], 0.0)
    before = jnp.where(
        lax.broadcasted_iota(jnp.int32, (rows, rows), 0) < lax.broadcasted_iota(jnp.int32, (rows, rows), 1),
        1.0, 0.0,
    ).astype(bf16)
    rank = jnp.dot(hits.astype(bf16), before, preferred_element_type=f32)
    slot_of = lax.broadcasted_iota(jnp.int32, (slots, lanes), 0)
    expand = jnp.where(
        (lax.shift_right_logical(slot_of, 4) ^ me_ref[0]) == lax.broadcasted_iota(jnp.int32, (slots, lanes), 1), 1.0, 0.0
    ).astype(bf16)
    hit_s = jnp.dot(expand, hits.astype(bf16), preferred_element_type=f32)
    rank_s = jnp.dot(expand, rank.astype(bf16), preferred_element_type=f32)
    place = (lax.broadcasted_iota(jnp.int32, (slots, rows), 0) & (CAP - 1)).astype(f32)
    pick = jnp.where((hit_s == 1.0) & (rank_s == place), 1.0, 0.0)
    pick_b = pick.astype(bf16)
    tok = jnp.dot(pick_b, tok_ref[...], preferred_element_type=f32).astype(bf16)
    grd = jnp.dot(pick_b, grd_ref[...], preferred_element_type=f32).astype(bf16)
    hi = gsel.astype(bf16).astype(f32)
    rest = gsel - hi
    mid = rest.astype(bf16).astype(f32)
    lo = rest - mid

    def per_slot(x):
        spread = jnp.dot(expand, x.astype(bf16), preferred_element_type=f32)
        return jnp.sum(spread * pick, axis=1, keepdims=True)

    s_hi, s_mid, s_lo = per_slot(hi), per_slot(mid), per_slot(lo)
    s_flag = jnp.sum(pick * flags, axis=1, keepdims=True)
    count = jnp.sum(flags, axis=1, keepdims=True)
    c_hi = jnp.floor(count / 256.0)
    c_lo = count - 256.0 * c_hi
    col = lax.broadcasted_iota(jnp.int32, (slots, side), 1)
    side_v = jnp.where(col == 0, s_hi, 0.0)
    for c, v in ((1, s_mid), (2, s_lo), (3, s_flag), (4, c_hi), (5, c_lo)):
        side_v = jnp.where(col == c, v, side_v)
    side_v = side_v.astype(bf16)
    if split:
        tok_out, grd_out, side_out, pick_out = outs
        tok_out[...] = tok
        grd_out[...] = grd
        side_out[...] = side_v
    else:
        pay_out, pick_out = outs
        pay_out[:, :width] = tok
        pay_out[:, width : 2 * width] = grd
        pay_out[:, 2 * width :] = side_v
    pick_out[...] = pick_b


def glue(me, expert_ids, gate_values, forget_flags, tokens, token_grads, n_dest):
    import functools

    rows, width = tokens.shape
    slots = n_dest * CAP
    side = 128
    split = width % 128 != 0
    bf16 = jnp.bfloat16
    if split:
        shapes = [(slots, width), (slots, width), (slots, side), (slots, rows)]
    else:
        shapes = [(slots, 2 * width + side), (slots, rows)]
    vmem = pl.BlockSpec(memory_space=pltpu.VMEM)
    outs = pl.pallas_call(
        functools.partial(glue_kernel, n_dest, width, side, split),
        out_shape=[jax.ShapeDtypeStruct(s, bf16) for s in shapes],
        in_specs=[pl.BlockSpec(memory_space=pltpu.SMEM)] + [vmem] * 5,
        out_specs=[vmem] * len(shapes),
    )(me.reshape(1), expert_ids.T, gate_values.T, forget_flags.reshape(1, rows), tokens, token_grads)
    if split:
        return jnp.concatenate(outs[:3], axis=1), outs[3]
    return outs[0], outs[1]


def silu_parts(pre):
    sigmoid_gate = jax.nn.sigmoid(pre)
    return (pre * sigmoid_gate, sigmoid_gate * (1.0 + pre * (1.0 - sigmoid_gate)))


def bf16_part(x):
    return lax.reduce_precision(x, exponent_bits=8, mantissa_bits=7)


def partner(x, bit, n):
    return lax.ppermute(x, "dp", [(i, i ^ bit) for i in range(n)])


def gather_dp(held, owners, bit, n):
    while bit >= 1:
        stacked = jnp.stack(held)
        got = partner(stacked, bit, n)
        held = held + [got[i] for i in range(len(held))]
        owners = owners + [o ^ bit for o in owners]
        bit //= 2
    at = lax.broadcasted_iota(jnp.int32, (n, 1, 1), 0)
    out = jnp.broadcast_to(held[0][None], (n,) + held[0].shape)
    for piece, owner in zip(held[1:], owners[1:]):
        out = jnp.where(at == owner, piece[None], out)
    return out


def swap(x, k, n):
    return lax.ppermute(x, "expert", [(i, i ^ k) for i in range(n)])


def scatter_dp(parts, n):
    me = lax.axis_index("dp")
    acc = parts
    bit = 1
    while bit < n:
        pairs = acc.reshape((acc.shape[0] // 2, 2) + acc.shape[1:])
        mine = (me & bit) != 0
        keep = jnp.where(mine, pairs[:, 1], pairs[:, 0])
        send = jnp.where(mine, pairs[:, 0], pairs[:, 1])
        got = partner(send.astype(jnp.bfloat16), bit, n)
        acc = keep.astype(jnp.float32) + got.astype(jnp.float32)
        bit *= 2
    return acc[0]


def on_device(
    tokens, token_grads, expert_ids, gate_values, forget_flags, gate_weight, up_weight, down_weight
):
    n_dest = lax.axis_size("expert")
    n_dp = lax.axis_size("dp")
    row_count, width = tokens.shape
    me = lax.axis_index("expert")
    me_dp = lax.axis_index("dp")
    payload, pick_t = glue(me, expert_ids, gate_values, forget_flags, tokens, token_grads, n_dest)
    side = payload.shape[1] - 2 * width
    pieces = payload.reshape(n_dest, CAP, payload.shape[1])
    half = max(n_dest // 2, 1)
    arrived_parts, across_parts = [], []
    for lo in range(0, n_dest, half):
        got = jnp.stack([pieces[0] if k == 0 else swap(pieces[k], k, n_dest) for k in range(lo, lo + half)])
        arrived_parts.append(got)
        across_parts.append(partner(got[:, :, : 2 * width], n_dp // 2, n_dp) if n_dp > 1 else None)
    arrived = jnp.concatenate(arrived_parts, axis=0).reshape(n_dest * CAP, payload.shape[1])
    slots = arrived.shape[0]
    info = arrived[:, 2 * width :].astype(jnp.float32)
    gate_sel = (info[:, 0] + info[:, 1]) + info[:, 2]
    flag = info[:, 3]
    first_row = jnp.where(lax.broadcasted_iota(jnp.int32, (slots,), 0) % CAP == 0, 1.0, 0.0)
    block_hi = (first_row * info[:, 4]).astype(jnp.bfloat16)
    block_lo = (first_row * info[:, 5]).astype(jnp.bfloat16)
    every = jnp.ones((slots, slots), jnp.bfloat16)
    forget_count = 256.0 * jnp.dot(every, block_hi, preferred_element_type=jnp.float32) + jnp.dot(
        every, block_lo, preferred_element_type=jnp.float32
    )
    all_rows = row_count * n_dest
    half_total = jnp.float32(all_rows) / 2.0
    weight = jnp.where(
        flag == 1.0,
        -half_total / forget_count,
        half_total / (jnp.float32(all_rows) - forget_count),
    )
    scale = gate_sel * weight
    own = arrived[:, : 2 * width]
    if n_dp > 1:
        across = jnp.concatenate(across_parts, axis=0).reshape(slots, 2 * width)
        gathered = gather_dp([own, across], [me_dp, me_dp ^ (n_dp // 2)], n_dp // 4, n_dp)
    else:
        gathered = own[None]
    slot_tokens = gathered[:, :, :width]
    slot_grads = (scale[None, :, None] * gathered[:, :, width:].astype(jnp.float32)).astype(jnp.bfloat16)
    ff = gate_weight.shape[2]
    w_gate = gate_weight[0].reshape(n_dp, width, ff)
    w_up = up_weight[0].reshape(n_dp, width, ff)
    w_down = down_weight[0]
    chunk_dims = (((0, 2), (0, 1)), ((), ()))
    gate_pre = lax.dot_general(slot_tokens, w_gate, chunk_dims, preferred_element_type=jnp.float32)
    up_pre = lax.dot_general(slot_tokens, w_up, chunk_dims, preferred_element_type=jnp.float32)
    last_dims = (((1,), (1,)), ((), ()))
    hidden_grad = lax.dot_general(
        slot_grads[0], w_down[:, :width], last_dims, preferred_element_type=jnp.float32
    )
    for j in range(1, n_dp):
        hidden_grad = hidden_grad + lax.dot_general(
            slot_grads[j], w_down[:, j * width : (j + 1) * width], last_dims,
            preferred_element_type=jnp.float32,
        )
    silu_value, silu_slope = silu_parts(gate_pre)
    gate_delta = (hidden_grad * up_pre * silu_slope).astype(jnp.bfloat16)
    up_delta = (hidden_grad * silu_value).astype(jnp.bfloat16)
    slot_dims = (((1,), (0,)), ((), ()))
    grad_gate = lax.dot_general(
        slot_tokens, gate_delta, slot_dims, preferred_element_type=jnp.float32
    ).astype(jnp.bfloat16)
    grad_up = lax.dot_general(
        slot_tokens, up_delta, slot_dims, preferred_element_type=jnp.float32
    ).astype(jnp.bfloat16)
    back_dims = (((2,), (1,)), ((), ()))
    from_gate = lax.dot_general(w_gate, gate_delta, back_dims, preferred_element_type=jnp.float32)
    from_up = lax.dot_general(w_up, up_delta, back_dims, preferred_element_type=jnp.float32)
    part = (from_gate + from_up).astype(jnp.bfloat16)
    summed = scatter_dp(jnp.swapaxes(part, 1, 2), n_dp).astype(jnp.bfloat16)
    back = summed.reshape(n_dest, CAP, width)
    returned = jnp.stack([back[0] if k == 0 else swap(back[k], k, n_dest) for k in range(n_dest)]).reshape(slots, width)
    input_grad = lax.dot_general(
        pick_t, returned, (((0,), (0,)), ((), ())), preferred_element_type=jnp.float32
    )
    return (
        grad_gate.reshape(1, n_dp * width, ff),
        grad_up.reshape(1, n_dp * width, ff),
        input_grad.astype(jnp.bfloat16),
    )


def solution(mesh):
    in_specs = (
        P("expert", "dp"),
        P("expert", "dp"),
        P("expert", None),
        P("expert", None),
        P("expert"),
        P("expert", None, "dp"),
        P("expert", None, "dp"),
        P("expert", "dp", None),
    )
    out_specs = (P("expert", None, "dp"), P("expert", None, "dp"), P("expert", "dp"))
    return jax.shard_map(
        on_device, mesh=mesh, in_specs=in_specs, out_specs=out_specs, check_vma=False
    )
```

```python
import jax
import jax.numpy as jnp
from jax import lax
from jax.sharding import PartitionSpec as P
from jax.experimental import pallas as pl
from jax.experimental.pallas import tpu as pltpu

EXP_DEV = 8
CAP = 16


def glue_kernel(n_dest, width, side, split, me_ref, ids_ref, gates_ref, flags_ref, tok_ref, grd_ref, *outs):
    f32, bf16 = jnp.float32, jnp.bfloat16
    rows = tok_ref.shape[0]
    slots = n_dest * CAP
    lanes = max(16, -(-n_dest // 16) * 16)
    ids = ids_ref[...]
    gates = gates_ref[...]
    flags = flags_ref[...].astype(f32)
    dest = lax.broadcasted_iota(jnp.int32, (lanes, rows), 0)
    edited = dest * EXP_DEV
    valid = dest < n_dest
    hits = jnp.zeros((lanes, rows), f32)
    gsel = jnp.zeros((lanes, rows), f32)
    for k in range(ids.shape[0]):
        m = (ids[k : k + 1, :] == edited) & valid
        hits = hits + jnp.where(m, 1.0, 0.0)
        gsel = gsel + jnp.where(m, gates[k : k + 1, :], 0.0)
    before = jnp.where(
        lax.broadcasted_iota(jnp.int32, (rows, rows), 0) < lax.broadcasted_iota(jnp.int32, (rows, rows), 1),
        1.0, 0.0,
    ).astype(bf16)
    rank = jnp.dot(hits.astype(bf16), before, preferred_element_type=f32)
    slot_of = lax.broadcasted_iota(jnp.int32, (slots, lanes), 0)
    expand = jnp.where(
        (lax.shift_right_logical(slot_of, 4) ^ me_ref[0]) == lax.broadcasted_iota(jnp.int32, (slots, lanes), 1), 1.0, 0.0
    ).astype(bf16)
    hit_s = jnp.dot(expand, hits.astype(bf16), preferred_element_type=f32)
    rank_s = jnp.dot(expand, rank.astype(bf16), preferred_element_type=f32)
    place = (lax.broadcasted_iota(jnp.int32, (slots, rows), 0) & (CAP - 1)).astype(f32)
    pick = jnp.where((hit_s == 1.0) & (rank_s == place), 1.0, 0.0)
    pick_b = pick.astype(bf16)
    expand_abs = jnp.where(
        lax.shift_right_logical(slot_of, 4) == lax.broadcasted_iota(jnp.int32, (slots, lanes), 1), 1.0, 0.0
    ).astype(bf16)
    hit_a = jnp.dot(expand_abs, hits.astype(bf16), preferred_element_type=f32)
    rank_a = jnp.dot(expand_abs, rank.astype(bf16), preferred_element_type=f32)
    pick_abs = jnp.where((hit_a == 1.0) & (rank_a == place), 1.0, 0.0).astype(bf16)
    tok = jnp.dot(pick_b, tok_ref[...], preferred_element_type=f32).astype(bf16)
    grd = jnp.dot(pick_b, grd_ref[...], preferred_element_type=f32).astype(bf16)
    hi = gsel.astype(bf16).astype(f32)
    rest = gsel - hi
    mid = rest.astype(bf16).astype(f32)
    lo = rest - mid

    def per_slot(x):
        spread = jnp.dot(expand, x.astype(bf16), preferred_element_type=f32)
        return jnp.sum(spread * pick, axis=1, keepdims=True)

    s_hi, s_mid, s_lo = per_slot(hi), per_slot(mid), per_slot(lo)
    s_flag = jnp.sum(pick * flags, axis=1, keepdims=True)
    count = jnp.sum(flags, axis=1, keepdims=True)
    c_hi = jnp.floor(count / 256.0)
    c_lo = count - 256.0 * c_hi
    col = lax.broadcasted_iota(jnp.int32, (slots, side), 1)
    side_v = jnp.where(col == 0, s_hi, 0.0)
    for c, v in ((1, s_mid), (2, s_lo), (3, s_flag), (4, c_hi), (5, c_lo)):
        side_v = jnp.where(col == c, v, side_v)
    side_v = side_v.astype(bf16)
    if split:
        tok_out, grd_out, side_out, pick_out = outs
        tok_out[...] = tok
        grd_out[...] = grd
        side_out[...] = side_v
    else:
        pay_out, pick_out = outs
        pay_out[:, :width] = tok
        pay_out[:, width : 2 * width] = grd
        pay_out[:, 2 * width :] = side_v
    pick_out[...] = pick_abs


def glue(me, expert_ids, gate_values, forget_flags, tokens, token_grads, n_dest):
    import functools

    rows, width = tokens.shape
    slots = n_dest * CAP
    side = 128
    split = width % 128 != 0
    bf16 = jnp.bfloat16
    if split:
        shapes = [(slots, width), (slots, width), (slots, side), (slots, rows)]
    else:
        shapes = [(slots, 2 * width + side), (slots, rows)]
    vmem = pl.BlockSpec(memory_space=pltpu.VMEM)
    outs = pl.pallas_call(
        functools.partial(glue_kernel, n_dest, width, side, split),
        out_shape=[jax.ShapeDtypeStruct(s, bf16) for s in shapes],
        in_specs=[pl.BlockSpec(memory_space=pltpu.SMEM)] + [vmem] * 5,
        out_specs=[vmem] * len(shapes),
    )(me.reshape(1), expert_ids.T, gate_values.T, forget_flags.reshape(1, rows), tokens, token_grads)
    if split:
        return jnp.concatenate(outs[:3], axis=1), outs[3]
    return outs[0], outs[1]


def silu_parts(pre):
    sigmoid_gate = jax.nn.sigmoid(pre)
    return (pre * sigmoid_gate, sigmoid_gate * (1.0 + pre * (1.0 - sigmoid_gate)))


def bf16_part(x):
    return lax.reduce_precision(x, exponent_bits=8, mantissa_bits=7)


def partner(x, bit, n):
    return lax.ppermute(x, "dp", [(i, i ^ bit) for i in range(n)])


def gather_dp(held, owners, bit, n):
    while bit >= 1:
        stacked = jnp.stack(held)
        got = partner(stacked, bit, n)
        held = held + [got[i] for i in range(len(held))]
        owners = owners + [o ^ bit for o in owners]
        bit //= 2
    at = lax.broadcasted_iota(jnp.int32, (n, 1, 1), 0)
    out = jnp.broadcast_to(held[0][None], (n,) + held[0].shape)
    for piece, owner in zip(held[1:], owners[1:]):
        out = jnp.where(at == owner, piece[None], out)
    return out


def swap(x, k, n):
    return lax.ppermute(x, "expert", [(i, i ^ k) for i in range(n)])


def scatter_dp(parts, n):
    me = lax.axis_index("dp")
    acc = parts
    bit = 1
    while bit < n:
        pairs = acc.reshape((acc.shape[0] // 2, 2) + acc.shape[1:])
        mine = (me & bit) != 0
        keep = jnp.where(mine, pairs[:, 1], pairs[:, 0])
        send = jnp.where(mine, pairs[:, 0], pairs[:, 1])
        got = partner(send.astype(jnp.bfloat16), bit, n)
        acc = keep.astype(jnp.float32) + got.astype(jnp.float32)
        bit *= 2
    return acc[0]


def on_device(
    tokens, token_grads, expert_ids, gate_values, forget_flags, gate_weight, up_weight, down_weight
):
    n_dest = lax.axis_size("expert")
    n_dp = lax.axis_size("dp")
    row_count, width = tokens.shape
    me = lax.axis_index("expert")
    me_dp = lax.axis_index("dp")
    payload, pick_t = glue(me, expert_ids, gate_values, forget_flags, tokens, token_grads, n_dest)
    side = payload.shape[1] - 2 * width
    pieces = payload.reshape(n_dest, CAP, payload.shape[1])
    half = max(n_dest // 2, 1)
    arrived_parts, across_parts = [], []
    for lo in range(0, n_dest, half):
        got = jnp.stack([pieces[0] if k == 0 else swap(pieces[k], k, n_dest) for k in range(lo, lo + half)])
        arrived_parts.append(got)
        across_parts.append(partner(got[:, :, : 2 * width], n_dp // 2, n_dp) if n_dp > 1 else None)
    arrived = jnp.concatenate(arrived_parts, axis=0).reshape(n_dest * CAP, payload.shape[1])
    slots = arrived.shape[0]
    info = arrived[:, 2 * width :].astype(jnp.float32)
    gate_sel = (info[:, 0] + info[:, 1]) + info[:, 2]
    flag = info[:, 3]
    first_row = jnp.where(lax.broadcasted_iota(jnp.int32, (slots,), 0) % CAP == 0, 1.0, 0.0)
    block_hi = (first_row * info[:, 4]).astype(jnp.bfloat16)
    block_lo = (first_row * info[:, 5]).astype(jnp.bfloat16)
    every = jnp.ones((slots, slots), jnp.bfloat16)
    forget_count = 256.0 * jnp.dot(every, block_hi, preferred_element_type=jnp.float32) + jnp.dot(
        every, block_lo, preferred_element_type=jnp.float32
    )
    all_rows = row_count * n_dest
    half_total = jnp.float32(all_rows) / 2.0
    weight = jnp.where(
        flag == 1.0,
        -half_total / forget_count,
        half_total / (jnp.float32(all_rows) - forget_count),
    )
    scale = gate_sel * weight
    own = arrived[:, : 2 * width]
    if n_dp > 1:
        across = jnp.concatenate(across_parts, axis=0).reshape(slots, 2 * width)
        gathered = gather_dp([own, across], [me_dp, me_dp ^ (n_dp // 2)], n_dp // 4, n_dp)
    else:
        gathered = own[None]
    slot_tokens = gathered[:, :, :width]
    slot_grads = (scale[None, :, None] * gathered[:, :, width:].astype(jnp.float32)).astype(jnp.bfloat16)
    ff = gate_weight.shape[2]
    w_gate = gate_weight[0].reshape(n_dp, width, ff)
    w_up = up_weight[0].reshape(n_dp, width, ff)
    w_down = down_weight[0]
    chunk_dims = (((0, 2), (0, 1)), ((), ()))
    gate_pre = lax.dot_general(slot_tokens, w_gate, chunk_dims, preferred_element_type=jnp.float32)
    up_pre = lax.dot_general(slot_tokens, w_up, chunk_dims, preferred_element_type=jnp.float32)
    last_dims = (((1,), (1,)), ((), ()))
    hidden_grad = lax.dot_general(
        slot_grads[0], w_down[:, :width], last_dims, preferred_element_type=jnp.float32
    )
    for j in range(1, n_dp):
        hidden_grad = hidden_grad + lax.dot_general(
            slot_grads[j], w_down[:, j * width : (j + 1) * width], last_dims,
            preferred_element_type=jnp.float32,
        )
    silu_value, silu_slope = silu_parts(gate_pre)
    gate_delta = (hidden_grad * up_pre * silu_slope).astype(jnp.bfloat16)
    up_delta = (hidden_grad * silu_value).astype(jnp.bfloat16)
    slot_dims = (((1,), (0,)), ((), ()))
    grad_gate = lax.dot_general(
        slot_tokens, gate_delta, slot_dims, preferred_element_type=jnp.float32
    ).astype(jnp.bfloat16)
    grad_up = lax.dot_general(
        slot_tokens, up_delta, slot_dims, preferred_element_type=jnp.float32
    ).astype(jnp.bfloat16)
    back_dims = (((2,), (1,)), ((), ()))
    from_gate = lax.dot_general(w_gate, gate_delta, back_dims, preferred_element_type=jnp.float32)
    from_up = lax.dot_general(w_up, up_delta, back_dims, preferred_element_type=jnp.float32)
    part = (from_gate + from_up).astype(jnp.bfloat16)
    summed = scatter_dp(jnp.swapaxes(part, 1, 2), n_dp).astype(jnp.bfloat16)
    back = summed.reshape(n_dest, CAP, width)
    in_order = jnp.take(back, jnp.arange(n_dest, dtype=jnp.int32) ^ me, axis=0).reshape(slots, width)
    returned = lax.all_to_all(in_order, "expert", split_axis=0, concat_axis=0, tiled=True)
    input_grad = lax.dot_general(
        pick_t, returned, (((0,), (0,)), ((), ())), preferred_element_type=jnp.float32
    )
    return (
        grad_gate.reshape(1, n_dp * width, ff),
        grad_up.reshape(1, n_dp * width, ff),
        input_grad.astype(jnp.bfloat16),
    )


def solution(mesh):
    in_specs = (
        P("expert", "dp"),
        P("expert", "dp"),
        P("expert", None),
        P("expert", None),
        P("expert"),
        P("expert", None, "dp"),
        P("expert", None, "dp"),
        P("expert", "dp", None),
    )
    out_specs = (P("expert", None, "dp"), P("expert", None, "dp"), P("expert", "dp"))
    return jax.shard_map(
        on_device, mesh=mesh, in_specs=in_specs, out_specs=out_specs, check_vma=False
    )
```

```python
import jax
import jax.numpy as jnp
from jax import lax
from jax.sharding import PartitionSpec as P
from jax.experimental import pallas as pl
from jax.experimental.pallas import tpu as pltpu

EXP_DEV = 8
CAP = 16


def glue_kernel(n_dest, width, side, split, ids_ref, gates_ref, flags_ref, tok_ref, grd_ref, *outs):
    f32, bf16 = jnp.float32, jnp.bfloat16
    rows = tok_ref.shape[0]
    slots = n_dest * CAP
    lanes = max(16, -(-n_dest // 16) * 16)
    ids = ids_ref[...]
    gates = gates_ref[...]
    flags = flags_ref[...].astype(f32)
    dest = lax.broadcasted_iota(jnp.int32, (lanes, rows), 0)
    edited = dest * EXP_DEV
    valid = dest < n_dest
    hits = jnp.zeros((lanes, rows), f32)
    gsel = jnp.zeros((lanes, rows), f32)
    for k in range(ids.shape[0]):
        m = (ids[k : k + 1, :] == edited) & valid
        hits = hits + jnp.where(m, 1.0, 0.0)
        gsel = gsel + jnp.where(m, gates[k : k + 1, :], 0.0)
    before = jnp.where(
        lax.broadcasted_iota(jnp.int32, (rows, rows), 0) < lax.broadcasted_iota(jnp.int32, (rows, rows), 1),
        1.0, 0.0,
    ).astype(bf16)
    rank = jnp.dot(hits.astype(bf16), before, preferred_element_type=f32)
    slot_of = lax.broadcasted_iota(jnp.int32, (slots, lanes), 0)
    expand = jnp.where(
        lax.shift_right_logical(slot_of, 4) == lax.broadcasted_iota(jnp.int32, (slots, lanes), 1), 1.0, 0.0
    ).astype(bf16)
    hit_s = jnp.dot(expand, hits.astype(bf16), preferred_element_type=f32)
    rank_s = jnp.dot(expand, rank.astype(bf16), preferred_element_type=f32)
    place = (lax.broadcasted_iota(jnp.int32, (slots, rows), 0) & (CAP - 1)).astype(f32)
    pick = jnp.where((hit_s == 1.0) & (rank_s == place), 1.0, 0.0)
    pick_b = pick.astype(bf16)
    tok = jnp.dot(pick_b, tok_ref[...], preferred_element_type=f32).astype(bf16)
    grd = jnp.dot(pick_b, grd_ref[...], preferred_element_type=f32).astype(bf16)
    hi = gsel.astype(bf16).astype(f32)
    rest = gsel - hi
    mid = rest.astype(bf16).astype(f32)
    lo = rest - mid

    def per_slot(x):
        spread = jnp.dot(expand, x.astype(bf16), preferred_element_type=f32)
        return jnp.sum(spread * pick, axis=1, keepdims=True)

    s_hi, s_mid, s_lo = per_slot(hi), per_slot(mid), per_slot(lo)
    s_flag = jnp.sum(pick * flags, axis=1, keepdims=True)
    count = jnp.sum(flags, axis=1, keepdims=True)
    c_hi = jnp.floor(count / 256.0)
    c_lo = count - 256.0 * c_hi
    col = lax.broadcasted_iota(jnp.int32, (slots, side), 1)
    side_v = jnp.where(col == 0, s_hi, 0.0)
    for c, v in ((1, s_mid), (2, s_lo), (3, s_flag), (4, c_hi), (5, c_lo)):
        side_v = jnp.where(col == c, v, side_v)
    side_v = side_v.astype(bf16)
    if split:
        tok_out, grd_out, side_out, pick_out = outs
        tok_out[...] = tok
        grd_out[...] = grd
        side_out[...] = side_v
    else:
        pay_out, pick_out = outs
        pay_out[:, :width] = tok
        pay_out[:, width : 2 * width] = grd
        pay_out[:, 2 * width :] = side_v
    pick_out[...] = pick_b


def glue(expert_ids, gate_values, forget_flags, tokens, token_grads, n_dest):
    import functools

    rows, width = tokens.shape
    slots = n_dest * CAP
    side = 128
    split = width % 128 != 0
    bf16 = jnp.bfloat16
    if split:
        shapes = [(slots, width), (slots, width), (slots, side), (slots, rows)]
    else:
        shapes = [(slots, 2 * width + side), (slots, rows)]
    vmem = pl.BlockSpec(memory_space=pltpu.VMEM)
    outs = pl.pallas_call(
        functools.partial(glue_kernel, n_dest, width, side, split),
        out_shape=[jax.ShapeDtypeStruct(s, bf16) for s in shapes],
        in_specs=[vmem] * 5,
        out_specs=[vmem] * len(shapes),
    )(expert_ids.T, gate_values.T, forget_flags.reshape(1, rows), tokens, token_grads)
    if split:
        return jnp.concatenate(outs[:3], axis=1), outs[3]
    return outs[0], outs[1]


def silu_parts(pre):
    sigmoid_gate = jax.nn.sigmoid(pre)
    return (pre * sigmoid_gate, sigmoid_gate * (1.0 + pre * (1.0 - sigmoid_gate)))


def bf16_part(x):
    return lax.reduce_precision(x, exponent_bits=8, mantissa_bits=7)


def partner(x, bit, n):
    return lax.ppermute(x, "dp", [(i, i ^ bit) for i in range(n)])


def gather_dp(x, n):
    me = lax.axis_index("dp")
    held = [x]
    owners = [me]
    bit = n // 2
    while bit >= 1:
        stacked = jnp.stack(held)
        got = partner(stacked, bit, n)
        held = held + [got[i] for i in range(len(held))]
        owners = owners + [o ^ bit for o in owners]
        bit //= 2
    at = lax.broadcasted_iota(jnp.int32, (n, 1, 1), 0)
    out = jnp.broadcast_to(held[0][None], (n,) + x.shape)
    for piece, owner in zip(held[1:], owners[1:]):
        out = jnp.where(at == owner, piece[None], out)
    return out


def gather_half(x, n):
    me = lax.axis_index("dp")
    top = n // 2
    base = me & top
    held = [x]
    owners = [me]
    bit = top // 2
    while bit >= 1:
        stacked = jnp.stack(held)
        got = partner(stacked, bit, n)
        held = held + [got[i] for i in range(len(held))]
        owners = owners + [o ^ bit for o in owners]
        bit //= 2
    at = lax.broadcasted_iota(jnp.int32, (top, 1, 1), 0)
    out = jnp.broadcast_to(held[0][None], (top,) + x.shape)
    for piece, owner in zip(held[1:], owners[1:]):
        out = jnp.where(at == owner - base, piece[None], out)
    return out, base


def scatter_dp(parts, n):
    me = lax.axis_index("dp")
    acc = parts
    bit = 1
    while bit < n:
        pairs = acc.reshape((acc.shape[0] // 2, 2) + acc.shape[1:])
        mine = (me & bit) != 0
        keep = jnp.where(mine, pairs[:, 1], pairs[:, 0])
        send = jnp.where(mine, pairs[:, 0], pairs[:, 1])
        got = partner(send.astype(jnp.bfloat16), bit, n)
        acc = keep.astype(jnp.float32) + got.astype(jnp.float32)
        bit *= 2
    return acc[0]


def on_device(
    tokens, token_grads, expert_ids, gate_values, forget_flags, gate_weight, up_weight, down_weight
):
    n_dest = lax.axis_size("expert")
    n_dp = lax.axis_size("dp")
    row_count, width = tokens.shape
    me_dp = lax.axis_index("dp")
    w_down = down_weight[0]
    top = n_dp // 2
    half_cols = (n_dp * width) // 2
    if n_dp > 1:
        upper_half = (me_dp & top) != 0
        lend = jnp.where(upper_half, w_down[:, :half_cols], w_down[:, half_cols:])
        borrowed = partner(lend, top, n_dp)
    payload, pick_t = glue(expert_ids, gate_values, forget_flags, tokens, token_grads, n_dest)
    side = payload.shape[1] - 2 * width
    arrived = lax.all_to_all(payload, "expert", split_axis=0, concat_axis=0, tiled=True)
    slots = arrived.shape[0]
    part_tokens = arrived[:, :width]
    raw_grads = arrived[:, width : 2 * width]
    info = arrived[:, 2 * width :].astype(jnp.float32)
    gate_sel = (info[:, 0] + info[:, 1]) + info[:, 2]
    flag = info[:, 3]
    first_row = jnp.where(lax.broadcasted_iota(jnp.int32, (slots,), 0) % CAP == 0, 1.0, 0.0)
    block_hi = (first_row * info[:, 4]).astype(jnp.bfloat16)
    block_lo = (first_row * info[:, 5]).astype(jnp.bfloat16)
    every = jnp.ones((slots, slots), jnp.bfloat16)
    forget_count = 256.0 * jnp.dot(every, block_hi, preferred_element_type=jnp.float32) + jnp.dot(
        every, block_lo, preferred_element_type=jnp.float32
    )
    all_rows = row_count * n_dest
    half_total = jnp.float32(all_rows) / 2.0
    weight = jnp.where(
        flag == 1.0,
        -half_total / forget_count,
        half_total / (jnp.float32(all_rows) - forget_count),
    )
    scale = gate_sel * weight
    part_grads = (scale[:, None] * raw_grads.astype(jnp.float32)).astype(jnp.bfloat16)
    ff = gate_weight.shape[2]
    w_gate = gate_weight[0].reshape(n_dp, width, ff)
    w_up = up_weight[0].reshape(n_dp, width, ff)
    last_dims = (((1,), (1,)), ((), ()))
    slot_tokens = gather_dp(part_tokens, n_dp)
    if n_dp > 1:
        half_grads, base = gather_half(part_grads, n_dp)
        hidden_grad = None
        lent = None
        for i in range(top):
            mine = lax.dot_general(
                half_grads[i], lax.dynamic_slice_in_dim(w_down, (base + i) * width, width, axis=1),
                last_dims, preferred_element_type=jnp.float32,
            )
            theirs = lax.dot_general(
                half_grads[i], borrowed[:, i * width : (i + 1) * width], last_dims,
                preferred_element_type=jnp.float32,
            )
            hidden_grad = mine if hidden_grad is None else hidden_grad + mine
            lent = theirs if lent is None else lent + theirs
        hidden_grad = hidden_grad + partner(lent, top, n_dp)
    else:
        hidden_grad = lax.dot_general(part_grads, w_down, last_dims, preferred_element_type=jnp.float32)
    chunk_dims = (((0, 2), (0, 1)), ((), ()))
    gate_pre = lax.dot_general(slot_tokens, w_gate, chunk_dims, preferred_element_type=jnp.float32)
    up_pre = lax.dot_general(slot_tokens, w_up, chunk_dims, preferred_element_type=jnp.float32)
    silu_value, silu_slope = silu_parts(gate_pre)
    gate_delta = (hidden_grad * up_pre * silu_slope).astype(jnp.bfloat16)
    up_delta = (hidden_grad * silu_value).astype(jnp.bfloat16)
    slot_dims = (((1,), (0,)), ((), ()))
    grad_gate = lax.dot_general(
        slot_tokens, gate_delta, slot_dims, preferred_element_type=jnp.float32
    ).astype(jnp.bfloat16)
    grad_up = lax.dot_general(
        slot_tokens, up_delta, slot_dims, preferred_element_type=jnp.float32
    ).astype(jnp.bfloat16)
    back_dims = (((2,), (1,)), ((), ()))
    from_gate = lax.dot_general(w_gate, gate_delta, back_dims, preferred_element_type=jnp.float32)
    from_up = lax.dot_general(w_up, up_delta, back_dims, preferred_element_type=jnp.float32)
    part = (from_gate + from_up).astype(jnp.bfloat16)
    summed = scatter_dp(jnp.swapaxes(part, 1, 2), n_dp).astype(jnp.bfloat16)
    returned = lax.all_to_all(summed, "expert", split_axis=0, concat_axis=0, tiled=True)
    input_grad = lax.dot_general(
        pick_t, returned, (((0,), (0,)), ((), ())), preferred_element_type=jnp.float32
    )
    return (
        grad_gate.reshape(1, n_dp * width, ff),
        grad_up.reshape(1, n_dp * width, ff),
        input_grad.astype(jnp.bfloat16),
    )


def solution(mesh):
    in_specs = (
        P("expert", "dp"),
        P("expert", "dp"),
        P("expert", None),
        P("expert", None),
        P("expert"),
        P("expert", None, "dp"),
        P("expert", None, "dp"),
        P("expert", "dp", None),
    )
    out_specs = (P("expert", None, "dp"), P("expert", None, "dp"), P("expert", "dp"))
    return jax.shard_map(
        on_device, mesh=mesh, in_specs=in_specs, out_specs=out_specs, check_vma=False
    )
```

```python
import jax
import jax.numpy as jnp
from jax import lax
from jax.sharding import PartitionSpec as P
from jax.experimental import pallas as pl
from jax.experimental.pallas import tpu as pltpu

EXP_DEV = 8
CAP = 16


def glue_kernel(n_dest, width, side, split, ids_ref, gates_ref, flags_ref, tok_ref, grd_ref, *outs):
    f32, bf16 = jnp.float32, jnp.bfloat16
    rows = tok_ref.shape[0]
    slots = n_dest * CAP
    lanes = max(16, -(-n_dest // 16) * 16)
    ids = ids_ref[...]
    gates = gates_ref[...]
    flags = flags_ref[...].astype(f32)
    dest = lax.broadcasted_iota(jnp.int32, (lanes, rows), 0)
    edited = dest * EXP_DEV
    valid = dest < n_dest
    hits = jnp.zeros((lanes, rows), f32)
    gsel = jnp.zeros((lanes, rows), f32)
    for k in range(ids.shape[0]):
        m = (ids[k : k + 1, :] == edited) & valid
        hits = hits + jnp.where(m, 1.0, 0.0)
        gsel = gsel + jnp.where(m, gates[k : k + 1, :], 0.0)
    before = jnp.where(
        lax.broadcasted_iota(jnp.int32, (rows, rows), 0) < lax.broadcasted_iota(jnp.int32, (rows, rows), 1),
        1.0, 0.0,
    ).astype(bf16)
    rank = jnp.dot(hits.astype(bf16), before, preferred_element_type=f32)
    slot_of = lax.broadcasted_iota(jnp.int32, (slots, lanes), 0)
    expand = jnp.where(
        lax.shift_right_logical(slot_of, 4) == lax.broadcasted_iota(jnp.int32, (slots, lanes), 1), 1.0, 0.0
    ).astype(bf16)
    hit_s = jnp.dot(expand, hits.astype(bf16), preferred_element_type=f32)
    rank_s = jnp.dot(expand, rank.astype(bf16), preferred_element_type=f32)
    place = (lax.broadcasted_iota(jnp.int32, (slots, rows), 0) & (CAP - 1)).astype(f32)
    pick = jnp.where((hit_s == 1.0) & (rank_s == place), 1.0, 0.0)
    pick_b = pick.astype(bf16)
    tok = jnp.dot(pick_b, tok_ref[...], preferred_element_type=f32).astype(bf16)
    grd = jnp.dot(pick_b, grd_ref[...], preferred_element_type=f32).astype(bf16)
    hi = gsel.astype(bf16).astype(f32)
    rest = gsel - hi
    mid = rest.astype(bf16).astype(f32)
    lo = rest - mid

    def per_slot(x):
        spread = jnp.dot(expand, x.astype(bf16), preferred_element_type=f32)
        return jnp.sum(spread * pick, axis=1, keepdims=True)

    s_hi, s_mid, s_lo = per_slot(hi), per_slot(mid), per_slot(lo)
    s_flag = jnp.sum(pick * flags, axis=1, keepdims=True)
    count = jnp.sum(flags, axis=1, keepdims=True)
    c_hi = jnp.floor(count / 256.0)
    c_lo = count - 256.0 * c_hi
    col = lax.broadcasted_iota(jnp.int32, (slots, side), 1)
    side_v = jnp.where(col == 0, s_hi, 0.0)
    for c, v in ((1, s_mid), (2, s_lo), (3, s_flag), (4, c_hi), (5, c_lo)):
        side_v = jnp.where(col == c, v, side_v)
    side_v = side_v.astype(bf16)
    if split:
        tok_out, grd_out, side_out, pick_out = outs
        tok_out[...] = tok
        grd_out[...] = grd
        side_out[...] = side_v
    else:
        pay_out, pick_out = outs
        pay_out[:, :width] = tok
        pay_out[:, width : 2 * width] = grd
        pay_out[:, 2 * width :] = side_v
    pick_out[...] = pick_b


def glue(expert_ids, gate_values, forget_flags, tokens, token_grads, n_dest):
    import functools

    rows, width = tokens.shape
    slots = n_dest * CAP
    side = 128
    split = width % 128 != 0
    bf16 = jnp.bfloat16
    if split:
        shapes = [(slots, width), (slots, width), (slots, side), (slots, rows)]
    else:
        shapes = [(slots, 2 * width + side), (slots, rows)]
    vmem = pl.BlockSpec(memory_space=pltpu.VMEM)
    outs = pl.pallas_call(
        functools.partial(glue_kernel, n_dest, width, side, split),
        out_shape=[jax.ShapeDtypeStruct(s, bf16) for s in shapes],
        in_specs=[vmem] * 5,
        out_specs=[vmem] * len(shapes),
    )(expert_ids.T, gate_values.T, forget_flags.reshape(1, rows), tokens, token_grads)
    if split:
        return jnp.concatenate(outs[:3], axis=1), outs[3]
    return outs[0], outs[1]


def silu_parts(pre):
    sigmoid_gate = jax.nn.sigmoid(pre)
    return (pre * sigmoid_gate, sigmoid_gate * (1.0 + pre * (1.0 - sigmoid_gate)))


def bf16_part(x):
    return lax.reduce_precision(x, exponent_bits=8, mantissa_bits=7)


def partner(x, bit, n):
    return lax.ppermute(x, "dp", [(i, i ^ bit) for i in range(n)])


def gather_dp(x, n):
    me = lax.axis_index("dp")
    held = [x]
    owners = [me]
    bit = n // 2
    while bit >= 1:
        stacked = jnp.stack(held)
        got = partner(stacked, bit, n)
        held = held + [got[i] for i in range(len(held))]
        owners = owners + [o ^ bit for o in owners]
        bit //= 2
    at = lax.broadcasted_iota(jnp.int32, (n, 1, 1), 0)
    out = jnp.broadcast_to(held[0][None], (n,) + x.shape)
    for piece, owner in zip(held[1:], owners[1:]):
        out = jnp.where(at == owner, piece[None], out)
    return out


def gather_half(x, n):
    me = lax.axis_index("dp")
    top = n // 2
    base = me & top
    held = [x]
    owners = [me]
    bit = top // 2
    while bit >= 1:
        stacked = jnp.stack(held)
        got = partner(stacked, bit, n)
        held = held + [got[i] for i in range(len(held))]
        owners = owners + [o ^ bit for o in owners]
        bit //= 2
    at = lax.broadcasted_iota(jnp.int32, (top, 1, 1), 0)
    out = jnp.broadcast_to(held[0][None], (top,) + x.shape)
    for piece, owner in zip(held[1:], owners[1:]):
        out = jnp.where(at == owner - base, piece[None], out)
    return out, base


def scatter_dp(parts, n):
    me = lax.axis_index("dp")
    acc = parts
    bit = 1
    while bit < n:
        pairs = acc.reshape((acc.shape[0] // 2, 2) + acc.shape[1:])
        mine = (me & bit) != 0
        keep = jnp.where(mine, pairs[:, 1], pairs[:, 0])
        send = jnp.where(mine, pairs[:, 0], pairs[:, 1])
        got = partner(send.astype(jnp.bfloat16), bit, n)
        acc = keep.astype(jnp.float32) + got.astype(jnp.float32)
        bit *= 2
    return acc[0]


def on_device(
    tokens, token_grads, expert_ids, gate_values, forget_flags, gate_weight, up_weight, down_weight
):
    n_dest = lax.axis_size("expert")
    n_dp = lax.axis_size("dp")
    row_count, width = tokens.shape
    me_dp = lax.axis_index("dp")
    w_down = down_weight[0]
    top = n_dp // 2
    half_cols = (n_dp * width) // 2
    if n_dp > 1:
        upper_half = (me_dp & top) != 0
        lend = jnp.where(upper_half, w_down[:, :half_cols], w_down[:, half_cols:])
        keep = jnp.where(upper_half, w_down[:, half_cols:], w_down[:, :half_cols])
        borrowed = partner(lend, top, n_dp)
    payload, pick_t = glue(expert_ids, gate_values, forget_flags, tokens, token_grads, n_dest)
    side = payload.shape[1] - 2 * width
    arrived = lax.all_to_all(payload, "expert", split_axis=0, concat_axis=0, tiled=True)
    slots = arrived.shape[0]
    part_tokens = arrived[:, :width]
    raw_grads = arrived[:, width : 2 * width]
    info = arrived[:, 2 * width :].astype(jnp.float32)
    gate_sel = (info[:, 0] + info[:, 1]) + info[:, 2]
    flag = info[:, 3]
    first_row = jnp.where(lax.broadcasted_iota(jnp.int32, (slots,), 0) % CAP == 0, 1.0, 0.0)
    block_hi = (first_row * info[:, 4]).astype(jnp.bfloat16)
    block_lo = (first_row * info[:, 5]).astype(jnp.bfloat16)
    every = jnp.ones((slots, slots), jnp.bfloat16)
    forget_count = 256.0 * jnp.dot(every, block_hi, preferred_element_type=jnp.float32) + jnp.dot(
        every, block_lo, preferred_element_type=jnp.float32
    )
    all_rows = row_count * n_dest
    half_total = jnp.float32(all_rows) / 2.0
    weight = jnp.where(
        flag == 1.0,
        -half_total / forget_count,
        half_total / (jnp.float32(all_rows) - forget_count),
    )
    scale = gate_sel * weight
    part_grads = (scale[:, None] * raw_grads.astype(jnp.float32)).astype(jnp.bfloat16)
    ff = gate_weight.shape[2]
    w_gate = gate_weight[0].reshape(n_dp, width, ff)
    w_up = up_weight[0].reshape(n_dp, width, ff)
    last_dims = (((1,), (1,)), ((), ()))
    slot_tokens = gather_dp(part_tokens, n_dp)
    if n_dp > 1:
        half_grads, _ = gather_half(part_grads, n_dp)
        hidden_grad = None
        lent = None
        for i in range(top):
            mine = lax.dot_general(
                half_grads[i], keep[:, i * width : (i + 1) * width],
                last_dims, preferred_element_type=jnp.float32,
            )
            theirs = lax.dot_general(
                half_grads[i], borrowed[:, i * width : (i + 1) * width], last_dims,
                preferred_element_type=jnp.float32,
            )
            hidden_grad = mine if hidden_grad is None else hidden_grad + mine
            lent = theirs if lent is None else lent + theirs
        hidden_grad = hidden_grad + partner(lent, top, n_dp)
    else:
        hidden_grad = lax.dot_general(part_grads, w_down, last_dims, preferred_element_type=jnp.float32)
    chunk_dims = (((0, 2), (0, 1)), ((), ()))
    gate_pre = lax.dot_general(slot_tokens, w_gate, chunk_dims, preferred_element_type=jnp.float32)
    up_pre = lax.dot_general(slot_tokens, w_up, chunk_dims, preferred_element_type=jnp.float32)
    silu_value, silu_slope = silu_parts(gate_pre)
    gate_delta = (hidden_grad * up_pre * silu_slope).astype(jnp.bfloat16)
    up_delta = (hidden_grad * silu_value).astype(jnp.bfloat16)
    slot_dims = (((1,), (0,)), ((), ()))
    grad_gate = lax.dot_general(
        slot_tokens, gate_delta, slot_dims, preferred_element_type=jnp.float32
    ).astype(jnp.bfloat16)
    grad_up = lax.dot_general(
        slot_tokens, up_delta, slot_dims, preferred_element_type=jnp.float32
    ).astype(jnp.bfloat16)
    back_dims = (((2,), (1,)), ((), ()))
    from_gate = lax.dot_general(w_gate, gate_delta, back_dims, preferred_element_type=jnp.float32)
    from_up = lax.dot_general(w_up, up_delta, back_dims, preferred_element_type=jnp.float32)
    part = (from_gate + from_up).astype(jnp.bfloat16)
    summed = scatter_dp(jnp.swapaxes(part, 1, 2), n_dp).astype(jnp.bfloat16)
    returned = lax.all_to_all(summed, "expert", split_axis=0, concat_axis=0, tiled=True)
    input_grad = lax.dot_general(
        pick_t, returned, (((0,), (0,)), ((), ())), preferred_element_type=jnp.float32
    )
    return (
        grad_gate.reshape(1, n_dp * width, ff),
        grad_up.reshape(1, n_dp * width, ff),
        input_grad.astype(jnp.bfloat16),
    )


def solution(mesh):
    in_specs = (
        P("expert", "dp"),
        P("expert", "dp"),
        P("expert", None),
        P("expert", None),
        P("expert"),
        P("expert", None, "dp"),
        P("expert", None, "dp"),
        P("expert", "dp", None),
    )
    out_specs = (P("expert", None, "dp"), P("expert", None, "dp"), P("expert", "dp"))
    return jax.shard_map(
        on_device, mesh=mesh, in_specs=in_specs, out_specs=out_specs, check_vma=False
    )
```

```python
import jax
import jax.numpy as jnp
from jax import lax
from jax.sharding import PartitionSpec as P
from jax.experimental import pallas as pl
from jax.experimental.pallas import tpu as pltpu

EXP_DEV = 8
CAP = 16


def glue_kernel(n_dest, width, side, split, ids_ref, gates_ref, flags_ref, tok_ref, grd_ref, *outs):
    f32, bf16 = jnp.float32, jnp.bfloat16
    rows = tok_ref.shape[0]
    slots = n_dest * CAP
    lanes = max(16, -(-n_dest // 16) * 16)
    ids = ids_ref[...]
    gates = gates_ref[...]
    flags = flags_ref[...].astype(f32)
    dest = lax.broadcasted_iota(jnp.int32, (lanes, rows), 0)
    edited = dest * EXP_DEV
    valid = dest < n_dest
    hits = jnp.zeros((lanes, rows), f32)
    gsel = jnp.zeros((lanes, rows), f32)
    for k in range(ids.shape[0]):
        m = (ids[k : k + 1, :] == edited) & valid
        hits = hits + jnp.where(m, 1.0, 0.0)
        gsel = gsel + jnp.where(m, gates[k : k + 1, :], 0.0)
    before = jnp.where(
        lax.broadcasted_iota(jnp.int32, (rows, rows), 0) < lax.broadcasted_iota(jnp.int32, (rows, rows), 1),
        1.0, 0.0,
    ).astype(bf16)
    rank = jnp.dot(hits.astype(bf16), before, preferred_element_type=f32)
    slot_of = lax.broadcasted_iota(jnp.int32, (slots, lanes), 0)
    expand = jnp.where(
        lax.shift_right_logical(slot_of, 4) == lax.broadcasted_iota(jnp.int32, (slots, lanes), 1), 1.0, 0.0
    ).astype(bf16)
    hit_s = jnp.dot(expand, hits.astype(bf16), preferred_element_type=f32)
    rank_s = jnp.dot(expand, rank.astype(bf16), preferred_element_type=f32)
    place = (lax.broadcasted_iota(jnp.int32, (slots, rows), 0) & (CAP - 1)).astype(f32)
    pick = jnp.where((hit_s == 1.0) & (rank_s == place), 1.0, 0.0)
    pick_b = pick.astype(bf16)
    tok = jnp.dot(pick_b, tok_ref[...], preferred_element_type=f32).astype(bf16)
    grd = jnp.dot(pick_b, grd_ref[...], preferred_element_type=f32).astype(bf16)
    hi = gsel.astype(bf16).astype(f32)
    rest = gsel - hi
    mid = rest.astype(bf16).astype(f32)
    lo = rest - mid

    def per_slot(x):
        spread = jnp.dot(expand, x.astype(bf16), preferred_element_type=f32)
        return jnp.sum(spread * pick, axis=1, keepdims=True)

    s_hi, s_mid, s_lo = per_slot(hi), per_slot(mid), per_slot(lo)
    s_flag = jnp.sum(pick * flags, axis=1, keepdims=True)
    count = jnp.sum(flags, axis=1, keepdims=True)
    c_hi = jnp.floor(count / 256.0)
    c_lo = count - 256.0 * c_hi
    col = lax.broadcasted_iota(jnp.int32, (slots, side), 1)
    side_v = jnp.where(col == 0, s_hi, 0.0)
    for c, v in ((1, s_mid), (2, s_lo), (3, s_flag), (4, c_hi), (5, c_lo)):
        side_v = jnp.where(col == c, v, side_v)
    side_v = side_v.astype(bf16)
    if split:
        tok_out, grd_out, side_out, pick_out = outs
        tok_out[...] = tok
        grd_out[...] = grd
        side_out[...] = side_v
    else:
        pay_out, pick_out = outs
        pay_out[:, :width] = tok
        pay_out[:, width : 2 * width] = grd
        pay_out[:, 2 * width :] = side_v
    pick_out[...] = pick_b


def glue(expert_ids, gate_values, forget_flags, tokens, token_grads, n_dest):
    import functools

    rows, width = tokens.shape
    slots = n_dest * CAP
    side = 128
    split = width % 128 != 0
    bf16 = jnp.bfloat16
    if split:
        shapes = [(slots, width), (slots, width), (slots, side), (slots, rows)]
    else:
        shapes = [(slots, 2 * width + side), (slots, rows)]
    vmem = pl.BlockSpec(memory_space=pltpu.VMEM)
    outs = pl.pallas_call(
        functools.partial(glue_kernel, n_dest, width, side, split),
        out_shape=[jax.ShapeDtypeStruct(s, bf16) for s in shapes],
        in_specs=[vmem] * 5,
        out_specs=[vmem] * len(shapes),
    )(expert_ids.T, gate_values.T, forget_flags.reshape(1, rows), tokens, token_grads)
    if split:
        return jnp.concatenate(outs[:3], axis=1), outs[3]
    return outs[0], outs[1]


def silu_parts(pre):
    sigmoid_gate = jax.nn.sigmoid(pre)
    return (pre * sigmoid_gate, sigmoid_gate * (1.0 + pre * (1.0 - sigmoid_gate)))


def bf16_part(x):
    return lax.reduce_precision(x, exponent_bits=8, mantissa_bits=7)


def partner(x, bit, n):
    return lax.ppermute(x, "dp", [(i, i ^ bit) for i in range(n)])


def gather_dp(x, n):
    me = lax.axis_index("dp")
    held = [x]
    owners = [me]
    bit = n // 2
    while bit >= 1:
        stacked = jnp.stack(held)
        got = partner(stacked, bit, n)
        held = held + [got[i] for i in range(len(held))]
        owners = owners + [o ^ bit for o in owners]
        bit //= 2
    at = lax.broadcasted_iota(jnp.int32, (n, 1, 1), 0)
    out = jnp.broadcast_to(held[0][None], (n,) + x.shape)
    for piece, owner in zip(held[1:], owners[1:]):
        out = jnp.where(at == owner, piece[None], out)
    return out


def gather_half(x, n):
    me = lax.axis_index("dp")
    top = n // 2
    base = me & top
    held = [x]
    owners = [me]
    bit = top // 2
    while bit >= 1:
        stacked = jnp.stack(held)
        got = partner(stacked, bit, n)
        held = held + [got[i] for i in range(len(held))]
        owners = owners + [o ^ bit for o in owners]
        bit //= 2
    at = lax.broadcasted_iota(jnp.int32, (top, 1, 1), 0)
    out = jnp.broadcast_to(held[0][None], (top,) + x.shape)
    for piece, owner in zip(held[1:], owners[1:]):
        out = jnp.where(at == owner - base, piece[None], out)
    return out, base


def scatter_dp(parts, n):
    me = lax.axis_index("dp")
    acc = parts
    bit = 1
    while bit < n:
        pairs = acc.reshape((acc.shape[0] // 2, 2) + acc.shape[1:])
        mine = (me & bit) != 0
        keep = jnp.where(mine, pairs[:, 1], pairs[:, 0])
        send = jnp.where(mine, pairs[:, 0], pairs[:, 1])
        got = partner(send.astype(jnp.bfloat16), bit, n)
        acc = keep.astype(jnp.float32) + got.astype(jnp.float32)
        bit *= 2
    return acc[0]


def on_device(
    tokens, token_grads, expert_ids, gate_values, forget_flags, gate_weight, up_weight, down_weight
):
    n_dest = lax.axis_size("expert")
    n_dp = lax.axis_size("dp")
    row_count, width = tokens.shape
    me_dp = lax.axis_index("dp")
    w_down = down_weight[0]
    top = n_dp // 2
    half_cols = (n_dp * width) // 2
    if n_dp > 1:
        upper_half = (me_dp & top) != 0
        lend = jnp.where(upper_half, w_down[:, :half_cols], w_down[:, half_cols:]).T
        keep = jnp.where(upper_half, w_down[:, half_cols:], w_down[:, :half_cols]).T
        borrowed = partner(lend, top, n_dp)
    payload, pick_t = glue(expert_ids, gate_values, forget_flags, tokens, token_grads, n_dest)
    side = payload.shape[1] - 2 * width
    arrived = lax.all_to_all(payload, "expert", split_axis=0, concat_axis=0, tiled=True)
    slots = arrived.shape[0]
    part_tokens = arrived[:, :width]
    raw_grads = arrived[:, width : 2 * width]
    info = arrived[:, 2 * width :].astype(jnp.float32)
    gate_sel = (info[:, 0] + info[:, 1]) + info[:, 2]
    flag = info[:, 3]
    first_row = jnp.where(lax.broadcasted_iota(jnp.int32, (slots,), 0) % CAP == 0, 1.0, 0.0)
    block_hi = (first_row * info[:, 4]).astype(jnp.bfloat16)
    block_lo = (first_row * info[:, 5]).astype(jnp.bfloat16)
    every = jnp.ones((slots, slots), jnp.bfloat16)
    forget_count = 256.0 * jnp.dot(every, block_hi, preferred_element_type=jnp.float32) + jnp.dot(
        every, block_lo, preferred_element_type=jnp.float32
    )
    all_rows = row_count * n_dest
    half_total = jnp.float32(all_rows) / 2.0
    weight = jnp.where(
        flag == 1.0,
        -half_total / forget_count,
        half_total / (jnp.float32(all_rows) - forget_count),
    )
    scale = gate_sel * weight
    part_grads = (scale[:, None] * raw_grads.astype(jnp.float32)).astype(jnp.bfloat16)
    ff = gate_weight.shape[2]
    w_gate = gate_weight[0].reshape(n_dp, width, ff)
    w_up = up_weight[0].reshape(n_dp, width, ff)
    last_dims = (((1,), (1,)), ((), ()))
    slot_tokens = gather_dp(part_tokens, n_dp)
    if n_dp > 1:
        half_grads, _ = gather_half(part_grads, n_dp)
        half_dims = (((0, 2), (0, 1)), ((), ()))
        ff_down = w_down.shape[0]
        hidden_grad = lax.dot_general(
            half_grads, keep.reshape(top, width, ff_down), half_dims, preferred_element_type=jnp.float32
        )
        lent = lax.dot_general(
            half_grads, borrowed.reshape(top, width, ff_down), half_dims, preferred_element_type=jnp.float32
        )
        hidden_grad = hidden_grad + partner(lent, top, n_dp)
    else:
        hidden_grad = lax.dot_general(part_grads, w_down, last_dims, preferred_element_type=jnp.float32)
    chunk_dims = (((0, 2), (0, 1)), ((), ()))
    gate_pre = lax.dot_general(slot_tokens, w_gate, chunk_dims, preferred_element_type=jnp.float32)
    up_pre = lax.dot_general(slot_tokens, w_up, chunk_dims, preferred_element_type=jnp.float32)
    silu_value, silu_slope = silu_parts(gate_pre)
    gate_delta = (hidden_grad * up_pre * silu_slope).astype(jnp.bfloat16)
    up_delta = (hidden_grad * silu_value).astype(jnp.bfloat16)
    slot_dims = (((1,), (0,)), ((), ()))
    grad_gate = lax.dot_general(
        slot_tokens, gate_delta, slot_dims, preferred_element_type=jnp.float32
    ).astype(jnp.bfloat16)
    grad_up = lax.dot_general(
        slot_tokens, up_delta, slot_dims, preferred_element_type=jnp.float32
    ).astype(jnp.bfloat16)
    back_dims = (((2,), (1,)), ((), ()))
    from_gate = lax.dot_general(w_gate, gate_delta, back_dims, preferred_element_type=jnp.float32)
    from_up = lax.dot_general(w_up, up_delta, back_dims, preferred_element_type=jnp.float32)
    part = (from_gate + from_up).astype(jnp.bfloat16)
    summed = scatter_dp(jnp.swapaxes(part, 1, 2), n_dp).astype(jnp.bfloat16)
    returned = lax.all_to_all(summed, "expert", split_axis=0, concat_axis=0, tiled=True)
    input_grad = lax.dot_general(
        pick_t, returned, (((0,), (0,)), ((), ())), preferred_element_type=jnp.float32
    )
    return (
        grad_gate.reshape(1, n_dp * width, ff),
        grad_up.reshape(1, n_dp * width, ff),
        input_grad.astype(jnp.bfloat16),
    )


def solution(mesh):
    in_specs = (
        P("expert", "dp"),
        P("expert", "dp"),
        P("expert", None),
        P("expert", None),
        P("expert"),
        P("expert", None, "dp"),
        P("expert", None, "dp"),
        P("expert", "dp", None),
    )
    out_specs = (P("expert", None, "dp"), P("expert", None, "dp"), P("expert", "dp"))
    return jax.shard_map(
        on_device, mesh=mesh, in_specs=in_specs, out_specs=out_specs, check_vma=False
    )
```

```python
import jax
import jax.numpy as jnp
from jax import lax
from jax.sharding import PartitionSpec as P
from jax.experimental import pallas as pl
from jax.experimental.pallas import tpu as pltpu

EXP_DEV = 8
CAP = 16


def glue_kernel(n_dest, width, side, split, ids_rows_ref, ids_ref, gates_ref, flags_ref, tok_ref, grd_ref, *outs):
    f32, bf16 = jnp.float32, jnp.bfloat16
    rows = tok_ref.shape[0]
    slots = n_dest * CAP
    lanes = max(16, -(-n_dest // 16) * 16)
    ids = ids_ref[...]
    gates = gates_ref[...]
    flags = flags_ref[...].astype(f32)
    dest = lax.broadcasted_iota(jnp.int32, (lanes, rows), 0)
    edited = dest * EXP_DEV
    valid = dest < n_dest
    hits = jnp.zeros((lanes, rows), f32)
    gsel = jnp.zeros((lanes, rows), f32)
    for k in range(ids.shape[0]):
        m = (ids[k : k + 1, :] == edited) & valid
        hits = hits + jnp.where(m, 1.0, 0.0)
        gsel = gsel + jnp.where(m, gates[k : k + 1, :], 0.0)
    before = jnp.where(
        lax.broadcasted_iota(jnp.int32, (rows, rows), 0) < lax.broadcasted_iota(jnp.int32, (rows, rows), 1),
        1.0, 0.0,
    ).astype(bf16)
    rank = jnp.dot(hits.astype(bf16), before, preferred_element_type=f32)
    slot_of = lax.broadcasted_iota(jnp.int32, (slots, lanes), 0)
    expand = jnp.where(
        lax.shift_right_logical(slot_of, 4) == lax.broadcasted_iota(jnp.int32, (slots, lanes), 1), 1.0, 0.0
    ).astype(bf16)
    hit_s = jnp.dot(expand, hits.astype(bf16), preferred_element_type=f32)
    rank_s = jnp.dot(expand, rank.astype(bf16), preferred_element_type=f32)
    place = (lax.broadcasted_iota(jnp.int32, (slots, rows), 0) & (CAP - 1)).astype(f32)
    pick = jnp.where((hit_s == 1.0) & (rank_s == place), 1.0, 0.0)
    pick_b = pick.astype(bf16)
    tok = jnp.dot(pick_b, tok_ref[...], preferred_element_type=f32).astype(bf16)
    grd = jnp.dot(pick_b, grd_ref[...], preferred_element_type=f32).astype(bf16)
    hi = gsel.astype(bf16).astype(f32)
    rest = gsel - hi
    mid = rest.astype(bf16).astype(f32)
    lo = rest - mid

    def per_slot(x):
        spread = jnp.dot(expand, x.astype(bf16), preferred_element_type=f32)
        return jnp.sum(spread * pick, axis=1, keepdims=True)

    s_hi, s_mid, s_lo = per_slot(hi), per_slot(mid), per_slot(lo)
    s_flag = jnp.sum(pick * flags, axis=1, keepdims=True)
    count = jnp.sum(flags, axis=1, keepdims=True)
    c_hi = jnp.floor(count / 256.0)
    c_lo = count - 256.0 * c_hi
    col = lax.broadcasted_iota(jnp.int32, (slots, side), 1)
    side_v = jnp.where(col == 0, s_hi, 0.0)
    for c, v in ((1, s_mid), (2, s_lo), (3, s_flag), (4, c_hi), (5, c_lo)):
        side_v = jnp.where(col == c, v, side_v)
    side_v = side_v.astype(bf16)
    if split:
        tok_out, grd_out, side_out, pick_out = outs
        tok_out[...] = tok
        grd_out[...] = grd
        side_out[...] = side_v
    else:
        pay_out, pick_out = outs
        pay_out[:, :width] = tok
        pay_out[:, width : 2 * width] = grd
        pay_out[:, 2 * width :] = side_v
    ids_rows = ids_rows_ref[...]
    edited_row = lax.broadcasted_iota(jnp.int32, (rows, lanes), 1) * EXP_DEV
    valid_row = lax.broadcasted_iota(jnp.int32, (rows, lanes), 1) < n_dest
    hits_t = jnp.zeros((rows, lanes), f32)
    for k in range(ids_rows.shape[1]):
        hits_t = hits_t + jnp.where((ids_rows[:, k : k + 1] == edited_row) & valid_row, 1.0, 0.0)
    after = jnp.where(
        lax.broadcasted_iota(jnp.int32, (rows, rows), 1) < lax.broadcasted_iota(jnp.int32, (rows, rows), 0),
        1.0, 0.0,
    ).astype(bf16)
    rank_t = jnp.dot(after, hits_t.astype(bf16), preferred_element_type=f32)
    lane_of = lax.broadcasted_iota(jnp.int32, (lanes, slots), 0)
    spread_t = jnp.where(
        lax.shift_right_logical(lax.broadcasted_iota(jnp.int32, (lanes, slots), 1), 4) == lane_of, 1.0, 0.0
    ).astype(bf16)
    hit_at = jnp.dot(hits_t.astype(bf16), spread_t, preferred_element_type=f32)
    rank_at = jnp.dot(rank_t.astype(bf16), spread_t, preferred_element_type=f32)
    place_t = (lax.broadcasted_iota(jnp.int32, (rows, slots), 1) & (CAP - 1)).astype(f32)
    pick_out[...] = jnp.where((hit_at == 1.0) & (rank_at == place_t), 1.0, 0.0).astype(bf16)


def glue(expert_ids, gate_values, forget_flags, tokens, token_grads, n_dest):
    import functools

    rows, width = tokens.shape
    slots = n_dest * CAP
    side = 128
    split = width % 128 != 0
    bf16 = jnp.bfloat16
    if split:
        shapes = [(slots, width), (slots, width), (slots, side), (rows, slots)]
    else:
        shapes = [(slots, 2 * width + side), (rows, slots)]
    vmem = pl.BlockSpec(memory_space=pltpu.VMEM)
    outs = pl.pallas_call(
        functools.partial(glue_kernel, n_dest, width, side, split),
        out_shape=[jax.ShapeDtypeStruct(s, bf16) for s in shapes],
        in_specs=[vmem] * 6,
        out_specs=[vmem] * len(shapes),
    )(expert_ids, expert_ids.T, gate_values.T, forget_flags.reshape(1, rows), tokens, token_grads)
    if split:
        return jnp.concatenate(outs[:3], axis=1), outs[3]
    return outs[0], outs[1]


def silu_parts(pre):
    sigmoid_gate = jax.nn.sigmoid(pre)
    return (pre * sigmoid_gate, sigmoid_gate * (1.0 + pre * (1.0 - sigmoid_gate)))


def bf16_part(x):
    return lax.reduce_precision(x, exponent_bits=8, mantissa_bits=7)


def partner(x, bit, n):
    return lax.ppermute(x, "dp", [(i, i ^ bit) for i in range(n)])


def gather_dp(x, n):
    me = lax.axis_index("dp")
    held = [x]
    owners = [me]
    bit = n // 2
    while bit >= 1:
        stacked = jnp.stack(held)
        got = partner(stacked, bit, n)
        held = held + [got[i] for i in range(len(held))]
        owners = owners + [o ^ bit for o in owners]
        bit //= 2
    at = lax.broadcasted_iota(jnp.int32, (n, 1, 1), 0)
    out = jnp.broadcast_to(held[0][None], (n,) + x.shape)
    for piece, owner in zip(held[1:], owners[1:]):
        out = jnp.where(at == owner, piece[None], out)
    return out


def gather_half(x, n):
    me = lax.axis_index("dp")
    top = n // 2
    base = me & top
    held = [x]
    owners = [me]
    bit = top // 2
    while bit >= 1:
        stacked = jnp.stack(held)
        got = partner(stacked, bit, n)
        held = held + [got[i] for i in range(len(held))]
        owners = owners + [o ^ bit for o in owners]
        bit //= 2
    at = lax.broadcasted_iota(jnp.int32, (top, 1, 1), 0)
    out = jnp.broadcast_to(held[0][None], (top,) + x.shape)
    for piece, owner in zip(held[1:], owners[1:]):
        out = jnp.where(at == owner - base, piece[None], out)
    return out, base


def scatter_dp(parts, n):
    me = lax.axis_index("dp")
    acc = parts
    bit = 1
    while bit < n:
        pairs = acc.reshape((acc.shape[0] // 2, 2) + acc.shape[1:])
        mine = (me & bit) != 0
        keep = jnp.where(mine, pairs[:, 1], pairs[:, 0])
        send = jnp.where(mine, pairs[:, 0], pairs[:, 1])
        got = partner(send.astype(jnp.bfloat16), bit, n)
        acc = keep.astype(jnp.float32) + got.astype(jnp.float32)
        bit *= 2
    return acc[0]


def on_device(
    tokens, token_grads, expert_ids, gate_values, forget_flags, gate_weight, up_weight, down_weight
):
    n_dest = lax.axis_size("expert")
    n_dp = lax.axis_size("dp")
    row_count, width = tokens.shape
    me_dp = lax.axis_index("dp")
    w_down = down_weight[0]
    top = n_dp // 2
    half_cols = (n_dp * width) // 2
    if n_dp > 1:
        upper_half = (me_dp & top) != 0
        lend = jnp.where(upper_half, w_down[:, :half_cols], w_down[:, half_cols:]).T
        keep = jnp.where(upper_half, w_down[:, half_cols:], w_down[:, :half_cols]).T
        borrowed = partner(lend, top, n_dp)
    payload, pick_t = glue(expert_ids, gate_values, forget_flags, tokens, token_grads, n_dest)
    side = payload.shape[1] - 2 * width
    arrived = lax.all_to_all(payload, "expert", split_axis=0, concat_axis=0, tiled=True)
    slots = arrived.shape[0]
    part_tokens = arrived[:, :width]
    raw_grads = arrived[:, width : 2 * width]
    info = arrived[:, 2 * width :].astype(jnp.float32)
    gate_sel = (info[:, 0] + info[:, 1]) + info[:, 2]
    flag = info[:, 3]
    first_row = jnp.where(lax.broadcasted_iota(jnp.int32, (slots,), 0) % CAP == 0, 1.0, 0.0)
    block_hi = (first_row * info[:, 4]).astype(jnp.bfloat16)
    block_lo = (first_row * info[:, 5]).astype(jnp.bfloat16)
    every = jnp.ones((slots, slots), jnp.bfloat16)
    forget_count = 256.0 * jnp.dot(every, block_hi, preferred_element_type=jnp.float32) + jnp.dot(
        every, block_lo, preferred_element_type=jnp.float32
    )
    all_rows = row_count * n_dest
    half_total = jnp.float32(all_rows) / 2.0
    weight = jnp.where(
        flag == 1.0,
        -half_total / forget_count,
        half_total / (jnp.float32(all_rows) - forget_count),
    )
    scale = gate_sel * weight
    part_grads = (scale[:, None] * raw_grads.astype(jnp.float32)).astype(jnp.bfloat16)
    ff = gate_weight.shape[2]
    w_gate = gate_weight[0].reshape(n_dp, width, ff)
    w_up = up_weight[0].reshape(n_dp, width, ff)
    last_dims = (((1,), (1,)), ((), ()))
    slot_tokens = gather_dp(part_tokens, n_dp)
    if n_dp > 1:
        half_grads, _ = gather_half(part_grads, n_dp)
        half_dims = (((0, 2), (0, 1)), ((), ()))
        ff_down = w_down.shape[0]
        hidden_grad = lax.dot_general(
            half_grads, keep.reshape(top, width, ff_down), half_dims, preferred_element_type=jnp.float32
        )
        lent = lax.dot_general(
            half_grads, borrowed.reshape(top, width, ff_down), half_dims, preferred_element_type=jnp.float32
        )
        hidden_grad = hidden_grad + partner(lent, top, n_dp)
    else:
        hidden_grad = lax.dot_general(part_grads, w_down, last_dims, preferred_element_type=jnp.float32)
    chunk_dims = (((0, 2), (0, 1)), ((), ()))
    gate_pre = lax.dot_general(slot_tokens, w_gate, chunk_dims, preferred_element_type=jnp.float32)
    up_pre = lax.dot_general(slot_tokens, w_up, chunk_dims, preferred_element_type=jnp.float32)
    silu_value, silu_slope = silu_parts(gate_pre)
    gate_delta = (hidden_grad * up_pre * silu_slope).astype(jnp.bfloat16)
    up_delta = (hidden_grad * silu_value).astype(jnp.bfloat16)
    slot_dims = (((1,), (0,)), ((), ()))
    grad_gate = lax.dot_general(
        slot_tokens, gate_delta, slot_dims, preferred_element_type=jnp.float32
    ).astype(jnp.bfloat16)
    grad_up = lax.dot_general(
        slot_tokens, up_delta, slot_dims, preferred_element_type=jnp.float32
    ).astype(jnp.bfloat16)
    back_dims = (((2,), (1,)), ((), ()))
    from_gate = lax.dot_general(w_gate, gate_delta, back_dims, preferred_element_type=jnp.float32)
    from_up = lax.dot_general(w_up, up_delta, back_dims, preferred_element_type=jnp.float32)
    part = (from_gate + from_up).astype(jnp.bfloat16)
    summed = scatter_dp(jnp.swapaxes(part, 1, 2), n_dp).astype(jnp.bfloat16)
    returned = lax.all_to_all(summed, "expert", split_axis=0, concat_axis=0, tiled=True)
    input_grad = jnp.dot(pick_t, returned, preferred_element_type=jnp.float32)
    return (
        grad_gate.reshape(1, n_dp * width, ff),
        grad_up.reshape(1, n_dp * width, ff),
        input_grad.astype(jnp.bfloat16),
    )


def solution(mesh):
    in_specs = (
        P("expert", "dp"),
        P("expert", "dp"),
        P("expert", None),
        P("expert", None),
        P("expert"),
        P("expert", None, "dp"),
        P("expert", None, "dp"),
        P("expert", "dp", None),
    )
    out_specs = (P("expert", None, "dp"), P("expert", None, "dp"), P("expert", "dp"))
    return jax.shard_map(
        on_device, mesh=mesh, in_specs=in_specs, out_specs=out_specs, check_vma=False
    )
```

```python
import jax
import jax.numpy as jnp
from jax import lax
from jax.sharding import PartitionSpec as P
from jax.experimental import pallas as pl
from jax.experimental.pallas import tpu as pltpu

EXP_DEV = 8
CAP = 16


def glue_kernel(n_dest, width, side, split, ids_ref, gates_ref, flags_ref, tok_ref, grd_ref, *outs):
    f32, bf16 = jnp.float32, jnp.bfloat16
    rows = tok_ref.shape[0]
    slots = n_dest * CAP
    lanes = max(16, -(-n_dest // 16) * 16)
    ids = ids_ref[...]
    gates = gates_ref[...]
    flags = flags_ref[...].astype(f32)
    dest = lax.broadcasted_iota(jnp.int32, (lanes, rows), 0)
    edited = dest * EXP_DEV
    valid = dest < n_dest
    hits = jnp.zeros((lanes, rows), f32)
    gsel = jnp.zeros((lanes, rows), f32)
    for k in range(ids.shape[0]):
        m = (ids[k : k + 1, :] == edited) & valid
        hits = hits + jnp.where(m, 1.0, 0.0)
        gsel = gsel + jnp.where(m, gates[k : k + 1, :], 0.0)
    before = jnp.where(
        lax.broadcasted_iota(jnp.int32, (rows, rows), 0) < lax.broadcasted_iota(jnp.int32, (rows, rows), 1),
        1.0, 0.0,
    ).astype(bf16)
    rank = jnp.dot(hits.astype(bf16), before, preferred_element_type=f32)
    slot_of = lax.broadcasted_iota(jnp.int32, (slots, lanes), 0)
    expand = jnp.where(
        lax.shift_right_logical(slot_of, 4) == lax.broadcasted_iota(jnp.int32, (slots, lanes), 1), 1.0, 0.0
    ).astype(bf16)
    hit_s = jnp.dot(expand, hits.astype(bf16), preferred_element_type=f32)
    rank_s = jnp.dot(expand, rank.astype(bf16), preferred_element_type=f32)
    place = (lax.broadcasted_iota(jnp.int32, (slots, rows), 0) & (CAP - 1)).astype(f32)
    pick = jnp.where((hit_s == 1.0) & (rank_s == place), 1.0, 0.0)
    pick_b = pick.astype(bf16)
    tok = jnp.dot(pick_b, tok_ref[...], preferred_element_type=f32).astype(bf16)
    grd = jnp.dot(pick_b, grd_ref[...], preferred_element_type=f32).astype(bf16)
    hi = gsel.astype(bf16).astype(f32)
    rest = gsel - hi
    mid = rest.astype(bf16).astype(f32)
    lo = rest - mid

    def per_slot(x):
        spread = jnp.dot(expand, x.astype(bf16), preferred_element_type=f32)
        return jnp.sum(spread * pick, axis=1, keepdims=True)

    s_hi, s_mid, s_lo = per_slot(hi), per_slot(mid), per_slot(lo)
    s_flag = jnp.sum(pick * flags, axis=1, keepdims=True)
    count = jnp.sum(flags, axis=1, keepdims=True)
    c_hi = jnp.floor(count / 256.0)
    c_lo = count - 256.0 * c_hi
    col = lax.broadcasted_iota(jnp.int32, (slots, side), 1)
    side_v = jnp.where(col == 0, s_hi, 0.0)
    for c, v in ((1, s_mid), (2, s_lo), (3, s_flag), (4, c_hi), (5, c_lo)):
        side_v = jnp.where(col == c, v, side_v)
    side_v = side_v.astype(bf16)
    if split:
        tok_out, grd_out, side_out, pick_out = outs
        tok_out[...] = tok
        grd_out[...] = grd
        side_out[...] = side_v
    else:
        pay_out, pick_out = outs
        pay_out[:, :width] = tok
        pay_out[:, width : 2 * width] = grd
        pay_out[:, 2 * width :] = side_v
    pick_out[...] = pick_b


def glue(expert_ids, gate_values, forget_flags, tokens, token_grads, n_dest):
    import functools

    rows, width = tokens.shape
    slots = n_dest * CAP
    side = 128
    split = width % 128 != 0
    bf16 = jnp.bfloat16
    if split:
        shapes = [(slots, width), (slots, width), (slots, side), (slots, rows)]
    else:
        shapes = [(slots, 2 * width + side), (slots, rows)]
    vmem = pl.BlockSpec(memory_space=pltpu.VMEM)
    outs = pl.pallas_call(
        functools.partial(glue_kernel, n_dest, width, side, split),
        out_shape=[jax.ShapeDtypeStruct(s, bf16) for s in shapes],
        in_specs=[vmem] * 5,
        out_specs=[vmem] * len(shapes),
    )(expert_ids.T, gate_values.T, forget_flags.reshape(1, rows), tokens, token_grads)
    if split:
        return jnp.concatenate(outs[:3], axis=1), outs[3]
    return outs[0], outs[1]


def silu_parts(pre):
    sigmoid_gate = jax.nn.sigmoid(pre)
    return (pre * sigmoid_gate, sigmoid_gate * (1.0 + pre * (1.0 - sigmoid_gate)))


def bf16_part(x):
    return lax.reduce_precision(x, exponent_bits=8, mantissa_bits=7)


def partner(x, bit, n):
    return lax.ppermute(x, "dp", [(i, i ^ bit) for i in range(n)])


def gather_dp(x, n):
    me = lax.axis_index("dp")
    held = [x]
    owners = [me]
    bit = n // 2
    while bit >= 1:
        stacked = jnp.stack(held)
        got = partner(stacked, bit, n)
        held = held + [got[i] for i in range(len(held))]
        owners = owners + [o ^ bit for o in owners]
        bit //= 2
    at = lax.broadcasted_iota(jnp.int32, (n, 1, 1), 0)
    out = jnp.broadcast_to(held[0][None], (n,) + x.shape)
    for piece, owner in zip(held[1:], owners[1:]):
        out = jnp.where(at == owner, piece[None], out)
    return out


def gather_from(held, owners, bit, n):
    while bit >= 1:
        stacked = jnp.stack(held)
        got = partner(stacked, bit, n)
        held = held + [got[i] for i in range(len(held))]
        owners = owners + [o ^ bit for o in owners]
        bit //= 2
    at = lax.broadcasted_iota(jnp.int32, (n, 1, 1), 0)
    out = jnp.broadcast_to(held[0][None], (n,) + held[0].shape)
    for piece, owner in zip(held[1:], owners[1:]):
        out = jnp.where(at == owner, piece[None], out)
    return out


def gather_half(x, n):
    me = lax.axis_index("dp")
    top = n // 2
    base = me & top
    held = [x]
    owners = [me]
    bit = top // 2
    while bit >= 1:
        stacked = jnp.stack(held)
        got = partner(stacked, bit, n)
        held = held + [got[i] for i in range(len(held))]
        owners = owners + [o ^ bit for o in owners]
        bit //= 2
    at = lax.broadcasted_iota(jnp.int32, (top, 1, 1), 0)
    out = jnp.broadcast_to(held[0][None], (top,) + x.shape)
    for piece, owner in zip(held[1:], owners[1:]):
        out = jnp.where(at == owner - base, piece[None], out)
    return out, base


def scatter_dp(parts, n):
    me = lax.axis_index("dp")
    acc = parts
    bit = 1
    while bit < n:
        pairs = acc.reshape((acc.shape[0] // 2, 2) + acc.shape[1:])
        mine = (me & bit) != 0
        keep = jnp.where(mine, pairs[:, 1], pairs[:, 0])
        send = jnp.where(mine, pairs[:, 0], pairs[:, 1])
        got = partner(send.astype(jnp.bfloat16), bit, n)
        acc = keep.astype(jnp.float32) + got.astype(jnp.float32)
        bit *= 2
    return acc[0]


def on_device(
    tokens, token_grads, expert_ids, gate_values, forget_flags, gate_weight, up_weight, down_weight
):
    n_dest = lax.axis_size("expert")
    n_dp = lax.axis_size("dp")
    row_count, width = tokens.shape
    me_dp = lax.axis_index("dp")
    w_down = down_weight[0]
    top = n_dp // 2
    half_cols = (n_dp * width) // 2
    if n_dp > 1:
        upper_half = (me_dp & top) != 0
        lend = jnp.where(upper_half, w_down[:, :half_cols], w_down[:, half_cols:]).T
        keep = jnp.where(upper_half, w_down[:, half_cols:], w_down[:, :half_cols]).T
        borrowed = partner(lend, top, n_dp)
    payload, pick_t = glue(expert_ids, gate_values, forget_flags, tokens, token_grads, n_dest)
    side = payload.shape[1] - 2 * width
    arrived = lax.all_to_all(payload, "expert", split_axis=0, concat_axis=0, tiled=True)
    slots = arrived.shape[0]
    part_tokens = arrived[:, :width]
    raw_grads = arrived[:, width : 2 * width]
    info = arrived[:, 2 * width :].astype(jnp.float32)
    gate_sel = (info[:, 0] + info[:, 1]) + info[:, 2]
    flag = info[:, 3]
    first_row = jnp.where(lax.broadcasted_iota(jnp.int32, (slots,), 0) % CAP == 0, 1.0, 0.0)
    block_hi = (first_row * info[:, 4]).astype(jnp.bfloat16)
    block_lo = (first_row * info[:, 5]).astype(jnp.bfloat16)
    every = jnp.ones((slots, slots), jnp.bfloat16)
    forget_count = 256.0 * jnp.dot(every, block_hi, preferred_element_type=jnp.float32) + jnp.dot(
        every, block_lo, preferred_element_type=jnp.float32
    )
    all_rows = row_count * n_dest
    half_total = jnp.float32(all_rows) / 2.0
    weight = jnp.where(
        flag == 1.0,
        -half_total / forget_count,
        half_total / (jnp.float32(all_rows) - forget_count),
    )
    scale = gate_sel * weight
    part_grads = (scale[:, None] * raw_grads.astype(jnp.float32)).astype(jnp.bfloat16)
    ff = gate_weight.shape[2]
    w_gate = gate_weight[0].reshape(n_dp, width, ff)
    w_up = up_weight[0].reshape(n_dp, width, ff)
    last_dims = (((1,), (1,)), ((), ()))
    if n_dp > 1:
        half_grads, _ = gather_half(part_grads, n_dp)
        half_dims = (((0, 2), (0, 1)), ((), ()))
        ff_down = w_down.shape[0]
        lent = lax.dot_general(
            half_grads, borrowed.reshape(top, width, ff_down), half_dims, preferred_element_type=jnp.float32
        )
        lent_hi = bf16_part(lent)
        lent_rest = lent - lent_hi
        lent_mid = bf16_part(lent_rest)
        lent_lo = lent_rest - lent_mid
        outgoing = jnp.concatenate(
            [part_tokens, lent_hi.astype(jnp.bfloat16), lent_mid.astype(jnp.bfloat16), lent_lo.astype(jnp.bfloat16)],
            axis=1,
        )
        incoming = partner(outgoing, top, n_dp)
        share = incoming[:, width:].astype(jnp.float32)
        returned_share = (share[:, :ff_down] + share[:, ff_down : 2 * ff_down]) + share[:, 2 * ff_down :]
        hidden_grad = lax.dot_general(
            half_grads, keep.reshape(top, width, ff_down), half_dims, preferred_element_type=jnp.float32
        )
        hidden_grad = hidden_grad + returned_share
        slot_tokens = gather_from([part_tokens, incoming[:, :width]], [me_dp, me_dp ^ top], top // 2, n_dp)
    else:
        hidden_grad = lax.dot_general(part_grads, w_down, last_dims, preferred_element_type=jnp.float32)
        slot_tokens = part_tokens[None]
    chunk_dims = (((0, 2), (0, 1)), ((), ()))
    gate_pre = lax.dot_general(slot_tokens, w_gate, chunk_dims, preferred_element_type=jnp.float32)
    up_pre = lax.dot_general(slot_tokens, w_up, chunk_dims, preferred_element_type=jnp.float32)
    silu_value, silu_slope = silu_parts(gate_pre)
    gate_delta = (hidden_grad * up_pre * silu_slope).astype(jnp.bfloat16)
    up_delta = (hidden_grad * silu_value).astype(jnp.bfloat16)
    slot_dims = (((1,), (0,)), ((), ()))
    grad_gate = lax.dot_general(
        slot_tokens, gate_delta, slot_dims, preferred_element_type=jnp.float32
    ).astype(jnp.bfloat16)
    grad_up = lax.dot_general(
        slot_tokens, up_delta, slot_dims, preferred_element_type=jnp.float32
    ).astype(jnp.bfloat16)
    back_dims = (((2,), (1,)), ((), ()))
    from_gate = lax.dot_general(w_gate, gate_delta, back_dims, preferred_element_type=jnp.float32)
    from_up = lax.dot_general(w_up, up_delta, back_dims, preferred_element_type=jnp.float32)
    part = (from_gate + from_up).astype(jnp.bfloat16)
    summed = scatter_dp(jnp.swapaxes(part, 1, 2), n_dp).astype(jnp.bfloat16)
    returned = lax.all_to_all(summed, "expert", split_axis=0, concat_axis=0, tiled=True)
    input_grad = lax.dot_general(
        pick_t, returned, (((0,), (0,)), ((), ())), preferred_element_type=jnp.float32
    )
    return (
        grad_gate.reshape(1, n_dp * width, ff),
        grad_up.reshape(1, n_dp * width, ff),
        input_grad.astype(jnp.bfloat16),
    )


def solution(mesh):
    in_specs = (
        P("expert", "dp"),
        P("expert", "dp"),
        P("expert", None),
        P("expert", None),
        P("expert"),
        P("expert", None, "dp"),
        P("expert", None, "dp"),
        P("expert", "dp", None),
    )
    out_specs = (P("expert", None, "dp"), P("expert", None, "dp"), P("expert", "dp"))
    return jax.shard_map(
        on_device, mesh=mesh, in_specs=in_specs, out_specs=out_specs, check_vma=False
    )
```

```python
import jax
import jax.numpy as jnp
from jax import lax
from jax.sharding import PartitionSpec as P
from jax.experimental import pallas as pl
from jax.experimental.pallas import tpu as pltpu

EXP_DEV = 8
CAP = 16


def glue_kernel(n_dest, width, side, split, ids_ref, gates_ref, flags_ref, tok_ref, grd_ref, *outs):
    f32, bf16 = jnp.float32, jnp.bfloat16
    rows = tok_ref.shape[0]
    slots = n_dest * CAP
    lanes = max(16, -(-n_dest // 16) * 16)
    ids = ids_ref[...]
    gates = gates_ref[...]
    flags = flags_ref[...].astype(f32)
    dest = lax.broadcasted_iota(jnp.int32, (lanes, rows), 0)
    edited = dest * EXP_DEV
    valid = dest < n_dest
    hits = jnp.zeros((lanes, rows), f32)
    gsel = jnp.zeros((lanes, rows), f32)
    for k in range(ids.shape[0]):
        m = (ids[k : k + 1, :] == edited) & valid
        hits = hits + jnp.where(m, 1.0, 0.0)
        gsel = gsel + jnp.where(m, gates[k : k + 1, :], 0.0)
    before = jnp.where(
        lax.broadcasted_iota(jnp.int32, (rows, rows), 0) < lax.broadcasted_iota(jnp.int32, (rows, rows), 1),
        1.0, 0.0,
    ).astype(bf16)
    rank = jnp.dot(hits.astype(bf16), before, preferred_element_type=f32)
    slot_of = lax.broadcasted_iota(jnp.int32, (slots, lanes), 0)
    expand = jnp.where(
        lax.shift_right_logical(slot_of, 4) == lax.broadcasted_iota(jnp.int32, (slots, lanes), 1), 1.0, 0.0
    ).astype(bf16)
    hit_s = jnp.dot(expand, hits.astype(bf16), preferred_element_type=f32)
    rank_s = jnp.dot(expand, rank.astype(bf16), preferred_element_type=f32)
    place = (lax.broadcasted_iota(jnp.int32, (slots, rows), 0) & (CAP - 1)).astype(f32)
    pick = jnp.where((hit_s == 1.0) & (rank_s == place), 1.0, 0.0)
    pick_b = pick.astype(bf16)
    tok = jnp.dot(pick_b, tok_ref[...], preferred_element_type=f32).astype(bf16)
    grd = jnp.dot(pick_b, grd_ref[...], preferred_element_type=f32).astype(bf16)
    hi = gsel.astype(bf16).astype(f32)
    rest = gsel - hi
    mid = rest.astype(bf16).astype(f32)
    lo = rest - mid

    def per_slot(x):
        spread = jnp.dot(expand, x.astype(bf16), preferred_element_type=f32)
        return jnp.sum(spread * pick, axis=1, keepdims=True)

    s_hi, s_mid, s_lo = per_slot(hi), per_slot(mid), per_slot(lo)
    s_flag = jnp.sum(pick * flags, axis=1, keepdims=True)
    count = jnp.sum(flags, axis=1, keepdims=True)
    c_hi = jnp.floor(count / 256.0)
    c_lo = count - 256.0 * c_hi
    col = lax.broadcasted_iota(jnp.int32, (slots, side), 1)
    side_v = jnp.where(col == 0, s_hi, 0.0)
    for c, v in ((1, s_mid), (2, s_lo), (3, s_flag), (4, c_hi), (5, c_lo)):
        side_v = jnp.where(col == c, v, side_v)
    side_v = side_v.astype(bf16)
    if split:
        tok_out, grd_out, side_out, pick_out = outs
        tok_out[...] = tok
        grd_out[...] = grd
        side_out[...] = side_v
    else:
        pay_out, pick_out = outs
        pay_out[:, :width] = tok
        pay_out[:, width : 2 * width] = grd
        pay_out[:, 2 * width :] = side_v
    pick_out[...] = pick_b


def glue(expert_ids, gate_values, forget_flags, tokens, token_grads, n_dest):
    import functools

    rows, width = tokens.shape
    slots = n_dest * CAP
    side = 128
    split = width % 128 != 0
    bf16 = jnp.bfloat16
    if split:
        shapes = [(slots, width), (slots, width), (slots, side), (slots, rows)]
    else:
        shapes = [(slots, 2 * width + side), (slots, rows)]
    vmem = pl.BlockSpec(memory_space=pltpu.VMEM)
    outs = pl.pallas_call(
        functools.partial(glue_kernel, n_dest, width, side, split),
        out_shape=[jax.ShapeDtypeStruct(s, bf16) for s in shapes],
        in_specs=[vmem] * 5,
        out_specs=[vmem] * len(shapes),
    )(expert_ids.T, gate_values.T, forget_flags.reshape(1, rows), tokens, token_grads)
    if split:
        return jnp.concatenate(outs[:3], axis=1), outs[3]
    return outs[0], outs[1]


def silu_parts(pre):
    sigmoid_gate = jax.nn.sigmoid(pre)
    return (pre * sigmoid_gate, sigmoid_gate * (1.0 + pre * (1.0 - sigmoid_gate)))


def bf16_part(x):
    return lax.reduce_precision(x, exponent_bits=8, mantissa_bits=7)


def partner(x, bit, n):
    return lax.ppermute(x, "dp", [(i, i ^ bit) for i in range(n)])


def gather_dp(x, n):
    me = lax.axis_index("dp")
    held = [x]
    owners = [me]
    bit = n // 2
    while bit >= 1:
        stacked = jnp.stack(held)
        got = partner(stacked, bit, n)
        held = held + [got[i] for i in range(len(held))]
        owners = owners + [o ^ bit for o in owners]
        bit //= 2
    at = lax.broadcasted_iota(jnp.int32, (n, 1, 1), 0)
    out = jnp.broadcast_to(held[0][None], (n,) + x.shape)
    for piece, owner in zip(held[1:], owners[1:]):
        out = jnp.where(at == owner, piece[None], out)
    return out


def gather_from(held, owners, bit, n):
    while bit >= 1:
        stacked = jnp.stack(held)
        got = partner(stacked, bit, n)
        held = held + [got[i] for i in range(len(held))]
        owners = owners + [o ^ bit for o in owners]
        bit //= 2
    at = lax.broadcasted_iota(jnp.int32, (n, 1, 1), 0)
    out = jnp.broadcast_to(held[0][None], (n,) + held[0].shape)
    for piece, owner in zip(held[1:], owners[1:]):
        out = jnp.where(at == owner, piece[None], out)
    return out


def gather_half(x, n):
    me = lax.axis_index("dp")
    top = n // 2
    base = me & top
    held = [x]
    owners = [me]
    bit = top // 2
    while bit >= 1:
        stacked = jnp.stack(held)
        got = partner(stacked, bit, n)
        held = held + [got[i] for i in range(len(held))]
        owners = owners + [o ^ bit for o in owners]
        bit //= 2
    at = lax.broadcasted_iota(jnp.int32, (top, 1, 1), 0)
    out = jnp.broadcast_to(held[0][None], (top,) + x.shape)
    for piece, owner in zip(held[1:], owners[1:]):
        out = jnp.where(at == owner - base, piece[None], out)
    return out, base


def scatter_dp(parts, n):
    me = lax.axis_index("dp")
    acc = parts
    bit = 1
    while bit < n:
        pairs = acc.reshape((acc.shape[0] // 2, 2) + acc.shape[1:])
        mine = (me & bit) != 0
        keep = jnp.where(mine, pairs[:, 1], pairs[:, 0])
        send = jnp.where(mine, pairs[:, 0], pairs[:, 1])
        got = partner(send.astype(jnp.bfloat16), bit, n)
        acc = keep.astype(jnp.float32) + got.astype(jnp.float32)
        bit *= 2
    return acc[0]


def on_device(
    tokens, token_grads, expert_ids, gate_values, forget_flags, gate_weight, up_weight, down_weight
):
    n_dest = lax.axis_size("expert")
    n_dp = lax.axis_size("dp")
    row_count, width = tokens.shape
    me_dp = lax.axis_index("dp")
    w_down = down_weight[0]
    top = n_dp // 2
    half_cols = (n_dp * width) // 2
    if n_dp > 1:
        upper_half = (me_dp & top) != 0
        lend = jnp.where(upper_half, w_down[:, :half_cols], w_down[:, half_cols:]).T
        keep = jnp.where(upper_half, w_down[:, half_cols:], w_down[:, :half_cols]).T
        borrowed = partner(lend, top, n_dp)
    payload, pick_t = glue(expert_ids, gate_values, forget_flags, tokens, token_grads, n_dest)
    side = payload.shape[1] - 2 * width
    arrived = lax.all_to_all(payload, "expert", split_axis=0, concat_axis=0, tiled=True)
    slots = arrived.shape[0]
    part_tokens = arrived[:, :width]
    raw_grads = arrived[:, width : 2 * width]
    info = arrived[:, 2 * width :].astype(jnp.float32)
    gate_sel = (info[:, 0] + info[:, 1]) + info[:, 2]
    flag = info[:, 3]
    first_row = jnp.where(lax.broadcasted_iota(jnp.int32, (slots,), 0) % CAP == 0, 1.0, 0.0)
    block_hi = (first_row * info[:, 4]).astype(jnp.bfloat16)
    block_lo = (first_row * info[:, 5]).astype(jnp.bfloat16)
    every = jnp.ones((slots, slots), jnp.bfloat16)
    forget_count = 256.0 * jnp.dot(every, block_hi, preferred_element_type=jnp.float32) + jnp.dot(
        every, block_lo, preferred_element_type=jnp.float32
    )
    all_rows = row_count * n_dest
    half_total = jnp.float32(all_rows) / 2.0
    weight = jnp.where(
        flag == 1.0,
        -half_total / forget_count,
        half_total / (jnp.float32(all_rows) - forget_count),
    )
    scale = gate_sel * weight
    part_grads = (scale[:, None] * raw_grads.astype(jnp.float32)).astype(jnp.bfloat16)
    ff = gate_weight.shape[2]
    w_gate = gate_weight[0].reshape(n_dp, width, ff)
    w_up = up_weight[0].reshape(n_dp, width, ff)
    last_dims = (((1,), (1,)), ((), ()))
    if n_dp > 1:
        half_grads, _ = gather_half(part_grads, n_dp)
        half_dims = (((0, 2), (0, 1)), ((), ()))
        ff_down = w_down.shape[0]
        lent = lax.dot_general(
            half_grads, borrowed.reshape(top, width, ff_down), half_dims, preferred_element_type=jnp.float32
        )
        lent_hi = bf16_part(lent)
        lent_lo = lent - lent_hi
        outgoing = jnp.concatenate(
            [part_tokens, lent_hi.astype(jnp.bfloat16), lent_lo.astype(jnp.bfloat16)], axis=1
        )
        incoming = partner(outgoing, top, n_dp)
        share = incoming[:, width:].astype(jnp.float32)
        returned_share = share[:, :ff_down] + share[:, ff_down:]
        hidden_grad = lax.dot_general(
            half_grads, keep.reshape(top, width, ff_down), half_dims, preferred_element_type=jnp.float32
        )
        hidden_grad = hidden_grad + returned_share
        slot_tokens = gather_from([part_tokens, incoming[:, :width]], [me_dp, me_dp ^ top], top // 2, n_dp)
    else:
        hidden_grad = lax.dot_general(part_grads, w_down, last_dims, preferred_element_type=jnp.float32)
        slot_tokens = part_tokens[None]
    chunk_dims = (((0, 2), (0, 1)), ((), ()))
    gate_pre = lax.dot_general(slot_tokens, w_gate, chunk_dims, preferred_element_type=jnp.float32)
    up_pre = lax.dot_general(slot_tokens, w_up, chunk_dims, preferred_element_type=jnp.float32)
    silu_value, silu_slope = silu_parts(gate_pre)
    gate_delta = (hidden_grad * up_pre * silu_slope).astype(jnp.bfloat16)
    up_delta = (hidden_grad * silu_value).astype(jnp.bfloat16)
    slot_dims = (((1,), (0,)), ((), ()))
    grad_gate = lax.dot_general(
        slot_tokens, gate_delta, slot_dims, preferred_element_type=jnp.float32
    ).astype(jnp.bfloat16)
    grad_up = lax.dot_general(
        slot_tokens, up_delta, slot_dims, preferred_element_type=jnp.float32
    ).astype(jnp.bfloat16)
    back_dims = (((2,), (1,)), ((), ()))
    from_gate = lax.dot_general(w_gate, gate_delta, back_dims, preferred_element_type=jnp.float32)
    from_up = lax.dot_general(w_up, up_delta, back_dims, preferred_element_type=jnp.float32)
    part = (from_gate + from_up).astype(jnp.bfloat16)
    summed = scatter_dp(jnp.swapaxes(part, 1, 2), n_dp).astype(jnp.bfloat16)
    returned = lax.all_to_all(summed, "expert", split_axis=0, concat_axis=0, tiled=True)
    input_grad = lax.dot_general(
        pick_t, returned, (((0,), (0,)), ((), ())), preferred_element_type=jnp.float32
    )
    return (
        grad_gate.reshape(1, n_dp * width, ff),
        grad_up.reshape(1, n_dp * width, ff),
        input_grad.astype(jnp.bfloat16),
    )


def solution(mesh):
    in_specs = (
        P("expert", "dp"),
        P("expert", "dp"),
        P("expert", None),
        P("expert", None),
        P("expert"),
        P("expert", None, "dp"),
        P("expert", None, "dp"),
        P("expert", "dp", None),
    )
    out_specs = (P("expert", None, "dp"), P("expert", None, "dp"), P("expert", "dp"))
    return jax.shard_map(
        on_device, mesh=mesh, in_specs=in_specs, out_specs=out_specs, check_vma=False
    )
```

```python
import jax
import jax.numpy as jnp
from jax import lax
from jax.sharding import PartitionSpec as P
from jax.experimental import pallas as pl
from jax.experimental.pallas import tpu as pltpu

EXP_DEV = 8
CAP = 16


def glue_kernel(n_dest, width, side, split, ids_ref, gates_ref, flags_ref, tok_ref, grd_ref, *outs):
    f32, bf16 = jnp.float32, jnp.bfloat16
    rows = tok_ref.shape[0]
    slots = n_dest * CAP
    lanes = max(16, -(-n_dest // 16) * 16)
    ids = ids_ref[...]
    gates = gates_ref[...]
    flags = flags_ref[...].astype(f32)
    dest = lax.broadcasted_iota(jnp.int32, (lanes, rows), 0)
    edited = dest * EXP_DEV
    valid = dest < n_dest
    hits = jnp.zeros((lanes, rows), f32)
    gsel = jnp.zeros((lanes, rows), f32)
    for k in range(ids.shape[0]):
        m = (ids[k : k + 1, :] == edited) & valid
        hits = hits + jnp.where(m, 1.0, 0.0)
        gsel = gsel + jnp.where(m, gates[k : k + 1, :], 0.0)
    before = jnp.where(
        lax.broadcasted_iota(jnp.int32, (rows, rows), 0) < lax.broadcasted_iota(jnp.int32, (rows, rows), 1),
        1.0, 0.0,
    ).astype(bf16)
    rank = jnp.dot(hits.astype(bf16), before, preferred_element_type=f32)
    slot_of = lax.broadcasted_iota(jnp.int32, (slots, lanes), 0)
    expand = jnp.where(
        lax.shift_right_logical(slot_of, 4) == lax.broadcasted_iota(jnp.int32, (slots, lanes), 1), 1.0, 0.0
    ).astype(bf16)
    hit_s = jnp.dot(expand, hits.astype(bf16), preferred_element_type=f32)
    rank_s = jnp.dot(expand, rank.astype(bf16), preferred_element_type=f32)
    place = (lax.broadcasted_iota(jnp.int32, (slots, rows), 0) & (CAP - 1)).astype(f32)
    pick = jnp.where((hit_s == 1.0) & (rank_s == place), 1.0, 0.0)
    pick_b = pick.astype(bf16)
    tok = jnp.dot(pick_b, tok_ref[...], preferred_element_type=f32).astype(bf16)
    grd = jnp.dot(pick_b, grd_ref[...], preferred_element_type=f32).astype(bf16)
    hi = gsel.astype(bf16).astype(f32)
    rest = gsel - hi
    mid = rest.astype(bf16).astype(f32)
    lo = rest - mid

    def per_slot(x):
        spread = jnp.dot(expand, x.astype(bf16), preferred_element_type=f32)
        return jnp.sum(spread * pick, axis=1, keepdims=True)

    s_hi, s_mid, s_lo = per_slot(hi), per_slot(mid), per_slot(lo)
    s_flag = jnp.sum(pick * flags, axis=1, keepdims=True)
    count = jnp.sum(flags, axis=1, keepdims=True)
    c_hi = jnp.floor(count / 256.0)
    c_lo = count - 256.0 * c_hi
    col = lax.broadcasted_iota(jnp.int32, (slots, side), 1)
    side_v = jnp.where(col == 0, s_hi, 0.0)
    for c, v in ((1, s_mid), (2, s_lo), (3, s_flag), (4, c_hi), (5, c_lo)):
        side_v = jnp.where(col == c, v, side_v)
    side_v = side_v.astype(bf16)
    if split:
        tok_out, grd_out, side_out, pick_out = outs
        tok_out[...] = tok
        grd_out[...] = grd
        side_out[...] = side_v
    else:
        pay_out, pick_out = outs
        pay_out[:, :width] = tok
        pay_out[:, width : 2 * width] = grd
        pay_out[:, 2 * width :] = side_v
    pick_out[...] = pick_b


def glue(expert_ids, gate_values, forget_flags, tokens, token_grads, n_dest):
    import functools

    rows, width = tokens.shape
    slots = n_dest * CAP
    side = 128
    split = width % 128 != 0
    bf16 = jnp.bfloat16
    if split:
        shapes = [(slots, width), (slots, width), (slots, side), (slots, rows)]
    else:
        shapes = [(slots, 2 * width + side), (slots, rows)]
    vmem = pl.BlockSpec(memory_space=pltpu.VMEM)
    outs = pl.pallas_call(
        functools.partial(glue_kernel, n_dest, width, side, split),
        out_shape=[jax.ShapeDtypeStruct(s, bf16) for s in shapes],
        in_specs=[vmem] * 5,
        out_specs=[vmem] * len(shapes),
    )(expert_ids.T, gate_values.T, forget_flags.reshape(1, rows), tokens, token_grads)
    if split:
        return jnp.concatenate(outs[:3], axis=1), outs[3]
    return outs[0], outs[1]


def silu_parts(pre):
    sigmoid_gate = jax.nn.sigmoid(pre)
    return (pre * sigmoid_gate, sigmoid_gate * (1.0 + pre * (1.0 - sigmoid_gate)))


def bf16_part(x):
    return lax.reduce_precision(x, exponent_bits=8, mantissa_bits=7)


def partner(x, bit, n):
    return lax.ppermute(x, "dp", [(i, i ^ bit) for i in range(n)])


def gather_dp(x, n):
    me = lax.axis_index("dp")
    held = [x]
    owners = [me]
    bit = n // 2
    while bit >= 1:
        stacked = jnp.stack(held)
        got = partner(stacked, bit, n)
        held = held + [got[i] for i in range(len(held))]
        owners = owners + [o ^ bit for o in owners]
        bit //= 2
    at = lax.broadcasted_iota(jnp.int32, (n, 1, 1), 0)
    out = jnp.broadcast_to(held[0][None], (n,) + x.shape)
    for piece, owner in zip(held[1:], owners[1:]):
        out = jnp.where(at == owner, piece[None], out)
    return out


def gather_from(held, owners, bit, n):
    while bit >= 1:
        stacked = jnp.stack(held)
        got = partner(stacked, bit, n)
        held = held + [got[i] for i in range(len(held))]
        owners = owners + [o ^ bit for o in owners]
        bit //= 2
    at = lax.broadcasted_iota(jnp.int32, (n, 1, 1), 0)
    out = jnp.broadcast_to(held[0][None], (n,) + held[0].shape)
    for piece, owner in zip(held[1:], owners[1:]):
        out = jnp.where(at == owner, piece[None], out)
    return out


def gather_half(x, n):
    me = lax.axis_index("dp")
    top = n // 2
    base = me & top
    held = [x]
    owners = [me]
    bit = top // 2
    while bit >= 1:
        stacked = jnp.stack(held)
        got = partner(stacked, bit, n)
        held = held + [got[i] for i in range(len(held))]
        owners = owners + [o ^ bit for o in owners]
        bit //= 2
    at = lax.broadcasted_iota(jnp.int32, (top, 1, 1), 0)
    out = jnp.broadcast_to(held[0][None], (top,) + x.shape)
    for piece, owner in zip(held[1:], owners[1:]):
        out = jnp.where(at == owner - base, piece[None], out)
    return out, base


def scatter_dp(parts, n):
    return scatter_from(parts, 1, n)


def scatter_from(acc, bit, n):
    me = lax.axis_index("dp")
    while bit < n:
        pairs = acc.reshape((acc.shape[0] // 2, 2) + acc.shape[1:])
        mine = (me & bit) != 0
        keep = jnp.where(mine, pairs[:, 1], pairs[:, 0])
        send = jnp.where(mine, pairs[:, 0], pairs[:, 1])
        got = partner(send.astype(jnp.bfloat16), bit, n)
        acc = keep.astype(jnp.float32) + got.astype(jnp.float32)
        bit *= 2
    return acc[0]


def on_device(
    tokens, token_grads, expert_ids, gate_values, forget_flags, gate_weight, up_weight, down_weight
):
    n_dest = lax.axis_size("expert")
    n_dp = lax.axis_size("dp")
    row_count, width = tokens.shape
    me_dp = lax.axis_index("dp")
    w_down = down_weight[0]
    top = n_dp // 2
    half_cols = (n_dp * width) // 2
    if n_dp > 1:
        upper_half = (me_dp & top) != 0
        lend = jnp.where(upper_half, w_down[:, :half_cols], w_down[:, half_cols:]).T
        keep = jnp.where(upper_half, w_down[:, half_cols:], w_down[:, :half_cols]).T
        borrowed = partner(lend, top, n_dp)
    payload, pick_t = glue(expert_ids, gate_values, forget_flags, tokens, token_grads, n_dest)
    side = payload.shape[1] - 2 * width
    arrived = lax.all_to_all(payload, "expert", split_axis=0, concat_axis=0, tiled=True)
    slots = arrived.shape[0]
    part_tokens = arrived[:, :width]
    raw_grads = arrived[:, width : 2 * width]
    info = arrived[:, 2 * width :].astype(jnp.float32)
    gate_sel = (info[:, 0] + info[:, 1]) + info[:, 2]
    flag = info[:, 3]
    first_row = jnp.where(lax.broadcasted_iota(jnp.int32, (slots,), 0) % CAP == 0, 1.0, 0.0)
    block_hi = (first_row * info[:, 4]).astype(jnp.bfloat16)
    block_lo = (first_row * info[:, 5]).astype(jnp.bfloat16)
    every = jnp.ones((slots, slots), jnp.bfloat16)
    forget_count = 256.0 * jnp.dot(every, block_hi, preferred_element_type=jnp.float32) + jnp.dot(
        every, block_lo, preferred_element_type=jnp.float32
    )
    all_rows = row_count * n_dest
    half_total = jnp.float32(all_rows) / 2.0
    weight = jnp.where(
        flag == 1.0,
        -half_total / forget_count,
        half_total / (jnp.float32(all_rows) - forget_count),
    )
    scale = gate_sel * weight
    part_grads = (scale[:, None] * raw_grads.astype(jnp.float32)).astype(jnp.bfloat16)
    ff = gate_weight.shape[2]
    w_gate = gate_weight[0].reshape(n_dp, width, ff)
    w_up = up_weight[0].reshape(n_dp, width, ff)
    last_dims = (((1,), (1,)), ((), ()))
    if n_dp > 1:
        half_grads, _ = gather_half(part_grads, n_dp)
        half_dims = (((0, 2), (0, 1)), ((), ()))
        ff_down = w_down.shape[0]
        lent = lax.dot_general(
            half_grads, borrowed.reshape(top, width, ff_down), half_dims, preferred_element_type=jnp.float32
        )
        lent_hi = bf16_part(lent)
        lent_lo = lent - lent_hi
        outgoing = jnp.concatenate(
            [part_tokens, lent_hi.astype(jnp.bfloat16), lent_lo.astype(jnp.bfloat16)], axis=1
        )
        incoming = partner(outgoing, top, n_dp)
        share = incoming[:, width:].astype(jnp.float32)
        returned_share = share[:, :ff_down] + share[:, ff_down:]
        hidden_grad = lax.dot_general(
            half_grads, keep.reshape(top, width, ff_down), half_dims, preferred_element_type=jnp.float32
        )
        hidden_grad = hidden_grad + returned_share
        slot_tokens = gather_from([part_tokens, incoming[:, :width]], [me_dp, me_dp ^ top], top // 2, n_dp)
    else:
        hidden_grad = lax.dot_general(part_grads, w_down, last_dims, preferred_element_type=jnp.float32)
        slot_tokens = part_tokens[None]
    chunk_dims = (((0, 2), (0, 1)), ((), ()))
    gate_pre = lax.dot_general(slot_tokens, w_gate, chunk_dims, preferred_element_type=jnp.float32)
    up_pre = lax.dot_general(slot_tokens, w_up, chunk_dims, preferred_element_type=jnp.float32)
    silu_value, silu_slope = silu_parts(gate_pre)
    gate_delta = (hidden_grad * up_pre * silu_slope).astype(jnp.bfloat16)
    up_delta = (hidden_grad * silu_value).astype(jnp.bfloat16)
    slot_dims = (((1,), (0,)), ((), ()))
    grad_gate = lax.dot_general(
        slot_tokens, gate_delta, slot_dims, preferred_element_type=jnp.float32
    ).astype(jnp.bfloat16)
    grad_up = lax.dot_general(
        slot_tokens, up_delta, slot_dims, preferred_element_type=jnp.float32
    ).astype(jnp.bfloat16)
    back_dims = (((2,), (1,)), ((), ()))
    if n_dp > 1:
        odd = (me_dp & 1) != 0
        gate_pairs = w_gate.reshape(n_dp // 2, 2, width, ff)
        up_pairs = w_up.reshape(n_dp // 2, 2, width, ff)
        gate_send = jnp.where(odd, gate_pairs[:, 0], gate_pairs[:, 1])
        gate_keep = jnp.where(odd, gate_pairs[:, 1], gate_pairs[:, 0])
        up_send = jnp.where(odd, up_pairs[:, 0], up_pairs[:, 1])
        up_keep = jnp.where(odd, up_pairs[:, 1], up_pairs[:, 0])
        send_part = (
            lax.dot_general(gate_send, gate_delta, back_dims, preferred_element_type=jnp.float32)
            + lax.dot_general(up_send, up_delta, back_dims, preferred_element_type=jnp.float32)
        ).astype(jnp.bfloat16)
        got = partner(jnp.swapaxes(send_part, 1, 2), 1, n_dp)
        keep_part = (
            lax.dot_general(gate_keep, gate_delta, back_dims, preferred_element_type=jnp.float32)
            + lax.dot_general(up_keep, up_delta, back_dims, preferred_element_type=jnp.float32)
        ).astype(jnp.bfloat16)
        first = jnp.swapaxes(keep_part, 1, 2).astype(jnp.float32) + got.astype(jnp.float32)
        summed = scatter_from(first, 2, n_dp).astype(jnp.bfloat16)
    else:
        from_gate = lax.dot_general(w_gate, gate_delta, back_dims, preferred_element_type=jnp.float32)
        from_up = lax.dot_general(w_up, up_delta, back_dims, preferred_element_type=jnp.float32)
        summed = ((from_gate + from_up).astype(jnp.bfloat16)[0].T).astype(jnp.bfloat16)
    returned = lax.all_to_all(summed, "expert", split_axis=0, concat_axis=0, tiled=True)
    input_grad = lax.dot_general(
        pick_t, returned, (((0,), (0,)), ((), ())), preferred_element_type=jnp.float32
    )
    return (
        grad_gate.reshape(1, n_dp * width, ff),
        grad_up.reshape(1, n_dp * width, ff),
        input_grad.astype(jnp.bfloat16),
    )


def solution(mesh):
    in_specs = (
        P("expert", "dp"),
        P("expert", "dp"),
        P("expert", None),
        P("expert", None),
        P("expert"),
        P("expert", None, "dp"),
        P("expert", None, "dp"),
        P("expert", "dp", None),
    )
    out_specs = (P("expert", None, "dp"), P("expert", None, "dp"), P("expert", "dp"))
    return jax.shard_map(
        on_device, mesh=mesh, in_specs=in_specs, out_specs=out_specs, check_vma=False
    )
```

```python
import jax
import jax.numpy as jnp
from jax import lax
from jax.sharding import PartitionSpec as P
from jax.experimental import pallas as pl
from jax.experimental.pallas import tpu as pltpu

EXP_DEV = 8
CAP = 16


def glue_kernel(n_dest, width, side, split, ids_ref, gates_ref, flags_ref, tok_ref, grd_ref, *outs):
    f32, bf16 = jnp.float32, jnp.bfloat16
    rows = tok_ref.shape[0]
    slots = n_dest * CAP
    lanes = max(16, -(-n_dest // 16) * 16)
    ids = ids_ref[...]
    gates = gates_ref[...]
    flags = flags_ref[...].astype(f32)
    dest = lax.broadcasted_iota(jnp.int32, (lanes, rows), 0)
    edited = dest * EXP_DEV
    valid = dest < n_dest
    hits = jnp.zeros((lanes, rows), f32)
    gsel = jnp.zeros((lanes, rows), f32)
    for k in range(ids.shape[0]):
        m = (ids[k : k + 1, :] == edited) & valid
        hits = hits + jnp.where(m, 1.0, 0.0)
        gsel = gsel + jnp.where(m, gates[k : k + 1, :], 0.0)
    before = jnp.where(
        lax.broadcasted_iota(jnp.int32, (rows, rows), 0) < lax.broadcasted_iota(jnp.int32, (rows, rows), 1),
        1.0, 0.0,
    ).astype(bf16)
    rank = jnp.dot(hits.astype(bf16), before, preferred_element_type=f32)
    slot_of = lax.broadcasted_iota(jnp.int32, (slots, lanes), 0)
    expand = jnp.where(
        lax.shift_right_logical(slot_of, 4) == lax.broadcasted_iota(jnp.int32, (slots, lanes), 1), 1.0, 0.0
    ).astype(bf16)
    hit_s = jnp.dot(expand, hits.astype(bf16), preferred_element_type=f32)
    rank_s = jnp.dot(expand, rank.astype(bf16), preferred_element_type=f32)
    place = (lax.broadcasted_iota(jnp.int32, (slots, rows), 0) & (CAP - 1)).astype(f32)
    pick = jnp.where((hit_s == 1.0) & (rank_s == place), 1.0, 0.0)
    pick_b = pick.astype(bf16)
    tok = jnp.dot(pick_b, tok_ref[...], preferred_element_type=f32).astype(bf16)
    grd = jnp.dot(pick_b, grd_ref[...], preferred_element_type=f32).astype(bf16)
    hi = gsel.astype(bf16).astype(f32)
    rest = gsel - hi
    mid = rest.astype(bf16).astype(f32)
    lo = rest - mid

    def per_slot(x):
        spread = jnp.dot(expand, x.astype(bf16), preferred_element_type=f32)
        return jnp.sum(spread * pick, axis=1, keepdims=True)

    s_hi, s_mid, s_lo = per_slot(hi), per_slot(mid), per_slot(lo)
    s_flag = jnp.sum(pick * flags, axis=1, keepdims=True)
    count = jnp.sum(flags, axis=1, keepdims=True)
    c_hi = jnp.floor(count / 256.0)
    c_lo = count - 256.0 * c_hi
    col = lax.broadcasted_iota(jnp.int32, (slots, side), 1)
    side_v = jnp.where(col == 0, s_hi, 0.0)
    for c, v in ((1, s_mid), (2, s_lo), (3, s_flag), (4, c_hi), (5, c_lo)):
        side_v = jnp.where(col == c, v, side_v)
    side_v = side_v.astype(bf16)
    if split:
        tok_out, grd_out, side_out, pick_out = outs
        tok_out[...] = tok
        grd_out[...] = grd
        side_out[...] = side_v
    else:
        pay_out, pick_out = outs
        pay_out[:, :width] = tok
        pay_out[:, width : 2 * width] = grd
        pay_out[:, 2 * width :] = side_v
    pick_out[...] = pick_b


def glue(expert_ids, gate_values, forget_flags, tokens, token_grads, n_dest):
    import functools

    rows, width = tokens.shape
    slots = n_dest * CAP
    side = 128
    split = width % 128 != 0
    bf16 = jnp.bfloat16
    if split:
        shapes = [(slots, width), (slots, width), (slots, side), (slots, rows)]
    else:
        shapes = [(slots, 2 * width + side), (slots, rows)]
    vmem = pl.BlockSpec(memory_space=pltpu.VMEM)
    outs = pl.pallas_call(
        functools.partial(glue_kernel, n_dest, width, side, split),
        out_shape=[jax.ShapeDtypeStruct(s, bf16) for s in shapes],
        in_specs=[vmem] * 5,
        out_specs=[vmem] * len(shapes),
    )(expert_ids.T, gate_values.T, forget_flags.reshape(1, rows), tokens, token_grads)
    if split:
        return jnp.concatenate(outs[:3], axis=1), outs[3]
    return outs[0], outs[1]


def silu_parts(pre):
    sigmoid_gate = jax.nn.sigmoid(pre)
    return (pre * sigmoid_gate, sigmoid_gate * (1.0 + pre * (1.0 - sigmoid_gate)))


def bf16_part(x):
    return lax.reduce_precision(x, exponent_bits=8, mantissa_bits=7)


def partner(x, bit, n):
    return lax.ppermute(x, "dp", [(i, i ^ bit) for i in range(n)])


def gather_dp(x, n):
    me = lax.axis_index("dp")
    held = [x]
    owners = [me]
    bit = n // 2
    while bit >= 1:
        stacked = jnp.stack(held)
        got = partner(stacked, bit, n)
        held = held + [got[i] for i in range(len(held))]
        owners = owners + [o ^ bit for o in owners]
        bit //= 2
    at = lax.broadcasted_iota(jnp.int32, (n, 1, 1), 0)
    out = jnp.broadcast_to(held[0][None], (n,) + x.shape)
    for piece, owner in zip(held[1:], owners[1:]):
        out = jnp.where(at == owner, piece[None], out)
    return out


def gather_from(held, owners, bit, n):
    while bit >= 1:
        stacked = jnp.stack(held)
        got = partner(stacked, bit, n)
        held = held + [got[i] for i in range(len(held))]
        owners = owners + [o ^ bit for o in owners]
        bit //= 2
    at = lax.broadcasted_iota(jnp.int32, (n, 1, 1), 0)
    out = jnp.broadcast_to(held[0][None], (n,) + held[0].shape)
    for piece, owner in zip(held[1:], owners[1:]):
        out = jnp.where(at == owner, piece[None], out)
    return out


def gather_half(x, n):
    me = lax.axis_index("dp")
    top = n // 2
    base = me & top
    held = [x]
    owners = [me]
    bit = top // 2
    while bit >= 1:
        stacked = jnp.stack(held)
        got = partner(stacked, bit, n)
        held = held + [got[i] for i in range(len(held))]
        owners = owners + [o ^ bit for o in owners]
        bit //= 2
    at = lax.broadcasted_iota(jnp.int32, (top, 1, 1), 0)
    out = jnp.broadcast_to(held[0][None], (top,) + x.shape)
    for piece, owner in zip(held[1:], owners[1:]):
        out = jnp.where(at == owner - base, piece[None], out)
    return out, base


def scatter_dp(parts, n):
    me = lax.axis_index("dp")
    acc = parts
    bit = 1
    while bit < n:
        pairs = acc.reshape((acc.shape[0] // 2, 2) + acc.shape[1:])
        mine = (me & bit) != 0
        keep = jnp.where(mine, pairs[:, 1], pairs[:, 0])
        send = jnp.where(mine, pairs[:, 0], pairs[:, 1])
        got = partner(send.astype(jnp.bfloat16), bit, n)
        acc = keep.astype(jnp.float32) + got.astype(jnp.float32)
        bit *= 2
    return acc[0]


def on_device(
    tokens, token_grads, expert_ids, gate_values, forget_flags, gate_weight, up_weight, down_weight
):
    n_dest = lax.axis_size("expert")
    n_dp = lax.axis_size("dp")
    row_count, width = tokens.shape
    me_dp = lax.axis_index("dp")
    w_down = down_weight[0]
    top = n_dp // 2
    half_cols = (n_dp * width) // 2
    if n_dp > 1:
        upper_half = (me_dp & top) != 0
        lend = jnp.where(upper_half, w_down[:, :half_cols], w_down[:, half_cols:]).T
        keep = jnp.where(upper_half, w_down[:, half_cols:], w_down[:, :half_cols]).T
        borrowed = partner(lend, top, n_dp)
    payload, pick_t = glue(expert_ids, gate_values, forget_flags, tokens, token_grads, n_dest)
    side = payload.shape[1] - 2 * width
    arrived = lax.all_to_all(payload, "expert", split_axis=0, concat_axis=0, tiled=True)
    slots = arrived.shape[0]
    part_tokens = arrived[:, :width]
    raw_grads = arrived[:, width : 2 * width]
    info = arrived[:, 2 * width :].astype(jnp.float32)
    gate_sel = (info[:, 0] + info[:, 1]) + info[:, 2]
    flag = info[:, 3]
    first_row = jnp.where(lax.broadcasted_iota(jnp.int32, (slots,), 0) % CAP == 0, 1.0, 0.0)
    block_hi = (first_row * info[:, 4]).astype(jnp.bfloat16)
    block_lo = (first_row * info[:, 5]).astype(jnp.bfloat16)
    every = jnp.ones((slots, slots), jnp.bfloat16)
    forget_count = 256.0 * jnp.dot(every, block_hi, preferred_element_type=jnp.float32) + jnp.dot(
        every, block_lo, preferred_element_type=jnp.float32
    )
    all_rows = row_count * n_dest
    half_total = jnp.float32(all_rows) / 2.0
    weight = jnp.where(
        flag == 1.0,
        -half_total / forget_count,
        half_total / (jnp.float32(all_rows) - forget_count),
    )
    scale = gate_sel * weight
    part_grads = (scale[:, None] * raw_grads.astype(jnp.float32)).astype(jnp.bfloat16)
    ff = gate_weight.shape[2]
    w_gate = gate_weight[0].reshape(n_dp, width, ff)
    w_up = up_weight[0].reshape(n_dp, width, ff)
    last_dims = (((1,), (1,)), ((), ()))
    if n_dp > 1:
        half_grads, _ = gather_half(part_grads, n_dp)
        half_dims = (((0, 2), (0, 1)), ((), ()))
        ff_down = w_down.shape[0]
        lent = lax.dot_general(
            half_grads, borrowed.reshape(top, width, ff_down), half_dims, preferred_element_type=jnp.float32
        )
        outgoing = jnp.concatenate([part_tokens, lent.astype(jnp.bfloat16)], axis=1)
        incoming = partner(outgoing, top, n_dp)
        returned_share = incoming[:, width:].astype(jnp.float32)
        hidden_grad = lax.dot_general(
            half_grads, keep.reshape(top, width, ff_down), half_dims, preferred_element_type=jnp.float32
        )
        hidden_grad = hidden_grad + returned_share
        slot_tokens = gather_from([part_tokens, incoming[:, :width]], [me_dp, me_dp ^ top], top // 2, n_dp)
    else:
        hidden_grad = lax.dot_general(part_grads, w_down, last_dims, preferred_element_type=jnp.float32)
        slot_tokens = part_tokens[None]
    chunk_dims = (((0, 2), (0, 1)), ((), ()))
    gate_pre = lax.dot_general(slot_tokens, w_gate, chunk_dims, preferred_element_type=jnp.float32)
    up_pre = lax.dot_general(slot_tokens, w_up, chunk_dims, preferred_element_type=jnp.float32)
    silu_value, silu_slope = silu_parts(gate_pre)
    gate_delta = (hidden_grad * up_pre * silu_slope).astype(jnp.bfloat16)
    up_delta = (hidden_grad * silu_value).astype(jnp.bfloat16)
    slot_dims = (((1,), (0,)), ((), ()))
    grad_gate = lax.dot_general(
        slot_tokens, gate_delta, slot_dims, preferred_element_type=jnp.float32
    ).astype(jnp.bfloat16)
    grad_up = lax.dot_general(
        slot_tokens, up_delta, slot_dims, preferred_element_type=jnp.float32
    ).astype(jnp.bfloat16)
    back_dims = (((2,), (1,)), ((), ()))
    from_gate = lax.dot_general(w_gate, gate_delta, back_dims, preferred_element_type=jnp.float32)
    from_up = lax.dot_general(w_up, up_delta, back_dims, preferred_element_type=jnp.float32)
    part = (from_gate + from_up).astype(jnp.bfloat16)
    summed = scatter_dp(jnp.swapaxes(part, 1, 2), n_dp).astype(jnp.bfloat16)
    returned = lax.all_to_all(summed, "expert", split_axis=0, concat_axis=0, tiled=True)
    input_grad = lax.dot_general(
        pick_t, returned, (((0,), (0,)), ((), ())), preferred_element_type=jnp.float32
    )
    return (
        grad_gate.reshape(1, n_dp * width, ff),
        grad_up.reshape(1, n_dp * width, ff),
        input_grad.astype(jnp.bfloat16),
    )


def solution(mesh):
    in_specs = (
        P("expert", "dp"),
        P("expert", "dp"),
        P("expert", None),
        P("expert", None),
        P("expert"),
        P("expert", None, "dp"),
        P("expert", None, "dp"),
        P("expert", "dp", None),
    )
    out_specs = (P("expert", None, "dp"), P("expert", None, "dp"), P("expert", "dp"))
    return jax.shard_map(
        on_device, mesh=mesh, in_specs=in_specs, out_specs=out_specs, check_vma=False
    )
```

```python
import jax
import jax.numpy as jnp
from jax import lax
from jax.sharding import PartitionSpec as P
from jax.experimental import pallas as pl
from jax.experimental.pallas import tpu as pltpu

EXP_DEV = 8
CAP = 16


def glue_kernel(n_dest, width, side, split, ids_ref, gates_ref, flags_ref, tok_hbm, grd_hbm, *rest):
    outs, (tok_ref, grd_ref, sems) = rest[:-3], rest[-3:]
    tok_copy = pltpu.make_async_copy(tok_hbm, tok_ref, sems.at[0])
    grd_copy = pltpu.make_async_copy(grd_hbm, grd_ref, sems.at[1])
    tok_copy.start()
    grd_copy.start()
    f32, bf16 = jnp.float32, jnp.bfloat16
    rows = tok_ref.shape[0]
    slots = n_dest * CAP
    lanes = max(16, -(-n_dest // 16) * 16)
    ids = ids_ref[...]
    gates = gates_ref[...]
    flags = flags_ref[...].astype(f32)
    dest = lax.broadcasted_iota(jnp.int32, (lanes, rows), 0)
    edited = dest * EXP_DEV
    valid = dest < n_dest
    hits = jnp.zeros((lanes, rows), f32)
    gsel = jnp.zeros((lanes, rows), f32)
    for k in range(ids.shape[0]):
        m = (ids[k : k + 1, :] == edited) & valid
        hits = hits + jnp.where(m, 1.0, 0.0)
        gsel = gsel + jnp.where(m, gates[k : k + 1, :], 0.0)
    before = jnp.where(
        lax.broadcasted_iota(jnp.int32, (rows, rows), 0) < lax.broadcasted_iota(jnp.int32, (rows, rows), 1),
        1.0, 0.0,
    ).astype(bf16)
    rank = jnp.dot(hits.astype(bf16), before, preferred_element_type=f32)
    slot_of = lax.broadcasted_iota(jnp.int32, (slots, lanes), 0)
    expand = jnp.where(
        lax.shift_right_logical(slot_of, 4) == lax.broadcasted_iota(jnp.int32, (slots, lanes), 1), 1.0, 0.0
    ).astype(bf16)
    hit_s = jnp.dot(expand, hits.astype(bf16), preferred_element_type=f32)
    rank_s = jnp.dot(expand, rank.astype(bf16), preferred_element_type=f32)
    place = (lax.broadcasted_iota(jnp.int32, (slots, rows), 0) & (CAP - 1)).astype(f32)
    pick = jnp.where((hit_s == 1.0) & (rank_s == place), 1.0, 0.0)
    pick_b = pick.astype(bf16)
    tok_copy.wait()
    grd_copy.wait()
    tok = jnp.dot(pick_b, tok_ref[...], preferred_element_type=f32).astype(bf16)
    grd = jnp.dot(pick_b, grd_ref[...], preferred_element_type=f32).astype(bf16)
    hi = gsel.astype(bf16).astype(f32)
    rest = gsel - hi
    mid = rest.astype(bf16).astype(f32)
    lo = rest - mid

    def per_slot(x):
        spread = jnp.dot(expand, x.astype(bf16), preferred_element_type=f32)
        return jnp.sum(spread * pick, axis=1, keepdims=True)

    s_hi, s_mid, s_lo = per_slot(hi), per_slot(mid), per_slot(lo)
    s_flag = jnp.sum(pick * flags, axis=1, keepdims=True)
    count = jnp.sum(flags, axis=1, keepdims=True)
    c_hi = jnp.floor(count / 256.0)
    c_lo = count - 256.0 * c_hi
    col = lax.broadcasted_iota(jnp.int32, (slots, side), 1)
    side_v = jnp.where(col == 0, s_hi, 0.0)
    for c, v in ((1, s_mid), (2, s_lo), (3, s_flag), (4, c_hi), (5, c_lo)):
        side_v = jnp.where(col == c, v, side_v)
    side_v = side_v.astype(bf16)
    if split:
        tok_out, grd_out, side_out, pick_out = outs
        tok_out[...] = tok
        grd_out[...] = grd
        side_out[...] = side_v
    else:
        pay_out, pick_out = outs
        pay_out[:, :width] = tok
        pay_out[:, width : 2 * width] = grd
        pay_out[:, 2 * width :] = side_v
    pick_out[...] = pick_b


def glue(expert_ids, gate_values, forget_flags, tokens, token_grads, n_dest):
    import functools

    rows, width = tokens.shape
    slots = n_dest * CAP
    side = 128
    split = width % 128 != 0
    bf16 = jnp.bfloat16
    if split:
        shapes = [(slots, width), (slots, width), (slots, side), (slots, rows)]
    else:
        shapes = [(slots, 2 * width + side), (slots, rows)]
    vmem = pl.BlockSpec(memory_space=pltpu.VMEM)
    outs = pl.pallas_call(
        functools.partial(glue_kernel, n_dest, width, side, split),
        out_shape=[jax.ShapeDtypeStruct(s, bf16) for s in shapes],
        in_specs=[vmem] * 3 + [pl.BlockSpec(memory_space=pl.ANY)] * 2,
        out_specs=[vmem] * len(shapes),
        scratch_shapes=[
            pltpu.VMEM((rows, width), bf16),
            pltpu.VMEM((rows, width), bf16),
            pltpu.SemaphoreType.DMA((2,)),
        ],
    )(expert_ids.T, gate_values.T, forget_flags.reshape(1, rows), tokens, token_grads)
    if split:
        return jnp.concatenate(outs[:3], axis=1), outs[3]
    return outs[0], outs[1]


def silu_parts(pre):
    sigmoid_gate = jax.nn.sigmoid(pre)
    return (pre * sigmoid_gate, sigmoid_gate * (1.0 + pre * (1.0 - sigmoid_gate)))


def bf16_part(x):
    return lax.reduce_precision(x, exponent_bits=8, mantissa_bits=7)


def partner(x, bit, n):
    return lax.ppermute(x, "dp", [(i, i ^ bit) for i in range(n)])


def gather_dp(x, n):
    me = lax.axis_index("dp")
    held = [x]
    owners = [me]
    bit = n // 2
    while bit >= 1:
        stacked = jnp.stack(held)
        got = partner(stacked, bit, n)
        held = held + [got[i] for i in range(len(held))]
        owners = owners + [o ^ bit for o in owners]
        bit //= 2
    at = lax.broadcasted_iota(jnp.int32, (n, 1, 1), 0)
    out = jnp.broadcast_to(held[0][None], (n,) + x.shape)
    for piece, owner in zip(held[1:], owners[1:]):
        out = jnp.where(at == owner, piece[None], out)
    return out


def gather_from(held, owners, bit, n):
    while bit >= 1:
        stacked = jnp.stack(held)
        got = partner(stacked, bit, n)
        held = held + [got[i] for i in range(len(held))]
        owners = owners + [o ^ bit for o in owners]
        bit //= 2
    at = lax.broadcasted_iota(jnp.int32, (n, 1, 1), 0)
    out = jnp.broadcast_to(held[0][None], (n,) + held[0].shape)
    for piece, owner in zip(held[1:], owners[1:]):
        out = jnp.where(at == owner, piece[None], out)
    return out


def gather_half(x, n):
    me = lax.axis_index("dp")
    top = n // 2
    base = me & top
    held = [x]
    owners = [me]
    bit = top // 2
    while bit >= 1:
        stacked = jnp.stack(held)
        got = partner(stacked, bit, n)
        held = held + [got[i] for i in range(len(held))]
        owners = owners + [o ^ bit for o in owners]
        bit //= 2
    at = lax.broadcasted_iota(jnp.int32, (top, 1, 1), 0)
    out = jnp.broadcast_to(held[0][None], (top,) + x.shape)
    for piece, owner in zip(held[1:], owners[1:]):
        out = jnp.where(at == owner - base, piece[None], out)
    return out, base


def scatter_dp(parts, n):
    me = lax.axis_index("dp")
    acc = parts
    bit = 1
    while bit < n:
        pairs = acc.reshape((acc.shape[0] // 2, 2) + acc.shape[1:])
        mine = (me & bit) != 0
        keep = jnp.where(mine, pairs[:, 1], pairs[:, 0])
        send = jnp.where(mine, pairs[:, 0], pairs[:, 1])
        got = partner(send.astype(jnp.bfloat16), bit, n)
        acc = keep.astype(jnp.float32) + got.astype(jnp.float32)
        bit *= 2
    return acc[0]


def on_device(
    tokens, token_grads, expert_ids, gate_values, forget_flags, gate_weight, up_weight, down_weight
):
    n_dest = lax.axis_size("expert")
    n_dp = lax.axis_size("dp")
    row_count, width = tokens.shape
    me_dp = lax.axis_index("dp")
    w_down = down_weight[0]
    top = n_dp // 2
    half_cols = (n_dp * width) // 2
    if n_dp > 1:
        upper_half = (me_dp & top) != 0
        lend = jnp.where(upper_half, w_down[:, :half_cols], w_down[:, half_cols:]).T
        keep = jnp.where(upper_half, w_down[:, half_cols:], w_down[:, :half_cols]).T
        borrowed = partner(lend, top, n_dp)
    payload, pick_t = glue(expert_ids, gate_values, forget_flags, tokens, token_grads, n_dest)
    side = payload.shape[1] - 2 * width
    arrived = lax.all_to_all(payload, "expert", split_axis=0, concat_axis=0, tiled=True)
    slots = arrived.shape[0]
    part_tokens = arrived[:, :width]
    raw_grads = arrived[:, width : 2 * width]
    info = arrived[:, 2 * width :].astype(jnp.float32)
    gate_sel = (info[:, 0] + info[:, 1]) + info[:, 2]
    flag = info[:, 3]
    first_row = jnp.where(lax.broadcasted_iota(jnp.int32, (slots,), 0) % CAP == 0, 1.0, 0.0)
    block_hi = (first_row * info[:, 4]).astype(jnp.bfloat16)
    block_lo = (first_row * info[:, 5]).astype(jnp.bfloat16)
    every = jnp.ones((slots, slots), jnp.bfloat16)
    forget_count = 256.0 * jnp.dot(every, block_hi, preferred_element_type=jnp.float32) + jnp.dot(
        every, block_lo, preferred_element_type=jnp.float32
    )
    all_rows = row_count * n_dest
    half_total = jnp.float32(all_rows) / 2.0
    weight = jnp.where(
        flag == 1.0,
        -half_total / forget_count,
        half_total / (jnp.float32(all_rows) - forget_count),
    )
    scale = gate_sel * weight
    part_grads = (scale[:, None] * raw_grads.astype(jnp.float32)).astype(jnp.bfloat16)
    ff = gate_weight.shape[2]
    w_gate = gate_weight[0].reshape(n_dp, width, ff)
    w_up = up_weight[0].reshape(n_dp, width, ff)
    last_dims = (((1,), (1,)), ((), ()))
    if n_dp > 1:
        half_grads, _ = gather_half(part_grads, n_dp)
        half_dims = (((0, 2), (0, 1)), ((), ()))
        ff_down = w_down.shape[0]
        lent = lax.dot_general(
            half_grads, borrowed.reshape(top, width, ff_down), half_dims, preferred_element_type=jnp.float32
        )
        lent_hi = bf16_part(lent)
        lent_lo = lent - lent_hi
        outgoing = jnp.concatenate(
            [part_tokens, lent_hi.astype(jnp.bfloat16), lent_lo.astype(jnp.bfloat16)], axis=1
        )
        incoming = partner(outgoing, top, n_dp)
        share = incoming[:, width:].astype(jnp.float32)
        returned_share = share[:, :ff_down] + share[:, ff_down:]
        hidden_grad = lax.dot_general(
            half_grads, keep.reshape(top, width, ff_down), half_dims, preferred_element_type=jnp.float32
        )
        hidden_grad = hidden_grad + returned_share
        slot_tokens = gather_from([part_tokens, incoming[:, :width]], [me_dp, me_dp ^ top], top // 2, n_dp)
    else:
        hidden_grad = lax.dot_general(part_grads, w_down, last_dims, preferred_element_type=jnp.float32)
        slot_tokens = part_tokens[None]
    chunk_dims = (((0, 2), (0, 1)), ((), ()))
    gate_pre = lax.dot_general(slot_tokens, w_gate, chunk_dims, preferred_element_type=jnp.float32)
    up_pre = lax.dot_general(slot_tokens, w_up, chunk_dims, preferred_element_type=jnp.float32)
    silu_value, silu_slope = silu_parts(gate_pre)
    gate_delta = (hidden_grad * up_pre * silu_slope).astype(jnp.bfloat16)
    up_delta = (hidden_grad * silu_value).astype(jnp.bfloat16)
    slot_dims = (((1,), (0,)), ((), ()))
    grad_gate = lax.dot_general(
        slot_tokens, gate_delta, slot_dims, preferred_element_type=jnp.float32
    ).astype(jnp.bfloat16)
    grad_up = lax.dot_general(
        slot_tokens, up_delta, slot_dims, preferred_element_type=jnp.float32
    ).astype(jnp.bfloat16)
    back_dims = (((2,), (1,)), ((), ()))
    from_gate = lax.dot_general(w_gate, gate_delta, back_dims, preferred_element_type=jnp.float32)
    from_up = lax.dot_general(w_up, up_delta, back_dims, preferred_element_type=jnp.float32)
    part = (from_gate + from_up).astype(jnp.bfloat16)
    summed = scatter_dp(jnp.swapaxes(part, 1, 2), n_dp).astype(jnp.bfloat16)
    returned = lax.all_to_all(summed, "expert", split_axis=0, concat_axis=0, tiled=True)
    input_grad = lax.dot_general(
        pick_t, returned, (((0,), (0,)), ((), ())), preferred_element_type=jnp.float32
    )
    return (
        grad_gate.reshape(1, n_dp * width, ff),
        grad_up.reshape(1, n_dp * width, ff),
        input_grad.astype(jnp.bfloat16),
    )


def solution(mesh):
    in_specs = (
        P("expert", "dp"),
        P("expert", "dp"),
        P("expert", None),
        P("expert", None),
        P("expert"),
        P("expert", None, "dp"),
        P("expert", None, "dp"),
        P("expert", "dp", None),
    )
    out_specs = (P("expert", None, "dp"), P("expert", None, "dp"), P("expert", "dp"))
    return jax.shard_map(
        on_device, mesh=mesh, in_specs=in_specs, out_specs=out_specs, check_vma=False
    )
```

```python
import jax
import jax.numpy as jnp
from jax import lax
from jax.sharding import PartitionSpec as P
from jax.experimental import pallas as pl
from jax.experimental.pallas import tpu as pltpu

EXP_DEV = 8
CAP = 16


def glue_kernel(n_dest, width, side, split, ids_ref, gates_ref, flags_ref, tok_ref, grd_ref, *outs):
    f32, bf16 = jnp.float32, jnp.bfloat16
    rows = tok_ref.shape[0]
    slots = n_dest * CAP
    lanes = max(16, -(-n_dest // 16) * 16)
    ids = ids_ref[...]
    gates = gates_ref[...]
    flags = flags_ref[...].astype(f32)
    dest = lax.broadcasted_iota(jnp.int32, (lanes, rows), 0)
    edited = dest * EXP_DEV
    valid = dest < n_dest
    hits = jnp.zeros((lanes, rows), f32)
    gsel = jnp.zeros((lanes, rows), f32)
    for k in range(ids.shape[0]):
        m = (ids[k : k + 1, :] == edited) & valid
        hits = hits + jnp.where(m, 1.0, 0.0)
        gsel = gsel + jnp.where(m, gates[k : k + 1, :], 0.0)
    before = jnp.where(
        lax.broadcasted_iota(jnp.int32, (rows, rows), 0) < lax.broadcasted_iota(jnp.int32, (rows, rows), 1),
        1.0, 0.0,
    ).astype(bf16)
    rank = jnp.dot(hits.astype(bf16), before, preferred_element_type=f32)
    slot_of = lax.broadcasted_iota(jnp.int32, (slots, lanes), 0)
    expand = jnp.where(
        lax.shift_right_logical(slot_of, 4) == lax.broadcasted_iota(jnp.int32, (slots, lanes), 1), 1.0, 0.0
    ).astype(bf16)
    hit_s = jnp.dot(expand, hits.astype(bf16), preferred_element_type=f32)
    rank_s = jnp.dot(expand, rank.astype(bf16), preferred_element_type=f32)
    place = (lax.broadcasted_iota(jnp.int32, (slots, rows), 0) & (CAP - 1)).astype(f32)
    pick = jnp.where((hit_s == 1.0) & (rank_s == place), 1.0, 0.0)
    pick_b = pick.astype(bf16)
    tok = jnp.dot(pick_b, tok_ref[...], preferred_element_type=f32).astype(bf16)
    grd = jnp.dot(pick_b, grd_ref[...], preferred_element_type=f32).astype(bf16)
    hi = gsel.astype(bf16).astype(f32)
    rest = gsel - hi
    mid = rest.astype(bf16).astype(f32)
    lo = rest - mid

    def per_slot(x):
        spread = jnp.dot(expand, x.astype(bf16), preferred_element_type=f32)
        return jnp.sum(spread * pick, axis=1, keepdims=True)

    s_hi, s_mid, s_lo = per_slot(hi), per_slot(mid), per_slot(lo)
    s_flag = jnp.sum(pick * flags, axis=1, keepdims=True)
    count = jnp.sum(flags, axis=1, keepdims=True)
    c_hi = jnp.floor(count / 256.0)
    c_lo = count - 256.0 * c_hi
    col = lax.broadcasted_iota(jnp.int32, (slots, side), 1)
    side_v = jnp.where(col == 0, s_hi, 0.0)
    for c, v in ((1, s_mid), (2, s_lo), (3, s_flag), (4, c_hi), (5, c_lo)):
        side_v = jnp.where(col == c, v, side_v)
    side_v = side_v.astype(bf16)
    if split:
        tok_out, grd_out, side_out, pick_out = outs
        tok_out[...] = tok
        grd_out[...] = grd
        side_out[...] = side_v
    else:
        pay_out, pick_out = outs
        pay_out[:, :width] = tok
        pay_out[:, width : 2 * width] = grd
        pay_out[:, 2 * width :] = side_v
    pick_out[...] = pick_b


def glue(expert_ids, gate_values, forget_flags, tokens, token_grads, n_dest):
    import functools

    rows, width = tokens.shape
    slots = n_dest * CAP
    side = 128
    split = width % 128 != 0
    bf16 = jnp.bfloat16
    if split:
        shapes = [(slots, width), (slots, width), (slots, side), (slots, rows)]
    else:
        shapes = [(slots, 2 * width + side), (slots, rows)]
    vmem = pl.BlockSpec(memory_space=pltpu.VMEM)
    outs = pl.pallas_call(
        functools.partial(glue_kernel, n_dest, width, side, split),
        out_shape=[jax.ShapeDtypeStruct(s, bf16) for s in shapes],
        in_specs=[vmem] * 5,
        out_specs=[vmem] * len(shapes),
    )(expert_ids.T, gate_values.T, forget_flags.reshape(1, rows), tokens, token_grads)
    if split:
        return jnp.concatenate(outs[:3], axis=1), outs[3]
    return outs[0], outs[1]


def silu_parts(pre):
    sigmoid_gate = jax.nn.sigmoid(pre)
    return (pre * sigmoid_gate, sigmoid_gate * (1.0 + pre * (1.0 - sigmoid_gate)))


def bf16_part(x):
    return lax.reduce_precision(x, exponent_bits=8, mantissa_bits=7)


def partner(x, bit, n):
    return lax.ppermute(x, "dp", [(i, i ^ bit) for i in range(n)])


def gather_dp(x, n):
    me = lax.axis_index("dp")
    held = [x]
    owners = [me]
    bit = n // 2
    while bit >= 1:
        stacked = jnp.stack(held)
        got = partner(stacked, bit, n)
        held = held + [got[i] for i in range(len(held))]
        owners = owners + [o ^ bit for o in owners]
        bit //= 2
    at = lax.broadcasted_iota(jnp.int32, (n, 1, 1), 0)
    out = jnp.broadcast_to(held[0][None], (n,) + x.shape)
    for piece, owner in zip(held[1:], owners[1:]):
        out = jnp.where(at == owner, piece[None], out)
    return out


def gather_from(held, owners, bit, n):
    while bit >= 1:
        stacked = jnp.stack(held)
        got = partner(stacked, bit, n)
        held = held + [got[i] for i in range(len(held))]
        owners = owners + [o ^ bit for o in owners]
        bit //= 2
    at = lax.broadcasted_iota(jnp.int32, (n, 1, 1), 0)
    out = jnp.broadcast_to(held[0][None], (n,) + held[0].shape)
    for piece, owner in zip(held[1:], owners[1:]):
        out = jnp.where(at == owner, piece[None], out)
    return out


def gather_half(x, n):
    me = lax.axis_index("dp")
    top = n // 2
    base = me & top
    held = [x]
    owners = [me]
    bit = top // 2
    while bit >= 1:
        stacked = jnp.stack(held)
        got = partner(stacked, bit, n)
        held = held + [got[i] for i in range(len(held))]
        owners = owners + [o ^ bit for o in owners]
        bit //= 2
    at = lax.broadcasted_iota(jnp.int32, (top, 1, 1), 0)
    out = jnp.broadcast_to(held[0][None], (top,) + x.shape)
    for piece, owner in zip(held[1:], owners[1:]):
        out = jnp.where(at == owner - base, piece[None], out)
    return out, base


def scatter_dp(parts, n):
    me = lax.axis_index("dp")
    acc = parts
    bit = 1
    while bit < n:
        pairs = acc.reshape((acc.shape[0] // 2, 2) + acc.shape[1:])
        mine = (me & bit) != 0
        keep = jnp.where(mine, pairs[:, 1], pairs[:, 0])
        send = jnp.where(mine, pairs[:, 0], pairs[:, 1])
        got = partner(send.astype(jnp.bfloat16), bit, n)
        acc = keep.astype(jnp.float32) + got.astype(jnp.float32)
        bit *= 2
    return acc[0]


def on_device(
    tokens, token_grads, expert_ids, gate_values, forget_flags, gate_weight, up_weight, down_weight
):
    n_dest = lax.axis_size("expert")
    n_dp = lax.axis_size("dp")
    row_count, width = tokens.shape
    me_dp = lax.axis_index("dp")
    w_down = down_weight[0]
    top = n_dp // 2
    half_cols = (n_dp * width) // 2
    if n_dp > 1:
        upper_half = (me_dp & top) != 0
        lend = jnp.where(upper_half, w_down[:, :half_cols], w_down[:, half_cols:]).T
        keep = jnp.where(upper_half, w_down[:, half_cols:], w_down[:, :half_cols]).T
        borrowed = partner(lend, top, n_dp)
    payload, pick_t = glue(expert_ids, gate_values, forget_flags, tokens, token_grads, n_dest)
    side = payload.shape[1] - 2 * width
    arrived = lax.all_to_all(payload, "expert", split_axis=0, concat_axis=0, tiled=True)
    slots = arrived.shape[0]
    part_tokens = arrived[:, :width]
    raw_grads = arrived[:, width : 2 * width]
    info = arrived[:, 2 * width :].astype(jnp.float32)
    gate_sel = (info[:, 0] + info[:, 1]) + info[:, 2]
    flag = info[:, 3]
    first_row = jnp.where(lax.broadcasted_iota(jnp.int32, (slots,), 0) % CAP == 0, 1.0, 0.0)
    block_hi = (first_row * info[:, 4]).astype(jnp.bfloat16)
    block_lo = (first_row * info[:, 5]).astype(jnp.bfloat16)
    every = jnp.ones((slots, slots), jnp.bfloat16)
    forget_count = 256.0 * jnp.dot(every, block_hi, preferred_element_type=jnp.float32) + jnp.dot(
        every, block_lo, preferred_element_type=jnp.float32
    )
    all_rows = row_count * n_dest
    half_total = jnp.float32(all_rows) / 2.0
    weight = jnp.where(
        flag == 1.0,
        -half_total / forget_count,
        half_total / (jnp.float32(all_rows) - forget_count),
    )
    scale = gate_sel * weight
    part_grads = (scale[:, None] * raw_grads.astype(jnp.float32)).astype(jnp.bfloat16)
    ff = gate_weight.shape[2]
    w_gate = gate_weight[0].reshape(n_dp, width, ff)
    w_up = up_weight[0].reshape(n_dp, width, ff)
    last_dims = (((1,), (1,)), ((), ()))
    if n_dp > 1:
        half_grads, _ = gather_half(part_grads, n_dp)
        half_dims = (((0, 2), (0, 1)), ((), ()))
        ff_down = w_down.shape[0]
        lent = lax.dot_general(
            half_grads, borrowed.reshape(top, width, ff_down), half_dims, preferred_element_type=jnp.float32
        )
        lent_hi = bf16_part(lent)
        lent_lo = lent - lent_hi
        outgoing = jnp.concatenate(
            [part_tokens, lent_hi.astype(jnp.bfloat16), lent_lo.astype(jnp.bfloat16)], axis=1
        )
        incoming = partner(outgoing, top, n_dp)
        share = incoming[:, width:].astype(jnp.float32)
        returned_share = share[:, :ff_down] + share[:, ff_down:]
        hidden_grad = lax.dot_general(
            half_grads, keep.reshape(top, width, ff_down), half_dims, preferred_element_type=jnp.float32
        )
        hidden_grad = hidden_grad + returned_share
        held, offs = [part_tokens, incoming[:, :width]], [0, top]
        bit = top // 2
        while bit >= 1:
            got = partner(jnp.stack(held), bit, n_dp)
            held = held + [got[i] for i in range(len(held))]
            offs = offs + [o ^ bit for o in offs]
            bit //= 2
        order = me_dp ^ jnp.array(offs, jnp.int32)
        gate_rel = jnp.take(w_gate, order, axis=0)
        up_rel = jnp.take(w_up, order, axis=0)
        early, late = jnp.stack(held[:top]), jnp.stack(held[top:])
        rel_dims = (((0, 2), (0, 1)), ((), ()))
        gate_pre = lax.dot_general(early, gate_rel[:top], rel_dims, preferred_element_type=jnp.float32) + lax.dot_general(
            late, gate_rel[top:], rel_dims, preferred_element_type=jnp.float32
        )
        up_pre = lax.dot_general(early, up_rel[:top], rel_dims, preferred_element_type=jnp.float32) + lax.dot_general(
            late, up_rel[top:], rel_dims, preferred_element_type=jnp.float32
        )
        at = lax.broadcasted_iota(jnp.int32, (n_dp, 1, 1), 0)
        slot_tokens = jnp.broadcast_to(held[0][None], (n_dp,) + held[0].shape)
        for piece, o in zip(held[1:], offs[1:]):
            slot_tokens = jnp.where(at == (me_dp ^ o), piece[None], slot_tokens)
    else:
        hidden_grad = lax.dot_general(part_grads, w_down, last_dims, preferred_element_type=jnp.float32)
        slot_tokens = part_tokens[None]
        chunk_dims = (((0, 2), (0, 1)), ((), ()))
        gate_pre = lax.dot_general(slot_tokens, w_gate, chunk_dims, preferred_element_type=jnp.float32)
        up_pre = lax.dot_general(slot_tokens, w_up, chunk_dims, preferred_element_type=jnp.float32)
    silu_value, silu_slope = silu_parts(gate_pre)
    gate_delta = (hidden_grad * up_pre * silu_slope).astype(jnp.bfloat16)
    up_delta = (hidden_grad * silu_value).astype(jnp.bfloat16)
    slot_dims = (((1,), (0,)), ((), ()))
    grad_gate = lax.dot_general(
        slot_tokens, gate_delta, slot_dims, preferred_element_type=jnp.float32
    ).astype(jnp.bfloat16)
    grad_up = lax.dot_general(
        slot_tokens, up_delta, slot_dims, preferred_element_type=jnp.float32
    ).astype(jnp.bfloat16)
    back_dims = (((2,), (1,)), ((), ()))
    from_gate = lax.dot_general(w_gate, gate_delta, back_dims, preferred_element_type=jnp.float32)
    from_up = lax.dot_general(w_up, up_delta, back_dims, preferred_element_type=jnp.float32)
    part = (from_gate + from_up).astype(jnp.bfloat16)
    summed = scatter_dp(jnp.swapaxes(part, 1, 2), n_dp).astype(jnp.bfloat16)
    returned = lax.all_to_all(summed, "expert", split_axis=0, concat_axis=0, tiled=True)
    input_grad = lax.dot_general(
        pick_t, returned, (((0,), (0,)), ((), ())), preferred_element_type=jnp.float32
    )
    return (
        grad_gate.reshape(1, n_dp * width, ff),
        grad_up.reshape(1, n_dp * width, ff),
        input_grad.astype(jnp.bfloat16),
    )


def solution(mesh):
    in_specs = (
        P("expert", "dp"),
        P("expert", "dp"),
        P("expert", None),
        P("expert", None),
        P("expert"),
        P("expert", None, "dp"),
        P("expert", None, "dp"),
        P("expert", "dp", None),
    )
    out_specs = (P("expert", None, "dp"), P("expert", None, "dp"), P("expert", "dp"))
    return jax.shard_map(
        on_device, mesh=mesh, in_specs=in_specs, out_specs=out_specs, check_vma=False
    )
```

```python
import jax
import jax.numpy as jnp
from jax import lax
from jax.sharding import PartitionSpec as P
from jax.experimental import pallas as pl
from jax.experimental.pallas import tpu as pltpu

EXP_DEV = 8
CAP = 16


def glue_kernel(n_dest, width, side, split, ids_ref, gates_ref, flags_ref, tok_ref, grd_ref, *outs):
    f32, bf16 = jnp.float32, jnp.bfloat16
    rows = tok_ref.shape[0]
    slots = n_dest * CAP
    lanes = max(16, -(-n_dest // 16) * 16)
    ids = ids_ref[...]
    gates = gates_ref[...]
    flags = flags_ref[...].astype(f32)
    dest = lax.broadcasted_iota(jnp.int32, (lanes, rows), 0)
    edited = dest * EXP_DEV
    valid = dest < n_dest
    hits = jnp.zeros((lanes, rows), f32)
    gsel = jnp.zeros((lanes, rows), f32)
    for k in range(ids.shape[0]):
        m = (ids[k : k + 1, :] == edited) & valid
        hits = hits + jnp.where(m, 1.0, 0.0)
        gsel = gsel + jnp.where(m, gates[k : k + 1, :], 0.0)
    before = jnp.where(
        lax.broadcasted_iota(jnp.int32, (rows, rows), 0) < lax.broadcasted_iota(jnp.int32, (rows, rows), 1),
        1.0, 0.0,
    ).astype(bf16)
    rank = jnp.dot(hits.astype(bf16), before, preferred_element_type=f32)
    slot_of = lax.broadcasted_iota(jnp.int32, (slots, lanes), 0)
    expand = jnp.where(
        lax.shift_right_logical(slot_of, 4) == lax.broadcasted_iota(jnp.int32, (slots, lanes), 1), 1.0, 0.0
    ).astype(bf16)
    hit_s = jnp.dot(expand, hits.astype(bf16), preferred_element_type=f32)
    rank_s = jnp.dot(expand, rank.astype(bf16), preferred_element_type=f32)
    place = (lax.broadcasted_iota(jnp.int32, (slots, rows), 0) & (CAP - 1)).astype(f32)
    pick = jnp.where((hit_s == 1.0) & (rank_s == place), 1.0, 0.0)
    pick_b = pick.astype(bf16)
    tok = jnp.dot(pick_b, tok_ref[...], preferred_element_type=f32).astype(bf16)
    grd = jnp.dot(pick_b, grd_ref[...], preferred_element_type=f32).astype(bf16)
    hi = gsel.astype(bf16).astype(f32)
    rest = gsel - hi
    mid = rest.astype(bf16).astype(f32)
    lo = rest - mid

    def per_slot(x):
        spread = jnp.dot(expand, x.astype(bf16), preferred_element_type=f32)
        return jnp.sum(spread * pick, axis=1, keepdims=True)

    s_hi, s_mid, s_lo = per_slot(hi), per_slot(mid), per_slot(lo)
    s_flag = jnp.sum(pick * flags, axis=1, keepdims=True)
    count = jnp.sum(flags, axis=1, keepdims=True)
    c_hi = jnp.floor(count / 256.0)
    c_lo = count - 256.0 * c_hi
    col = lax.broadcasted_iota(jnp.int32, (slots, side), 1)
    side_v = jnp.where(col == 0, s_hi, 0.0)
    for c, v in ((1, s_mid), (2, s_lo), (3, s_flag), (4, c_hi), (5, c_lo)):
        side_v = jnp.where(col == c, v, side_v)
    side_v = side_v.astype(bf16)
    if split:
        tok_out, grd_out, side_out, pick_out = outs
        tok_out[...] = tok
        grd_out[...] = grd
        side_out[...] = side_v
    else:
        pay_out, pick_out = outs
        pay_out[:, :width] = tok
        pay_out[:, width : 2 * width] = grd
        pay_out[:, 2 * width :] = side_v
    pick_out[...] = pick_b


def glue(expert_ids, gate_values, forget_flags, tokens, token_grads, n_dest):
    import functools

    rows, width = tokens.shape
    slots = n_dest * CAP
    side = 128
    split = width % 128 != 0
    bf16 = jnp.bfloat16
    if split:
        shapes = [(slots, width), (slots, width), (slots, side), (slots, rows)]
    else:
        shapes = [(slots, 2 * width + side), (slots, rows)]
    vmem = pl.BlockSpec(memory_space=pltpu.VMEM)
    outs = pl.pallas_call(
        functools.partial(glue_kernel, n_dest, width, side, split),
        out_shape=[jax.ShapeDtypeStruct(s, bf16) for s in shapes],
        in_specs=[vmem] * 5,
        out_specs=[vmem] * len(shapes),
    )(expert_ids.T, gate_values.T, forget_flags.reshape(1, rows), tokens, token_grads)
    if split:
        return jnp.concatenate(outs[:3], axis=1), outs[3]
    return outs[0], outs[1]


def silu_parts(pre):
    sigmoid_gate = jax.nn.sigmoid(pre)
    return (pre * sigmoid_gate, sigmoid_gate * (1.0 + pre * (1.0 - sigmoid_gate)))


def bf16_part(x):
    return lax.reduce_precision(x, exponent_bits=8, mantissa_bits=7)


def partner(x, bit, n):
    return lax.ppermute(x, "dp", [(i, i ^ bit) for i in range(n)])


def gather_dp(x, n):
    me = lax.axis_index("dp")
    held = [x]
    owners = [me]
    bit = n // 2
    while bit >= 1:
        stacked = jnp.stack(held)
        got = partner(stacked, bit, n)
        held = held + [got[i] for i in range(len(held))]
        owners = owners + [o ^ bit for o in owners]
        bit //= 2
    at = lax.broadcasted_iota(jnp.int32, (n, 1, 1), 0)
    out = jnp.broadcast_to(held[0][None], (n,) + x.shape)
    for piece, owner in zip(held[1:], owners[1:]):
        out = jnp.where(at == owner, piece[None], out)
    return out


def gather_from(held, owners, bit, n):
    while bit >= 1:
        stacked = jnp.stack(held)
        got = partner(stacked, bit, n)
        held = held + [got[i] for i in range(len(held))]
        owners = owners + [o ^ bit for o in owners]
        bit //= 2
    at = lax.broadcasted_iota(jnp.int32, (n, 1, 1), 0)
    out = jnp.broadcast_to(held[0][None], (n,) + held[0].shape)
    for piece, owner in zip(held[1:], owners[1:]):
        out = jnp.where(at == owner, piece[None], out)
    return out


def gather_half(x, n):
    me = lax.axis_index("dp")
    top = n // 2
    base = me & top
    held = [x]
    owners = [me]
    bit = top // 2
    while bit >= 1:
        stacked = jnp.stack(held)
        got = partner(stacked, bit, n)
        held = held + [got[i] for i in range(len(held))]
        owners = owners + [o ^ bit for o in owners]
        bit //= 2
    at = lax.broadcasted_iota(jnp.int32, (top, 1, 1), 0)
    out = jnp.broadcast_to(held[0][None], (top,) + x.shape)
    for piece, owner in zip(held[1:], owners[1:]):
        out = jnp.where(at == owner - base, piece[None], out)
    return out, base


def scatter_dp(parts, n):
    me = lax.axis_index("dp")
    acc = parts
    bit = 1
    while bit < n:
        pairs = acc.reshape((acc.shape[0] // 2, 2) + acc.shape[1:])
        mine = (me & bit) != 0
        keep = jnp.where(mine, pairs[:, 1], pairs[:, 0])
        send = jnp.where(mine, pairs[:, 0], pairs[:, 1])
        got = partner(send.astype(jnp.bfloat16), bit, n)
        acc = keep.astype(jnp.float32) + got.astype(jnp.float32)
        bit *= 2
    return acc[0]


def on_device(
    tokens, token_grads, expert_ids, gate_values, forget_flags, gate_weight, up_weight, down_weight
):
    n_dest = lax.axis_size("expert")
    n_dp = lax.axis_size("dp")
    row_count, width = tokens.shape
    me_dp = lax.axis_index("dp")
    w_down = down_weight[0]
    top = n_dp // 2
    half_cols = (n_dp * width) // 2
    if n_dp > 1:
        upper_half = (me_dp & top) != 0
        lend = jnp.where(upper_half, w_down[:, :half_cols], w_down[:, half_cols:]).T
        keep = jnp.where(upper_half, w_down[:, half_cols:], w_down[:, :half_cols]).T
        borrowed = partner(lend, top, n_dp)
    payload, pick_t = glue(expert_ids, gate_values, forget_flags, tokens, token_grads, n_dest)
    side = payload.shape[1] - 2 * width
    arrived = lax.all_to_all(payload, "expert", split_axis=0, concat_axis=0, tiled=True)
    slots = arrived.shape[0]
    part_tokens = arrived[:, :width]
    raw_grads = arrived[:, width : 2 * width]
    info = arrived[:, 2 * width :].astype(jnp.float32)
    gate_sel = (info[:, 0] + info[:, 1]) + info[:, 2]
    flag = info[:, 3]
    first_row = jnp.where(lax.broadcasted_iota(jnp.int32, (slots,), 0) % CAP == 0, 1.0, 0.0)
    block_hi = (first_row * info[:, 4]).astype(jnp.bfloat16)
    block_lo = (first_row * info[:, 5]).astype(jnp.bfloat16)
    every = jnp.ones((slots, slots), jnp.bfloat16)
    forget_count = 256.0 * jnp.dot(every, block_hi, preferred_element_type=jnp.float32) + jnp.dot(
        every, block_lo, preferred_element_type=jnp.float32
    )
    all_rows = row_count * n_dest
    half_total = jnp.float32(all_rows) / 2.0
    weight = jnp.where(
        flag == 1.0,
        -half_total / forget_count,
        half_total / (jnp.float32(all_rows) - forget_count),
    )
    scale = gate_sel * weight
    part_grads = (scale[:, None] * raw_grads.astype(jnp.float32)).astype(jnp.bfloat16)
    ff = gate_weight.shape[2]
    w_gate = gate_weight[0].reshape(n_dp, width, ff)
    w_up = up_weight[0].reshape(n_dp, width, ff)
    last_dims = (((1,), (1,)), ((), ()))
    if n_dp > 1:
        half_grads, _ = gather_half(part_grads, n_dp)
        half_dims = (((0, 2), (0, 1)), ((), ()))
        ff_down = w_down.shape[0]
        offs = [0]
        bit = top // 2
        while bit >= 1:
            offs = offs + [o ^ bit for o in offs]
            bit //= 2
        own_pos = me_dp & (top - 1)
        lent_rel = jnp.take(
            borrowed.reshape(top, width, ff_down), own_pos ^ jnp.array(offs, jnp.int32), axis=0
        )
        lent = lax.dot_general(part_grads, lent_rel[0], (((1,), (0,)), ((), ())), preferred_element_type=jnp.float32)
        if top > 1:
            rest = jnp.stack([half_grads[0]] * 0 + [
                jnp.sum(jnp.where(
                    lax.broadcasted_iota(jnp.int32, (top, 1, 1), 0) == (own_pos ^ o), half_grads, 0
                ), axis=0).astype(jnp.bfloat16) for o in offs[1:]
            ])
            lent = lent + lax.dot_general(rest, lent_rel[1:], half_dims, preferred_element_type=jnp.float32)
        lent_hi = bf16_part(lent)
        lent_lo = lent - lent_hi
        outgoing = jnp.concatenate(
            [part_tokens, lent_hi.astype(jnp.bfloat16), lent_lo.astype(jnp.bfloat16)], axis=1
        )
        incoming = partner(outgoing, top, n_dp)
        share = incoming[:, width:].astype(jnp.float32)
        returned_share = share[:, :ff_down] + share[:, ff_down:]
        hidden_grad = lax.dot_general(
            half_grads, keep.reshape(top, width, ff_down), half_dims, preferred_element_type=jnp.float32
        )
        hidden_grad = hidden_grad + returned_share
        slot_tokens = gather_from([part_tokens, incoming[:, :width]], [me_dp, me_dp ^ top], top // 2, n_dp)
    else:
        hidden_grad = lax.dot_general(part_grads, w_down, last_dims, preferred_element_type=jnp.float32)
        slot_tokens = part_tokens[None]
    chunk_dims = (((0, 2), (0, 1)), ((), ()))
    gate_pre = lax.dot_general(slot_tokens, w_gate, chunk_dims, preferred_element_type=jnp.float32)
    up_pre = lax.dot_general(slot_tokens, w_up, chunk_dims, preferred_element_type=jnp.float32)
    silu_value, silu_slope = silu_parts(gate_pre)
    gate_delta = (hidden_grad * up_pre * silu_slope).astype(jnp.bfloat16)
    up_delta = (hidden_grad * silu_value).astype(jnp.bfloat16)
    slot_dims = (((1,), (0,)), ((), ()))
    grad_gate = lax.dot_general(
        slot_tokens, gate_delta, slot_dims, preferred_element_type=jnp.float32
    ).astype(jnp.bfloat16)
    grad_up = lax.dot_general(
        slot_tokens, up_delta, slot_dims, preferred_element_type=jnp.float32
    ).astype(jnp.bfloat16)
    back_dims = (((2,), (1,)), ((), ()))
    from_gate = lax.dot_general(w_gate, gate_delta, back_dims, preferred_element_type=jnp.float32)
    from_up = lax.dot_general(w_up, up_delta, back_dims, preferred_element_type=jnp.float32)
    part = (from_gate + from_up).astype(jnp.bfloat16)
    summed = scatter_dp(jnp.swapaxes(part, 1, 2), n_dp).astype(jnp.bfloat16)
    returned = lax.all_to_all(summed, "expert", split_axis=0, concat_axis=0, tiled=True)
    input_grad = lax.dot_general(
        pick_t, returned, (((0,), (0,)), ((), ())), preferred_element_type=jnp.float32
    )
    return (
        grad_gate.reshape(1, n_dp * width, ff),
        grad_up.reshape(1, n_dp * width, ff),
        input_grad.astype(jnp.bfloat16),
    )


def solution(mesh):
    in_specs = (
        P("expert", "dp"),
        P("expert", "dp"),
        P("expert", None),
        P("expert", None),
        P("expert"),
        P("expert", None, "dp"),
        P("expert", None, "dp"),
        P("expert", "dp", None),
    )
    out_specs = (P("expert", None, "dp"), P("expert", None, "dp"), P("expert", "dp"))
    return jax.shard_map(
        on_device, mesh=mesh, in_specs=in_specs, out_specs=out_specs, check_vma=False
    )
```

```python
import jax
import jax.numpy as jnp
from jax import lax
from jax.sharding import PartitionSpec as P
from jax.experimental import pallas as pl
from jax.experimental.pallas import tpu as pltpu

EXP_DEV = 8
CAP = 16


def glue_kernel(n_dest, width, side, split, ids_ref, gates_ref, flags_ref, tok_ref, grd_ref, *outs):
    f32, bf16 = jnp.float32, jnp.bfloat16
    rows = tok_ref.shape[0]
    slots = n_dest * CAP
    lanes = max(16, -(-n_dest // 16) * 16)
    ids = ids_ref[...]
    gates = gates_ref[...]
    flags = flags_ref[...].astype(f32)
    dest = lax.broadcasted_iota(jnp.int32, (lanes, rows), 0)
    edited = dest * EXP_DEV
    valid = dest < n_dest
    hits = jnp.zeros((lanes, rows), f32)
    gsel = jnp.zeros((lanes, rows), f32)
    for k in range(ids.shape[0]):
        m = (ids[k : k + 1, :] == edited) & valid
        hits = hits + jnp.where(m, 1.0, 0.0)
        gsel = gsel + jnp.where(m, gates[k : k + 1, :], 0.0)
    before = jnp.where(
        lax.broadcasted_iota(jnp.int32, (rows, rows), 0) < lax.broadcasted_iota(jnp.int32, (rows, rows), 1),
        1.0, 0.0,
    ).astype(bf16)
    rank = jnp.dot(hits.astype(bf16), before, preferred_element_type=f32)
    slot_of = lax.broadcasted_iota(jnp.int32, (slots, lanes), 0)
    expand = jnp.where(
        lax.shift_right_logical(slot_of, 4) == lax.broadcasted_iota(jnp.int32, (slots, lanes), 1), 1.0, 0.0
    ).astype(bf16)
    hit_s = jnp.dot(expand, hits.astype(bf16), preferred_element_type=f32)
    rank_s = jnp.dot(expand, rank.astype(bf16), preferred_element_type=f32)
    place = (lax.broadcasted_iota(jnp.int32, (slots, rows), 0) & (CAP - 1)).astype(f32)
    pick = jnp.where((hit_s == 1.0) & (rank_s == place), 1.0, 0.0)
    pick_b = pick.astype(bf16)
    tok = jnp.dot(pick_b, tok_ref[...], preferred_element_type=f32).astype(bf16)
    grd = jnp.dot(pick_b, grd_ref[...], preferred_element_type=f32).astype(bf16)
    hi = gsel.astype(bf16).astype(f32)
    rest = gsel - hi
    mid = rest.astype(bf16).astype(f32)
    lo = rest - mid

    into = lax.broadcasted_iota(jnp.int32, (rows, side), 1)

    def to_column(x, c):
        return jnp.dot(x.astype(bf16), jnp.where(into == c, 1.0, 0.0).astype(bf16), preferred_element_type=f32)

    side_v = to_column(jnp.dot(expand, hi.astype(bf16), preferred_element_type=f32) * pick, 0)
    side_v = side_v + to_column(jnp.dot(expand, mid.astype(bf16), preferred_element_type=f32) * pick, 1)
    side_v = side_v + to_column(jnp.dot(expand, lo.astype(bf16), preferred_element_type=f32) * pick, 2)
    side_v = side_v + to_column(pick * flags, 3)
    count = jnp.sum(flags, axis=1, keepdims=True)
    c_hi = jnp.floor(count / 256.0)
    c_lo = count - 256.0 * c_hi
    col = lax.broadcasted_iota(jnp.int32, (slots, side), 1)
    side_v = jnp.where(col == 4, c_hi, jnp.where(col == 5, c_lo, side_v)).astype(bf16)
    if split:
        tok_out, grd_out, side_out, pick_out = outs
        tok_out[...] = tok
        grd_out[...] = grd
        side_out[...] = side_v
    else:
        pay_out, pick_out = outs
        pay_out[:, :width] = tok
        pay_out[:, width : 2 * width] = grd
        pay_out[:, 2 * width :] = side_v
    pick_out[...] = pick_b


def glue(expert_ids, gate_values, forget_flags, tokens, token_grads, n_dest):
    import functools

    rows, width = tokens.shape
    slots = n_dest * CAP
    side = 128
    split = width % 128 != 0
    bf16 = jnp.bfloat16
    if split:
        shapes = [(slots, width), (slots, width), (slots, side), (slots, rows)]
    else:
        shapes = [(slots, 2 * width + side), (slots, rows)]
    vmem = pl.BlockSpec(memory_space=pltpu.VMEM)
    outs = pl.pallas_call(
        functools.partial(glue_kernel, n_dest, width, side, split),
        out_shape=[jax.ShapeDtypeStruct(s, bf16) for s in shapes],
        in_specs=[vmem] * 5,
        out_specs=[vmem] * len(shapes),
    )(expert_ids.T, gate_values.T, forget_flags.reshape(1, rows), tokens, token_grads)
    if split:
        return jnp.concatenate(outs[:3], axis=1), outs[3]
    return outs[0], outs[1]


def silu_parts(pre):
    sigmoid_gate = jax.nn.sigmoid(pre)
    return (pre * sigmoid_gate, sigmoid_gate * (1.0 + pre * (1.0 - sigmoid_gate)))


def bf16_part(x):
    return lax.reduce_precision(x, exponent_bits=8, mantissa_bits=7)


def partner(x, bit, n):
    return lax.ppermute(x, "dp", [(i, i ^ bit) for i in range(n)])


def gather_dp(x, n):
    me = lax.axis_index("dp")
    held = [x]
    owners = [me]
    bit = n // 2
    while bit >= 1:
        stacked = jnp.stack(held)
        got = partner(stacked, bit, n)
        held = held + [got[i] for i in range(len(held))]
        owners = owners + [o ^ bit for o in owners]
        bit //= 2
    at = lax.broadcasted_iota(jnp.int32, (n, 1, 1), 0)
    out = jnp.broadcast_to(held[0][None], (n,) + x.shape)
    for piece, owner in zip(held[1:], owners[1:]):
        out = jnp.where(at == owner, piece[None], out)
    return out


def gather_from(held, owners, bit, n):
    while bit >= 1:
        stacked = jnp.stack(held)
        got = partner(stacked, bit, n)
        held = held + [got[i] for i in range(len(held))]
        owners = owners + [o ^ bit for o in owners]
        bit //= 2
    at = lax.broadcasted_iota(jnp.int32, (n, 1, 1), 0)
    out = jnp.broadcast_to(held[0][None], (n,) + held[0].shape)
    for piece, owner in zip(held[1:], owners[1:]):
        out = jnp.where(at == owner, piece[None], out)
    return out


def gather_half(x, n):
    me = lax.axis_index("dp")
    top = n // 2
    base = me & top
    held = [x]
    owners = [me]
    bit = top // 2
    while bit >= 1:
        stacked = jnp.stack(held)
        got = partner(stacked, bit, n)
        held = held + [got[i] for i in range(len(held))]
        owners = owners + [o ^ bit for o in owners]
        bit //= 2
    at = lax.broadcasted_iota(jnp.int32, (top, 1, 1), 0)
    out = jnp.broadcast_to(held[0][None], (top,) + x.shape)
    for piece, owner in zip(held[1:], owners[1:]):
        out = jnp.where(at == owner - base, piece[None], out)
    return out, base


def scatter_dp(parts, n):
    me = lax.axis_index("dp")
    acc = parts
    bit = 1
    while bit < n:
        pairs = acc.reshape((acc.shape[0] // 2, 2) + acc.shape[1:])
        mine = (me & bit) != 0
        keep = jnp.where(mine, pairs[:, 1], pairs[:, 0])
        send = jnp.where(mine, pairs[:, 0], pairs[:, 1])
        got = partner(send.astype(jnp.bfloat16), bit, n)
        acc = keep.astype(jnp.float32) + got.astype(jnp.float32)
        bit *= 2
    return acc[0]


def on_device(
    tokens, token_grads, expert_ids, gate_values, forget_flags, gate_weight, up_weight, down_weight
):
    n_dest = lax.axis_size("expert")
    n_dp = lax.axis_size("dp")
    row_count, width = tokens.shape
    me_dp = lax.axis_index("dp")
    w_down = down_weight[0]
    top = n_dp // 2
    half_cols = (n_dp * width) // 2
    if n_dp > 1:
        upper_half = (me_dp & top) != 0
        lend = jnp.where(upper_half, w_down[:, :half_cols], w_down[:, half_cols:]).T
        keep = jnp.where(upper_half, w_down[:, half_cols:], w_down[:, :half_cols]).T
        borrowed = partner(lend, top, n_dp)
    payload, pick_t = glue(expert_ids, gate_values, forget_flags, tokens, token_grads, n_dest)
    side = payload.shape[1] - 2 * width
    arrived = lax.all_to_all(payload, "expert", split_axis=0, concat_axis=0, tiled=True)
    slots = arrived.shape[0]
    part_tokens = arrived[:, :width]
    raw_grads = arrived[:, width : 2 * width]
    info = arrived[:, 2 * width :].astype(jnp.float32)
    gate_sel = (info[:, 0] + info[:, 1]) + info[:, 2]
    flag = info[:, 3]
    first_row = jnp.where(lax.broadcasted_iota(jnp.int32, (slots,), 0) % CAP == 0, 1.0, 0.0)
    block_hi = (first_row * info[:, 4]).astype(jnp.bfloat16)
    block_lo = (first_row * info[:, 5]).astype(jnp.bfloat16)
    every = jnp.ones((slots, slots), jnp.bfloat16)
    forget_count = 256.0 * jnp.dot(every, block_hi, preferred_element_type=jnp.float32) + jnp.dot(
        every, block_lo, preferred_element_type=jnp.float32
    )
    all_rows = row_count * n_dest
    half_total = jnp.float32(all_rows) / 2.0
    weight = jnp.where(
        flag == 1.0,
        -half_total / forget_count,
        half_total / (jnp.float32(all_rows) - forget_count),
    )
    scale = gate_sel * weight
    part_grads = (scale[:, None] * raw_grads.astype(jnp.float32)).astype(jnp.bfloat16)
    ff = gate_weight.shape[2]
    w_gate = gate_weight[0].reshape(n_dp, width, ff)
    w_up = up_weight[0].reshape(n_dp, width, ff)
    last_dims = (((1,), (1,)), ((), ()))
    if n_dp > 1:
        half_grads, _ = gather_half(part_grads, n_dp)
        half_dims = (((0, 2), (0, 1)), ((), ()))
        ff_down = w_down.shape[0]
        lent = lax.dot_general(
            half_grads, borrowed.reshape(top, width, ff_down), half_dims, preferred_element_type=jnp.float32
        )
        lent_hi = bf16_part(lent)
        lent_lo = lent - lent_hi
        outgoing = jnp.concatenate(
            [part_tokens, lent_hi.astype(jnp.bfloat16), lent_lo.astype(jnp.bfloat16)], axis=1
        )
        incoming = partner(outgoing, top, n_dp)
        share = incoming[:, width:].astype(jnp.float32)
        returned_share = share[:, :ff_down] + share[:, ff_down:]
        hidden_grad = lax.dot_general(
            half_grads, keep.reshape(top, width, ff_down), half_dims, preferred_element_type=jnp.float32
        )
        hidden_grad = hidden_grad + returned_share
        slot_tokens = gather_from([part_tokens, incoming[:, :width]], [me_dp, me_dp ^ top], top // 2, n_dp)
    else:
        hidden_grad = lax.dot_general(part_grads, w_down, last_dims, preferred_element_type=jnp.float32)
        slot_tokens = part_tokens[None]
    chunk_dims = (((0, 2), (0, 1)), ((), ()))
    gate_pre = lax.dot_general(slot_tokens, w_gate, chunk_dims, preferred_element_type=jnp.float32)
    up_pre = lax.dot_general(slot_tokens, w_up, chunk_dims, preferred_element_type=jnp.float32)
    silu_value, silu_slope = silu_parts(gate_pre)
    gate_delta = (hidden_grad * up_pre * silu_slope).astype(jnp.bfloat16)
    up_delta = (hidden_grad * silu_value).astype(jnp.bfloat16)
    slot_dims = (((1,), (0,)), ((), ()))
    grad_gate = lax.dot_general(
        slot_tokens, gate_delta, slot_dims, preferred_element_type=jnp.float32
    ).astype(jnp.bfloat16)
    grad_up = lax.dot_general(
        slot_tokens, up_delta, slot_dims, preferred_element_type=jnp.float32
    ).astype(jnp.bfloat16)
    back_dims = (((2,), (1,)), ((), ()))
    from_gate = lax.dot_general(w_gate, gate_delta, back_dims, preferred_element_type=jnp.float32)
    from_up = lax.dot_general(w_up, up_delta, back_dims, preferred_element_type=jnp.float32)
    part = (from_gate + from_up).astype(jnp.bfloat16)
    summed = scatter_dp(jnp.swapaxes(part, 1, 2), n_dp).astype(jnp.bfloat16)
    returned = lax.all_to_all(summed, "expert", split_axis=0, concat_axis=0, tiled=True)
    input_grad = lax.dot_general(
        pick_t, returned, (((0,), (0,)), ((), ())), preferred_element_type=jnp.float32
    )
    return (
        grad_gate.reshape(1, n_dp * width, ff),
        grad_up.reshape(1, n_dp * width, ff),
        input_grad.astype(jnp.bfloat16),
    )


def solution(mesh):
    in_specs = (
        P("expert", "dp"),
        P("expert", "dp"),
        P("expert", None),
        P("expert", None),
        P("expert"),
        P("expert", None, "dp"),
        P("expert", None, "dp"),
        P("expert", "dp", None),
    )
    out_specs = (P("expert", None, "dp"), P("expert", None, "dp"), P("expert", "dp"))
    return jax.shard_map(
        on_device, mesh=mesh, in_specs=in_specs, out_specs=out_specs, check_vma=False
    )
```
